512 devices in a mesh: ctx: 16 (over z), head: 32 (over x, y, core).
Axes of the slice: x: 4, y: 4, z: 16, core: 2. Of those that a mesh axis runs over, the one named last changes fastest.
Arguments:
- tokens_in: bfloat16 [4096, 4096], P('ctx', 'head'), may hold values from -6 to 6
- w_qkv: bfloat16 [4096, 32, 384], P(None, 'head'), may hold values from -0.125 to 0.125
- w_out: bfloat16 [32, 128, 4096], P('head'), may hold values from -0.375 to 0.375
- codebook: bfloat16 [32, 512, 128], P('head'), may hold values from -184 to 184
- codes: int32 [32, 4096], P('head', 'ctx'), may hold values from 0 to 511
- reach: int32 [16], P('ctx'), may hold values from 1 to 256, as said below
Outputs:
- mixed: bfloat16 [4096, 4096], P(('ctx', 'head'))
The draws below stay inside these ranges and needn't reach their ends.
Inputs may be any that keep to these rules, and one draw needn't show every extreme that they name: reach[g] is how many of the last positions of block g - 1 block g sees with exact keys; reach[0] has no effect.
All inputs are finite; a program needn't handle non-finite values.
Results may differ from the reference program's by a relative error of at most 0.015.
Values may be sent and summed in bfloat16 or wider, within the bound.
No kernel may reach another device: no remote copies, remote signals or barrier semaphores. Data moves between devices by JAX's collectives and lax.ppermute only.
A program may use at most 64 MiB of HBM per device.

```python
import functools
import math
import jax
import jax.numpy as jnp
from jax import lax

D = 4096
HD = 128
CODES = 512
BLK = 256
HEADS = 32
SEQ = 4096
NBLK = 16


def draw_codebook(key, part):
    key_base = jax.random.fold_in(key, 0)
    base = 1.4 * jax.random.truncated_normal(key_base, -4.0, 4.0, (HEADS, CODES, HD), jnp.float32)
    return base.astype(jnp.bfloat16)


def draw_reach(key, part):
    key_base, key_high, key_low = jax.random.split(key, 3)
    base = jax.random.randint(key_base, (NBLK,), 1, BLK + 1, jnp.int32)
    high_pos = jax.random.randint(key_high, (), 0, NBLK, jnp.int32)
    low_pos = (high_pos + 1 + jax.random.randint(key_low, (), 0, NBLK - 1, jnp.int32)) % NBLK
    index_row = jnp.arange(NBLK, dtype=jnp.int32)
    return jnp.where(index_row == high_pos, BLK, jnp.where(index_row == low_pos, 1, base)).astype(jnp.int32)


def plant(array, rng, low, high):
    spot = [jax.random.randint(jax.random.fold_in(rng, axis), (), 0, length) for axis, length in enumerate(array.shape)]
    main_axis = array.shape.index(max(array.shape))
    neighbour = spot[:main_axis] + [(spot[main_axis] + 1) % array.shape[main_axis]] + spot[main_axis + 1:]
    return array.at[tuple(spot)].set(low).at[tuple(neighbour)].set(high)


def levels(key, extent, shards, smallest, top_value):
    def one(position, parts):
        draws = jax.random.uniform(jax.random.fold_in(jax.random.fold_in(key, 6), position), (parts,), jnp.float32, smallest / len(shards), top_value / len(shards))
        return jnp.repeat(jnp.exp(draws), extent[position] // parts).reshape((-1,) + (1,) * (len(extent) - position - 1))

    gain = one(*shards[0])
    for cut in shards[1:]:
        gain = gain * one(*cut)
    return gain


def noise(key, shape, spread, limit, pieces=(), held_as=jnp.bfloat16):
    result = jax.random.normal(key, shape, jnp.float32) * spread
    if len(pieces) > 0:
        result = levels(key, shape, pieces, -0.22, 0.18) * result
    return jnp.clip(result, min=-limit, max=limit).astype(held_as)


def setup_inputs(seed: int = 0) -> dict:
    key_of = jax.random.split(jax.random.key(seed), 7)
    tokens_in = noise(key_of[0], (SEQ, D), 1.0, 6.0, ((0, 16), (1, 32)))
    w_qkv = noise(key_of[1], (D, HEADS, 3 * HD), (D // 2) ** -0.5, 0.125, ((1, 32),))
    w_out = noise(key_of[2], (HEADS, HD, D), (HEADS * HD // 16) ** -0.5, 0.375, ((0, 32),))
    codebook = draw_codebook(jax.random.fold_in(key_of[6], 71), 0)
    codes = plant(jax.random.randint(key_of[4], (HEADS, SEQ), 0, CODES), jax.random.fold_in(key_of[4], 1), 0, CODES - 1).astype(jnp.int32)
    reach = draw_reach(jax.random.fold_in(key_of[6], 71), 0)
    return {"tokens_in": tokens_in, "w_qkv": w_qkv, "w_out": w_out, "codebook": codebook, "codes": codes, "reach": reach}


def attend_block(queries, keys_win, vals_win, cache_v, cache_c, book, reach_one, prev_flag, block_len, scale):
    exact = lax.dot_general(queries, keys_win, (((1,), (1,)), ((), ())), preferred_element_type=jnp.float32) * scale
    coded = lax.dot_general(queries, book, (((1,), (1,)), ((), ())), preferred_element_type=jnp.float32) * scale
    rows = lax.broadcasted_iota(jnp.int32, exact.shape, 0)
    cols = lax.broadcasted_iota(jnp.int32, exact.shape, 1)
    prev_ok = (cols < block_len) & (cols >= block_len - reach_one) & prev_flag
    curr_ok = (cols >= block_len) & (cols - block_len <= rows)
    allowed = prev_ok | curr_ok
    valid = cache_c > 0.5
    top = jnp.maximum(lax.optimization_barrier(jnp.max(jnp.where(allowed, exact, -jnp.inf), axis=1)), lax.optimization_barrier(jnp.max(jnp.where(valid[None, :], coded, -jnp.inf), axis=1)))
    probs = jnp.exp(jnp.where(allowed, exact - top[:, None], -jnp.inf))
    weights = jnp.exp(jnp.where(valid[None, :], coded - top[:, None], -jnp.inf))
    numer = jnp.dot(probs.astype(jnp.bfloat16), vals_win, preferred_element_type=jnp.float32)
    numer = numer + jnp.dot(weights, cache_v, precision=lax.Precision.HIGHEST)
    denom = lax.optimization_barrier(jnp.sum(probs, axis=1)) + jnp.dot(weights, cache_c, precision=lax.Precision.HIGHEST)
    return (numer / denom[:, None]).astype(jnp.bfloat16)

def shift_blocks(blocks):
    return jnp.concatenate([jnp.zeros_like(blocks[:1]), blocks[:-1]], axis=0)

def reference(tokens_in, w_qkv, w_out, codebook, codes, reach):
    scale = 1.0 / math.sqrt(HD)
    num_blocks = SEQ // BLK
    w_heads = jnp.moveaxis(w_qkv, 1, 0)
    code_ids = jnp.arange(CODES, dtype=jnp.int32)
    prev_flags = jnp.arange(num_blocks, dtype=jnp.int32) > 0
    offsets = jnp.arange(BLK, dtype=jnp.int32)
    cut = (offsets[None, :] < (BLK - reach)[:, None]).astype(jnp.float32)
    attend = jax.vmap(functools.partial(attend_block, block_len=BLK, scale=scale), in_axes=(0, 0, 0, 0, 0, None, 0, 0))

    def head_step(total, inputs):
        w_head, w_proj, book, code_row = inputs
        proj = jnp.dot(tokens_in, w_head, preferred_element_type=jnp.float32)
        queries = proj[:, :HD].astype(jnp.bfloat16)
        keys = proj[:, HD:2 * HD].astype(jnp.bfloat16)
        values = proj[:, 2 * HD:].astype(jnp.bfloat16)
        onehot = (code_row[:, None] == code_ids[None, :]).astype(jnp.float32).reshape(num_blocks, BLK, CODES)
        vals_f = values.astype(jnp.float32).reshape(num_blocks, BLK, HD)
        block_v = jnp.einsum('nbs,nbd->nsd', onehot, vals_f, precision=lax.Precision.HIGHEST)
        block_c = lax.optimization_barrier(jnp.sum(onehot, axis=1))
        before_v = shift_blocks(jnp.cumsum(block_v, axis=0) - block_v)
        before_c = shift_blocks(jnp.cumsum(block_c, axis=0) - block_c)
        masked = shift_blocks(onehot) * cut[:, :, None]
        cache_v = before_v + jnp.einsum('nbs,nbd->nsd', masked, shift_blocks(vals_f), precision=lax.Precision.HIGHEST)
        cache_c = before_c + lax.optimization_barrier(jnp.sum(masked, axis=1))
        keys_b = keys.reshape(num_blocks, BLK, HD)
        vals_b = values.reshape(num_blocks, BLK, HD)
        keys_win = jnp.concatenate([shift_blocks(keys_b), keys_b], axis=1)
        vals_win = jnp.concatenate([shift_blocks(vals_b), vals_b], axis=1)
        outs = attend(queries.reshape(num_blocks, BLK, HD), keys_win, vals_win, cache_v, cache_c, book, reach, prev_flags)
        attended = outs.reshape(SEQ, HD)
        term = jnp.dot(attended, w_proj, preferred_element_type=jnp.float32).astype(jnp.bfloat16)
        term = lax.optimization_barrier(term)
        return (total + term.astype(jnp.float32), None)
    start = jnp.zeros((SEQ, D), jnp.float32)
    total, unused = lax.scan(head_step, start, (w_heads, w_out, codebook, codes))
    return total.astype(jnp.bfloat16)
```

```python
import math

import jax
import jax.numpy as jnp
from jax import lax
from jax.sharding import Mesh
from jax.sharding import PartitionSpec as P

BLK = 256
HEAD_AXES = ("hx", "hy", "hc")


def _flat(x, y, c, ny, nc):
    return (x * ny + y) * nc + c


def _ring_perm(stage, d, nx, ny, nc):
    pairs = []
    for x in range(nx):
        for y in range(ny):
            for c in range(nc):
                along_y = (c == 0) == (stage == 0)
                if along_y:
                    tx, ty = x, (y + d) % ny
                else:
                    tx, ty = (x + d) % nx, y
                pairs.append((_flat(x, y, c, ny, nc), _flat(tx, ty, c, ny, nc)))
    return pairs


def _core_perm(nx, ny, nc):
    pairs = []
    for x in range(nx):
        for y in range(ny):
            for c in range(nc):
                pairs.append((_flat(x, y, c, ny, nc), _flat(x, y, 1 - c, ny, nc)))
    return pairs


def _send(value, perm):
    return lax.ppermute(value, HEAD_AXES, perm)


def gather_ring(blk, stage, sizes):
    p1 = _send(blk, _ring_perm(stage, 1, *sizes))
    m1 = _send(blk, _ring_perm(stage, -1, *sizes))
    h = blk.shape[0] // 2
    a = _send(p1[:h], _ring_perm(stage, 1, *sizes))
    b = _send(m1[h:], _ring_perm(stage, -1, *sizes))
    far = jnp.concatenate([a, b], axis=0)
    return jnp.stack([blk, p1, far, m1])


def reduce_ring(data, stage, sizes):
    h = data.shape[1] // 2
    rp = _send(data[2, :h].astype(jnp.bfloat16), _ring_perm(stage, 1, *sizes))
    rm = _send(data[2, h:].astype(jnp.bfloat16), _ring_perm(stage, -1, *sizes))
    ahead = jnp.concatenate([data[1, :h] + rp, data[1, h:]], axis=0)
    behind = jnp.concatenate([data[3, :h], data[3, h:] + rm], axis=0)
    gp = _send(ahead.astype(jnp.bfloat16), _ring_perm(stage, 1, *sizes))
    gm = _send(behind.astype(jnp.bfloat16), _ring_perm(stage, -1, *sizes))
    return data[0] + gp.astype(jnp.float32) + gm.astype(jnp.float32)


def attend_block(
    queries, keys_win, vals_win, cache_v, cache_c, book, reach_one, prev_flag, block_len, scale
):
    exact = (
        lax.dot_general(
            queries, keys_win, (((1,), (1,)), ((), ())), preferred_element_type=jnp.float32
        )
        * scale
    )
    coded = (
        lax.dot_general(queries, book, (((1,), (1,)), ((), ())), preferred_element_type=jnp.float32)
        * scale
    )
    rows = lax.broadcasted_iota(jnp.int32, exact.shape, 0)
    cols = lax.broadcasted_iota(jnp.int32, exact.shape, 1)
    prev_ok = (cols < block_len) & (cols >= block_len - reach_one) & prev_flag
    curr_ok = (cols >= block_len) & (cols - block_len <= rows)
    allowed = prev_ok | curr_ok
    valid = cache_c > 0.5
    top = jnp.maximum(
        jnp.max(jnp.where(allowed, exact, -jnp.inf), axis=1),
        jnp.max(jnp.where(valid[None, :], coded, -jnp.inf), axis=1),
    )
    probs = jnp.exp(jnp.where(allowed, exact - top[:, None], -jnp.inf))
    weights = jnp.exp(jnp.where(valid[None, :], coded - top[:, None], -jnp.inf))
    numer = jnp.dot(probs.astype(jnp.bfloat16), vals_win, preferred_element_type=jnp.float32)
    numer = numer + jnp.dot(weights, cache_v, precision=lax.Precision.HIGHEST)
    denom = jnp.sum(probs, axis=1) + jnp.dot(weights, cache_c, precision=lax.Precision.HIGHEST)
    return (numer / denom[:, None]).astype(jnp.bfloat16)


def on_device(tokens_in, w_qkv, w_out, codebook, codes, reach):
    nx, ny, nc = lax.axis_size("hx"), lax.axis_size("hy"), lax.axis_size("hc")
    sizes = (nx, ny, nc)
    core_perm = _core_perm(*sizes)
    me_x, me_y, me_c = lax.axis_index("hx"), lax.axis_index("hy"), lax.axis_index("hc")
    n_ctx = lax.axis_size("ctx")
    g = lax.axis_index("ctx")
    rows, width = tokens_in.shape
    head_dim = codebook.shape[2]
    num_codes = codebook.shape[1]
    scale = 1.0 / math.sqrt(head_dim)
    half = rows // 2

    code_row = codes[0]
    codes_all = lax.all_gather(code_row, "ctx").reshape(n_ctx * rows)
    limit = g * BLK - reach[0]
    cached = jnp.arange(n_ctx * rows, dtype=jnp.int32) < limit
    code_ids = jnp.arange(num_codes, dtype=jnp.int32)
    onehot = ((codes_all[:, None] == code_ids[None, :]) & cached[:, None]).astype(jnp.bfloat16)
    cache_c = jnp.sum(onehot.astype(jnp.float32), axis=0)

    projected = project(tokens_in, w_qkv, sizes)
    queries = projected[:, :head_dim].astype(jnp.bfloat16)
    key_vals = projected[:, head_dim:].astype(jnp.bfloat16)
    values = key_vals[:, head_dim:]

    route = [(i, i + 1) for i in range(n_ctx - 1)]
    prev_kv = lax.ppermute(key_vals, "ctx", route)
    vals_all = lax.all_gather(values, "ctx").reshape(n_ctx * rows, head_dim)
    cache_v = lax.dot_general(
        onehot, vals_all, (((0,), (0,)), ((), ())), preferred_element_type=jnp.float32
    )

    ext_kv = jnp.concatenate([prev_kv, key_vals], axis=0)
    attended = attend_block(
        queries,
        ext_kv[:, :head_dim],
        ext_kv[:, head_dim:],
        cache_v,
        cache_c,
        codebook[0],
        reach[0],
        g > 0,
        BLK,
        scale,
    )

    return reduce_out(attended, w_out, sizes)


def project(tokens_in, w_qkv, sizes):
    nx, ny, nc = sizes
    core_perm = _core_perm(*sizes)
    me_x, me_y, me_c = lax.axis_index("hx"), lax.axis_index("hy"), lax.axis_index("hc")
    rows, width = tokens_in.shape
    half = rows // 2
    mine = lax.dynamic_slice_in_dim(tokens_in, me_c * half, half, 0)
    other = lax.dynamic_slice_in_dim(tokens_in, (1 - me_c) * half, half, 0)
    got = _send(other, core_perm)
    chip = jnp.where(
        me_c == 0, jnp.concatenate([mine, got], axis=1), jnp.concatenate([got, mine], axis=1)
    )
    g1 = gather_ring(chip, 0, sizes)
    g2 = gather_ring(g1, 1, sizes)
    g2p = _send(g2, core_perm)

    w_local = w_qkv[:, 0, :]
    nw = w_local.shape[1]
    w16 = w_local.reshape(nx * ny, nc * width, nw)
    k2 = jnp.arange(4, dtype=jnp.int32)[:, None]
    k1 = jnp.arange(4, dtype=jnp.int32)[None, :]

    def source_rows(cc):
        xs = jnp.where(cc == 0, (me_x - k2) % nx, (me_x - k1) % nx)
        ys = jnp.where(cc == 0, (me_y - k1) % ny, (me_y - k2) % ny)
        return (xs * ny + ys).reshape(nx * ny)

    w_own = jnp.take(w16, source_rows(me_c), axis=0, mode="clip")
    w_oth = jnp.take(w16, source_rows(1 - me_c), axis=0, mode="clip")
    dims = (((0, 2), (0, 1)), ((), ()))
    proj_own = lax.dot_general(
        g2.reshape(nx * ny, half, nc * width), w_own, dims, preferred_element_type=jnp.float32
    )
    proj_oth = lax.dot_general(
        g2p.reshape(nx * ny, half, nc * width), w_oth, dims, preferred_element_type=jnp.float32
    )
    projected = jnp.where(
        me_c == 0,
        jnp.concatenate([proj_own, proj_oth], axis=0),
        jnp.concatenate([proj_oth, proj_own], axis=0),
    )
    return projected


def reduce_out(attended, w_out, sizes):
    nx, ny, nc = sizes
    core_perm = _core_perm(*sizes)
    me_x, me_y, me_c = lax.axis_index("hx"), lax.axis_index("hy"), lax.axis_index("hc")
    rows = attended.shape[0]
    e1 = jnp.arange(4, dtype=jnp.int32)[:, None, None, None]
    e2 = jnp.arange(4, dtype=jnp.int32)[None, :, None, None]
    ch = jnp.arange(nc, dtype=jnp.int32)[None, None, :, None]
    t = jnp.arange(rows // (nx * ny * nc), dtype=jnp.int32)[None, None, None, :]
    tt = t.shape[-1]

    def row_order(cc):
        xh = jnp.where(cc == 0, (me_x + e2) % nx, (me_x + e1) % nx)
        yh = jnp.where(cc == 0, (me_y + e1) % ny, (me_y + e2) % ny)
        return (((xh * ny + yh) * nc + ch) * tt + t).reshape(rows)

    w_full = w_out[0]
    cols = w_full.shape[1] // 2
    w_keep = lax.dynamic_slice_in_dim(w_full, me_c * cols, cols, 1)
    w_give = lax.dynamic_slice_in_dim(w_full, (1 - me_c) * cols, cols, 1)
    own_rows = jnp.take(attended, row_order(me_c), axis=0, mode="clip")
    oth_rows = jnp.take(attended, row_order(1 - me_c), axis=0, mode="clip")
    keep = jnp.dot(own_rows, w_keep, preferred_element_type=jnp.float32)
    give = jnp.dot(oth_rows, w_give, preferred_element_type=jnp.float32)
    got = _send(give.astype(jnp.bfloat16), core_perm)
    summed = (keep + got.astype(jnp.float32)).reshape(4, 4, nc, rows // (nx * ny * nc), cols)
    r1 = reduce_ring(summed, 0, sizes)
    r2 = reduce_ring(r1, 1, sizes)
    mine = lax.dynamic_index_in_dim(r2, me_c, 0, keepdims=False)
    other = lax.dynamic_index_in_dim(r2, 1 - me_c, 0, keepdims=False)
    got = _send(other.astype(jnp.bfloat16), core_perm).astype(jnp.float32)
    out = jnp.where(
        me_c == 0, jnp.concatenate([mine, got], axis=1), jnp.concatenate([got, mine], axis=1)
    )
    return out.astype(jnp.bfloat16)


def solution(mesh):
    n_ctx, n_head = mesh.devices.shape
    devices = mesh.devices.reshape(n_ctx, 4, 4, n_head // 16)
    grid = Mesh(devices, ("ctx",) + HEAD_AXES)
    in_specs = (
        P("ctx", HEAD_AXES),
        P(None, HEAD_AXES, None),
        P(HEAD_AXES, None, None),
        P(HEAD_AXES, None, None),
        P(HEAD_AXES, "ctx"),
        P("ctx"),
    )
    out_specs = P(("ctx",) + HEAD_AXES, None)
    return jax.shard_map(
        on_device, mesh=grid, in_specs=in_specs, out_specs=out_specs, check_vma=False
    )
```

```python
import math

import jax
import jax.numpy as jnp
from jax import lax
from jax.sharding import Mesh
from jax.sharding import PartitionSpec as P

BLK = 256
HEAD_AXES = ("hx", "hy", "hc")


def _flat(x, y, c, ny, nc):
    return (x * ny + y) * nc + c


def _ring_perm(stage, d, nx, ny, nc):
    pairs = []
    for x in range(nx):
        for y in range(ny):
            for c in range(nc):
                along_y = (c == 0) == (stage == 0)
                if along_y:
                    tx, ty = x, (y + d) % ny
                else:
                    tx, ty = (x + d) % nx, y
                pairs.append((_flat(x, y, c, ny, nc), _flat(tx, ty, c, ny, nc)))
    return pairs


def _core_perm(nx, ny, nc):
    pairs = []
    for x in range(nx):
        for y in range(ny):
            for c in range(nc):
                pairs.append((_flat(x, y, c, ny, nc), _flat(x, y, 1 - c, ny, nc)))
    return pairs


def _send(value, perm):
    return lax.ppermute(value, HEAD_AXES, perm)


def gather_ring(blk, stage, sizes):
    p1 = _send(blk, _ring_perm(stage, 1, *sizes))
    m1 = _send(blk, _ring_perm(stage, -1, *sizes))
    h = blk.shape[0] // 2
    a = _send(p1[:h], _ring_perm(stage, 1, *sizes))
    b = _send(m1[h:], _ring_perm(stage, -1, *sizes))
    far = jnp.concatenate([a, b], axis=0)
    return jnp.stack([blk, p1, far, m1])


def reduce_ring(data, stage, sizes):
    h = data.shape[1] // 2
    rp = _send(data[2, :h].astype(jnp.bfloat16), _ring_perm(stage, 1, *sizes))
    rm = _send(data[2, h:].astype(jnp.bfloat16), _ring_perm(stage, -1, *sizes))
    ahead = jnp.concatenate([data[1, :h] + rp, data[1, h:]], axis=0)
    behind = jnp.concatenate([data[3, :h], data[3, h:] + rm], axis=0)
    gp = _send(ahead.astype(jnp.bfloat16), _ring_perm(stage, 1, *sizes))
    gm = _send(behind.astype(jnp.bfloat16), _ring_perm(stage, -1, *sizes))
    return data[0] + gp.astype(jnp.float32) + gm.astype(jnp.float32)


def attend_block(
    queries, keys_win, vals_win, cache_v, cache_c, book, reach_one, prev_flag, block_len, scale
):
    exact = (
        lax.dot_general(
            queries, keys_win, (((1,), (1,)), ((), ())), preferred_element_type=jnp.float32
        )
        * scale
    )
    coded = (
        lax.dot_general(queries, book, (((1,), (1,)), ((), ())), preferred_element_type=jnp.float32)
        * scale
    )
    rows = lax.broadcasted_iota(jnp.int32, exact.shape, 0)
    cols = lax.broadcasted_iota(jnp.int32, exact.shape, 1)
    prev_ok = (cols < block_len) & (cols >= block_len - reach_one) & prev_flag
    curr_ok = (cols >= block_len) & (cols - block_len <= rows)
    allowed = prev_ok | curr_ok
    valid = cache_c > 0.5
    top = jnp.maximum(
        jnp.max(jnp.where(allowed, exact, -jnp.inf), axis=1),
        jnp.max(jnp.where(valid[None, :], coded, -jnp.inf), axis=1),
    )
    probs = jnp.exp(jnp.where(allowed, exact - top[:, None], -jnp.inf))
    weights = jnp.exp(jnp.where(valid[None, :], coded - top[:, None], -jnp.inf))
    numer = jnp.dot(probs.astype(jnp.bfloat16), vals_win, preferred_element_type=jnp.float32)
    numer = numer + jnp.dot(weights, cache_v, precision=lax.Precision.HIGHEST)
    denom = jnp.sum(probs, axis=1) + jnp.dot(weights, cache_c, precision=lax.Precision.HIGHEST)
    return (numer / denom[:, None]).astype(jnp.bfloat16)


def on_device(tokens_in, w_qkv, w_out, codebook, codes, reach):
    nx, ny, nc = lax.axis_size("hx"), lax.axis_size("hy"), lax.axis_size("hc")
    sizes = (nx, ny, nc)
    core_perm = _core_perm(*sizes)
    me_x, me_y, me_c = lax.axis_index("hx"), lax.axis_index("hy"), lax.axis_index("hc")
    n_ctx = lax.axis_size("ctx")
    g = lax.axis_index("ctx")
    rows, width = tokens_in.shape
    head_dim = codebook.shape[2]
    num_codes = codebook.shape[1]
    scale = 1.0 / math.sqrt(head_dim)
    half = rows // 2

    projected = project(tokens_in, w_qkv, sizes)
    queries = projected[:, :head_dim].astype(jnp.bfloat16)
    key_vals = projected[:, head_dim:].astype(jnp.bfloat16)
    values = key_vals[:, head_dim:]

    route = [(i, i + 1) for i in range(n_ctx - 1)]
    prev_kv = lax.ppermute(key_vals, "ctx", route)
    code_row = codes[0].reshape(-1, head_dim)
    hi = (code_row // 16).astype(jnp.bfloat16)
    lo = (code_row % 16).astype(jnp.bfloat16)
    pad = jnp.zeros((16 - 2 * code_row.shape[0], head_dim), jnp.bfloat16)
    blob = jnp.concatenate([values, hi, lo, pad], axis=0)
    blobs = lax.all_gather(blob, "ctx")
    vals_all = blobs[:, :rows].reshape(n_ctx * rows, head_dim)
    nr = code_row.shape[0]
    hi_all = blobs[:, rows : rows + nr].astype(jnp.int32)
    lo_all = blobs[:, rows + nr : rows + 2 * nr].astype(jnp.int32)
    codes_all = (hi_all * 16 + lo_all).reshape(n_ctx * rows)
    limit = g * BLK - reach[0]
    cached = jnp.arange(n_ctx * rows, dtype=jnp.int32) < limit
    code_ids = jnp.arange(num_codes, dtype=jnp.int32)
    onehot = ((codes_all[:, None] == code_ids[None, :]) & cached[:, None]).astype(jnp.bfloat16)
    cache_c = jnp.sum(onehot.astype(jnp.float32), axis=0)
    cache_v = lax.dot_general(
        onehot, vals_all, (((0,), (0,)), ((), ())), preferred_element_type=jnp.float32
    )

    ext_kv = jnp.concatenate([prev_kv, key_vals], axis=0)
    attended = attend_block(
        queries,
        ext_kv[:, :head_dim],
        ext_kv[:, head_dim:],
        cache_v,
        cache_c,
        codebook[0],
        reach[0],
        g > 0,
        BLK,
        scale,
    )

    return reduce_out(attended, w_out, sizes)


def project(tokens_in, w_qkv, sizes):
    nx, ny, nc = sizes
    n_head = nx * ny * nc
    core_perm = _core_perm(*sizes)
    me_c = lax.axis_index("hc")
    rows, width = tokens_in.shape
    half = rows // nc
    spread = jnp.broadcast_to(
        tokens_in.reshape(1, nc, half, width), (n_head // nc, nc, half, width)
    ).reshape(n_head, half, width)
    mine = lax.all_to_all(spread, HEAD_AXES, 0, 0, tiled=True)
    theirs = _send(mine, core_perm)
    w_local = w_qkv[:, 0, :].reshape(n_head, width, -1)
    dims = (((0, 2), (0, 1)), ((), ()))
    proj_own = lax.dot_general(mine, w_local, dims, preferred_element_type=jnp.float32)
    proj_oth = lax.dot_general(theirs, w_local, dims, preferred_element_type=jnp.float32)
    projected = jnp.where(
        me_c == 0,
        jnp.concatenate([proj_own, proj_oth], axis=0),
        jnp.concatenate([proj_oth, proj_own], axis=0),
    )
    return projected


def reduce_out(attended, w_out, sizes):
    nx, ny, nc = sizes
    n_head = nx * ny * nc
    core_perm = _core_perm(*sizes)
    me_c = lax.axis_index("hc")
    rows = attended.shape[0]
    w_full = w_out[0]
    cols = w_full.shape[1] // nc
    full = jnp.dot(attended, w_full, preferred_element_type=jnp.float32)
    keep = lax.dynamic_slice_in_dim(full, me_c * cols, cols, 1)
    give = lax.dynamic_slice_in_dim(full, (1 - me_c) * cols, cols, 1)
    got = _send(give.astype(jnp.bfloat16), core_perm)
    summed = (keep + got.astype(jnp.float32)).astype(jnp.bfloat16)
    chunks = summed.reshape(n_head, rows // n_head, cols)
    parts = lax.all_to_all(chunks, HEAD_AXES, 0, 0, tiled=True).astype(jnp.float32)
    parts = parts.reshape(n_head // nc, nc, rows // n_head, cols).sum(axis=0)
    out = jnp.concatenate([parts[i] for i in range(nc)], axis=1)
    return out.astype(jnp.bfloat16)


def solution(mesh):
    n_ctx, n_head = mesh.devices.shape
    devices = mesh.devices.reshape(n_ctx, 4, 4, n_head // 16)
    grid = Mesh(devices, ("ctx",) + HEAD_AXES)
    in_specs = (
        P("ctx", HEAD_AXES),
        P(None, HEAD_AXES, None),
        P(HEAD_AXES, None, None),
        P(HEAD_AXES, None, None),
        P(HEAD_AXES, "ctx"),
        P("ctx"),
    )
    out_specs = P(("ctx",) + HEAD_AXES, None)
    return jax.shard_map(
        on_device, mesh=grid, in_specs=in_specs, out_specs=out_specs, check_vma=False
    )
```

```python
import math

import jax
import jax.numpy as jnp
from jax import lax
from jax.sharding import Mesh
from jax.sharding import PartitionSpec as P

BLK = 256
HEAD_AXES = ("hx", "hy", "hc")


def _flat(x, y, c, ny, nc):
    return (x * ny + y) * nc + c


def _ring_perm(stage, d, nx, ny, nc):
    pairs = []
    for x in range(nx):
        for y in range(ny):
            for c in range(nc):
                along_y = (c == 0) == (stage == 0)
                if along_y:
                    tx, ty = x, (y + d) % ny
                else:
                    tx, ty = (x + d) % nx, y
                pairs.append((_flat(x, y, c, ny, nc), _flat(tx, ty, c, ny, nc)))
    return pairs


def _core_perm(nx, ny, nc):
    pairs = []
    for x in range(nx):
        for y in range(ny):
            for c in range(nc):
                pairs.append((_flat(x, y, c, ny, nc), _flat(x, y, 1 - c, ny, nc)))
    return pairs


def _send(value, perm):
    return lax.ppermute(value, HEAD_AXES, perm)


def gather_ring(blk, stage, sizes):
    p1 = _send(blk, _ring_perm(stage, 1, *sizes))
    m1 = _send(blk, _ring_perm(stage, -1, *sizes))
    h = blk.shape[0] // 2
    a = _send(p1[:h], _ring_perm(stage, 1, *sizes))
    b = _send(m1[h:], _ring_perm(stage, -1, *sizes))
    far = jnp.concatenate([a, b], axis=0)
    return jnp.stack([blk, p1, far, m1])


def reduce_ring(data, stage, sizes):
    h = data.shape[1] // 2
    rp = _send(data[2, :h].astype(jnp.bfloat16), _ring_perm(stage, 1, *sizes))
    rm = _send(data[2, h:].astype(jnp.bfloat16), _ring_perm(stage, -1, *sizes))
    ahead = jnp.concatenate([data[1, :h] + rp, data[1, h:]], axis=0)
    behind = jnp.concatenate([data[3, :h], data[3, h:] + rm], axis=0)
    gp = _send(ahead.astype(jnp.bfloat16), _ring_perm(stage, 1, *sizes))
    gm = _send(behind.astype(jnp.bfloat16), _ring_perm(stage, -1, *sizes))
    return data[0] + gp.astype(jnp.float32) + gm.astype(jnp.float32)


def attend_block(
    queries, keys_win, vals_win, cache_v, cache_c, book, reach_one, prev_flag, block_len, scale
):
    exact = (
        lax.dot_general(
            queries, keys_win, (((1,), (1,)), ((), ())), preferred_element_type=jnp.float32
        )
        * scale
    )
    coded = (
        lax.dot_general(queries, book, (((1,), (1,)), ((), ())), preferred_element_type=jnp.float32)
        * scale
    )
    rows = lax.broadcasted_iota(jnp.int32, exact.shape, 0)
    cols = lax.broadcasted_iota(jnp.int32, exact.shape, 1)
    prev_ok = (cols < block_len) & (cols >= block_len - reach_one) & prev_flag
    curr_ok = (cols >= block_len) & (cols - block_len <= rows)
    allowed = prev_ok | curr_ok
    valid = cache_c > 0.5
    top = jnp.maximum(
        jnp.max(jnp.where(allowed, exact, -jnp.inf), axis=1),
        jnp.max(jnp.where(valid[None, :], coded, -jnp.inf), axis=1),
    )
    probs = jnp.exp(jnp.where(allowed, exact - top[:, None], -jnp.inf))
    weights = jnp.exp(jnp.where(valid[None, :], coded - top[:, None], -jnp.inf))
    numer = jnp.dot(probs.astype(jnp.bfloat16), vals_win, preferred_element_type=jnp.float32)
    numer = numer + jnp.dot(weights, cache_v, precision=lax.Precision.HIGHEST)
    denom = jnp.sum(probs, axis=1) + jnp.dot(weights, cache_c, precision=lax.Precision.HIGHEST)
    return (numer / denom[:, None]).astype(jnp.bfloat16)


def on_device(tokens_in, w_qkv, w_out, codebook, codes, reach):
    nx, ny, nc = lax.axis_size("hx"), lax.axis_size("hy"), lax.axis_size("hc")
    sizes = (nx, ny, nc)
    core_perm = _core_perm(*sizes)
    me_x, me_y, me_c = lax.axis_index("hx"), lax.axis_index("hy"), lax.axis_index("hc")
    n_ctx = lax.axis_size("ctx")
    g = lax.axis_index("ctx")
    rows, width = tokens_in.shape
    head_dim = codebook.shape[2]
    num_codes = codebook.shape[1]
    scale = 1.0 / math.sqrt(head_dim)
    half = rows // 2

    projected = project(tokens_in, w_qkv, sizes)
    queries = projected[:, :head_dim].astype(jnp.bfloat16)
    key_vals = projected[:, head_dim:].astype(jnp.bfloat16)
    values = key_vals[:, head_dim:]

    code_row = codes[0]
    code_ids = jnp.arange(num_codes, dtype=jnp.int32)
    hi = (code_row // 16).astype(jnp.bfloat16).reshape(1, -1)
    lo = (code_row % 16).astype(jnp.bfloat16).reshape(1, -1)
    kvw = key_vals.shape[1]
    code_rows = jnp.pad(jnp.concatenate([hi, lo], axis=0), ((0, 0), (0, kvw - rows)))
    kv_blob = jnp.concatenate([key_vals, code_rows, jnp.zeros((14, kvw), jnp.bfloat16)], axis=0)
    route = [(i, i + 1) for i in range(n_ctx - 1)]
    prev_blob = lax.ppermute(kv_blob, "ctx", route)
    prev_kv = prev_blob[:rows]
    prev_codes = (
        prev_blob[rows, :rows].astype(jnp.int32) * 16 + prev_blob[rows + 1, :rows].astype(jnp.int32)
    )

    onehot_own = (code_row[:, None] == code_ids[None, :]).astype(jnp.bfloat16)
    sums = lax.dot_general(
        onehot_own, values, (((0,), (0,)), ((), ())), preferred_element_type=jnp.float32
    )
    counts = jnp.sum(onehot_own.astype(jnp.float32), axis=0)
    span = num_codes // n_ctx
    cache_v, cache_c = code_prefix(sums, counts, span, n_ctx, head_dim)
    prev_ok = (jnp.arange(rows, dtype=jnp.int32) < BLK - reach[0]) & (g > 0)
    onehot_prev = (
        (prev_codes[:, None] == code_ids[None, :]) & prev_ok[:, None]
    ).astype(jnp.bfloat16)
    cache_v = cache_v + lax.dot_general(
        onehot_prev, prev_kv[:, head_dim:], (((0,), (0,)), ((), ())),
        preferred_element_type=jnp.float32,
    )
    cache_c = cache_c + jnp.sum(onehot_prev.astype(jnp.float32), axis=0)

    ext_kv = jnp.concatenate([prev_kv, key_vals], axis=0)
    attended = attend_block(
        queries,
        ext_kv[:, :head_dim],
        ext_kv[:, head_dim:],
        cache_v,
        cache_c,
        codebook[0],
        reach[0],
        g > 0,
        BLK,
        scale,
    )

    return reduce_out(attended, w_out, sizes)


def _pack(sums, counts, span, n, head_dim):
    hi = jnp.floor(counts / 64.0)
    lo = counts - hi * 64.0
    tail = jnp.zeros((n, 8, head_dim), jnp.float32)
    tail = tail.at[:, 0, :span].set(hi.reshape(n, span)).at[:, 1, :span].set(lo.reshape(n, span))
    return jnp.concatenate([sums.reshape(n, span, head_dim), tail], axis=1).astype(jnp.bfloat16)


def _unpack(blob, span):
    blob = blob.astype(jnp.float32)
    sums = blob[:, :span]
    counts = blob[:, span, :span] * 64.0 + blob[:, span + 1, :span]
    return sums, counts


def code_prefix(sums, counts, span, n, head_dim):
    got = lax.all_to_all(_pack(sums, counts, span, n, head_dim), "ctx", 0, 0, tiled=True)
    block_sums, block_counts = _unpack(got, span)
    b = jnp.arange(n, dtype=jnp.int32)
    before = (b[None, :] <= b[:, None] - 2).astype(jnp.bfloat16)
    pre_sums = jnp.einsum(
        "bc,cxd->bxd", before, block_sums.astype(jnp.bfloat16), preferred_element_type=jnp.float32
    )
    pre_counts = jnp.dot(
        before, block_counts.astype(jnp.bfloat16), preferred_element_type=jnp.float32
    )
    back = lax.all_to_all(_pack(pre_sums, pre_counts, span, n, head_dim), "ctx", 0, 0, tiled=True)
    cache_v, cache_c = _unpack(back, span)
    return cache_v.reshape(n * span, head_dim), cache_c.reshape(n * span)


def project(tokens_in, w_qkv, sizes):
    nx, ny, nc = sizes
    n_head = nx * ny * nc
    core_perm = _core_perm(*sizes)
    me_c = lax.axis_index("hc")
    rows, width = tokens_in.shape
    half = rows // nc
    spread = jnp.broadcast_to(
        tokens_in.reshape(1, nc, half, width), (n_head // nc, nc, half, width)
    ).reshape(n_head, half, width)
    mine = lax.all_to_all(spread, HEAD_AXES, 0, 0, tiled=True)
    theirs = _send(mine, core_perm)
    w_local = w_qkv[:, 0, :].reshape(n_head, width, -1)
    dims = (((0, 2), (0, 1)), ((), ()))
    proj_own = lax.dot_general(mine, w_local, dims, preferred_element_type=jnp.float32)
    proj_oth = lax.dot_general(theirs, w_local, dims, preferred_element_type=jnp.float32)
    projected = jnp.where(
        me_c == 0,
        jnp.concatenate([proj_own, proj_oth], axis=0),
        jnp.concatenate([proj_oth, proj_own], axis=0),
    )
    return projected


def reduce_out(attended, w_out, sizes):
    nx, ny, nc = sizes
    n_head = nx * ny * nc
    core_perm = _core_perm(*sizes)
    me_c = lax.axis_index("hc")
    rows = attended.shape[0]
    w_full = w_out[0]
    cols = w_full.shape[1] // nc
    full = jnp.dot(attended, w_full, preferred_element_type=jnp.float32)
    keep = lax.dynamic_slice_in_dim(full, me_c * cols, cols, 1)
    give = lax.dynamic_slice_in_dim(full, (1 - me_c) * cols, cols, 1)
    got = _send(give.astype(jnp.bfloat16), core_perm)
    summed = (keep + got.astype(jnp.float32)).astype(jnp.bfloat16)
    chunks = summed.reshape(n_head, rows // n_head, cols)
    parts = lax.all_to_all(chunks, HEAD_AXES, 0, 0, tiled=True).astype(jnp.float32)
    parts = parts.reshape(n_head // nc, nc, rows // n_head, cols).sum(axis=0)
    out = jnp.concatenate([parts[i] for i in range(nc)], axis=1)
    return out.astype(jnp.bfloat16)


def solution(mesh):
    n_ctx, n_head = mesh.devices.shape
    devices = mesh.devices.reshape(n_ctx, 4, 4, n_head // 16)
    grid = Mesh(devices, ("ctx",) + HEAD_AXES)
    in_specs = (
        P("ctx", HEAD_AXES),
        P(None, HEAD_AXES, None),
        P(HEAD_AXES, None, None),
        P(HEAD_AXES, None, None),
        P(HEAD_AXES, "ctx"),
        P("ctx"),
    )
    out_specs = P(("ctx",) + HEAD_AXES, None)
    return jax.shard_map(
        on_device, mesh=grid, in_specs=in_specs, out_specs=out_specs, check_vma=False
    )
```

```python
import math

import jax
import jax.numpy as jnp
from jax import lax
from jax.sharding import Mesh
from jax.sharding import PartitionSpec as P

BLK = 256
HEAD_AXES = ("hx", "hy", "hc")


def _flat(x, y, c, ny, nc):
    return (x * ny + y) * nc + c


def _ring_perm(stage, d, nx, ny, nc):
    pairs = []
    for x in range(nx):
        for y in range(ny):
            for c in range(nc):
                along_y = (c == 0) == (stage == 0)
                if along_y:
                    tx, ty = x, (y + d) % ny
                else:
                    tx, ty = (x + d) % nx, y
                pairs.append((_flat(x, y, c, ny, nc), _flat(tx, ty, c, ny, nc)))
    return pairs


def _core_perm(nx, ny, nc):
    pairs = []
    for x in range(nx):
        for y in range(ny):
            for c in range(nc):
                pairs.append((_flat(x, y, c, ny, nc), _flat(x, y, 1 - c, ny, nc)))
    return pairs


def _send(value, perm):
    return lax.ppermute(value, HEAD_AXES, perm)


def gather_ring(blk, stage, sizes):
    p1 = _send(blk, _ring_perm(stage, 1, *sizes))
    m1 = _send(blk, _ring_perm(stage, -1, *sizes))
    h = blk.shape[0] // 2
    a = _send(p1[:h], _ring_perm(stage, 1, *sizes))
    b = _send(m1[h:], _ring_perm(stage, -1, *sizes))
    far = jnp.concatenate([a, b], axis=0)
    return jnp.stack([blk, p1, far, m1])


def reduce_ring(data, stage, sizes):
    h = data.shape[1] // 2
    rp = _send(data[2, :h].astype(jnp.bfloat16), _ring_perm(stage, 1, *sizes))
    rm = _send(data[2, h:].astype(jnp.bfloat16), _ring_perm(stage, -1, *sizes))
    ahead = jnp.concatenate([data[1, :h] + rp, data[1, h:]], axis=0)
    behind = jnp.concatenate([data[3, :h], data[3, h:] + rm], axis=0)
    gp = _send(ahead.astype(jnp.bfloat16), _ring_perm(stage, 1, *sizes))
    gm = _send(behind.astype(jnp.bfloat16), _ring_perm(stage, -1, *sizes))
    return data[0] + gp.astype(jnp.float32) + gm.astype(jnp.float32)


def attend_exact(queries, keys_win, vals_win, book, reach_one, prev_flag, block_len, scale):
    exact = (
        lax.dot_general(
            queries, keys_win, (((1,), (1,)), ((), ())), preferred_element_type=jnp.float32
        )
        * scale
    )
    coded = (
        lax.dot_general(queries, book, (((1,), (1,)), ((), ())), preferred_element_type=jnp.float32)
        * scale
    )
    rows = lax.broadcasted_iota(jnp.int32, exact.shape, 0)
    cols = lax.broadcasted_iota(jnp.int32, exact.shape, 1)
    prev_ok = (cols < block_len) & (cols >= block_len - reach_one) & prev_flag
    curr_ok = (cols >= block_len) & (cols - block_len <= rows)
    allowed = prev_ok | curr_ok
    top_e = jnp.max(jnp.where(allowed, exact, -jnp.inf), axis=1)
    probs = jnp.exp(jnp.where(allowed, exact - top_e[:, None], -jnp.inf))
    numer = jnp.dot(probs.astype(jnp.bfloat16), vals_win, preferred_element_type=jnp.float32)
    denom = jnp.sum(probs, axis=1)
    return top_e, numer, denom, coded


def attend_cache(top_e, numer_e, denom_e, coded, cache_v, cache_c):
    valid = cache_c > 0.5
    top = jnp.maximum(top_e, jnp.max(jnp.where(valid[None, :], coded, -jnp.inf), axis=1))
    alpha = jnp.exp(top_e - top)
    weights = jnp.exp(jnp.where(valid[None, :], coded - top[:, None], -jnp.inf))
    numer = alpha[:, None] * numer_e + jnp.dot(weights, cache_v, precision=lax.Precision.HIGHEST)
    denom = alpha * denom_e + jnp.dot(weights, cache_c, precision=lax.Precision.HIGHEST)
    return (numer / denom[:, None]).astype(jnp.bfloat16)


def on_device(tokens_in, w_qkv, w_out, codebook, codes, reach):
    nx, ny, nc = lax.axis_size("hx"), lax.axis_size("hy"), lax.axis_size("hc")
    sizes = (nx, ny, nc)
    core_perm = _core_perm(*sizes)
    me_x, me_y, me_c = lax.axis_index("hx"), lax.axis_index("hy"), lax.axis_index("hc")
    n_ctx = lax.axis_size("ctx")
    g = lax.axis_index("ctx")
    rows, width = tokens_in.shape
    head_dim = codebook.shape[2]
    num_codes = codebook.shape[1]
    scale = 1.0 / math.sqrt(head_dim)
    half = rows // 2

    projected = project(tokens_in, w_qkv, sizes)
    queries = projected[:, :head_dim].astype(jnp.bfloat16)
    key_vals = projected[:, head_dim:].astype(jnp.bfloat16)
    values = key_vals[:, head_dim:]

    code_row = codes[0]
    code_ids = jnp.arange(num_codes, dtype=jnp.int32)
    hi = (code_row // 16).astype(jnp.bfloat16).reshape(1, -1)
    lo = (code_row % 16).astype(jnp.bfloat16).reshape(1, -1)
    kvw = key_vals.shape[1]
    code_rows = jnp.pad(jnp.concatenate([hi, lo], axis=0), ((0, 0), (0, kvw - rows)))
    kv_blob = jnp.concatenate([key_vals, code_rows, jnp.zeros((14, kvw), jnp.bfloat16)], axis=0)
    route = [(i, i + 1) for i in range(n_ctx - 1)]
    prev_blob = lax.ppermute(kv_blob, "ctx", route)
    prev_kv = prev_blob[:rows]
    prev_codes = (
        prev_blob[rows, :rows].astype(jnp.int32) * 16 + prev_blob[rows + 1, :rows].astype(jnp.int32)
    )

    onehot_own = (code_row[:, None] == code_ids[None, :]).astype(jnp.bfloat16)
    sums = lax.dot_general(
        onehot_own, values, (((0,), (0,)), ((), ())), preferred_element_type=jnp.float32
    )
    counts = jnp.sum(onehot_own.astype(jnp.float32), axis=0)
    span = num_codes // n_ctx
    cache_v, cache_c = code_prefix(sums, counts, span, n_ctx, head_dim)
    prev_ok = (jnp.arange(rows, dtype=jnp.int32) < BLK - reach[0]) & (g > 0)
    onehot_prev = (
        (prev_codes[:, None] == code_ids[None, :]) & prev_ok[:, None]
    ).astype(jnp.bfloat16)
    cache_v = cache_v + lax.dot_general(
        onehot_prev, prev_kv[:, head_dim:], (((0,), (0,)), ((), ())),
        preferred_element_type=jnp.float32,
    )
    cache_c = cache_c + jnp.sum(onehot_prev.astype(jnp.float32), axis=0)

    ext_kv = jnp.concatenate([prev_kv, key_vals], axis=0)
    top_e, numer_e, denom_e, coded = attend_exact(
        queries,
        ext_kv[:, :head_dim],
        ext_kv[:, head_dim:],
        codebook[0],
        reach[0],
        g > 0,
        BLK,
        scale,
    )
    attended = attend_cache(top_e, numer_e, denom_e, coded, cache_v, cache_c)

    return reduce_out(attended, w_out, sizes)


def _pack(sums, counts, span, n, head_dim):
    hi = jnp.floor(counts / 64.0)
    lo = counts - hi * 64.0
    tail = jnp.zeros((n, 8, head_dim), jnp.float32)
    tail = tail.at[:, 0, :span].set(hi.reshape(n, span)).at[:, 1, :span].set(lo.reshape(n, span))
    return jnp.concatenate([sums.reshape(n, span, head_dim), tail], axis=1).astype(jnp.bfloat16)


def _unpack(blob, span):
    blob = blob.astype(jnp.float32)
    sums = blob[:, :span]
    counts = blob[:, span, :span] * 64.0 + blob[:, span + 1, :span]
    return sums, counts


def code_prefix(sums, counts, span, n, head_dim):
    got = lax.all_to_all(_pack(sums, counts, span, n, head_dim), "ctx", 0, 0, tiled=True)
    block_sums, block_counts = _unpack(got, span)
    b = jnp.arange(n, dtype=jnp.int32)
    before = (b[None, :] <= b[:, None] - 2).astype(jnp.bfloat16)
    pre_sums = jnp.einsum(
        "bc,cxd->bxd", before, block_sums.astype(jnp.bfloat16), preferred_element_type=jnp.float32
    )
    pre_counts = jnp.dot(
        before, block_counts.astype(jnp.bfloat16), preferred_element_type=jnp.float32
    )
    back = lax.all_to_all(_pack(pre_sums, pre_counts, span, n, head_dim), "ctx", 0, 0, tiled=True)
    cache_v, cache_c = _unpack(back, span)
    return cache_v.reshape(n * span, head_dim), cache_c.reshape(n * span)


def project(tokens_in, w_qkv, sizes):
    nx, ny, nc = sizes
    n_head = nx * ny * nc
    core_perm = _core_perm(*sizes)
    me_c = lax.axis_index("hc")
    rows, width = tokens_in.shape
    half = rows // nc
    spread = jnp.broadcast_to(
        tokens_in.reshape(1, nc, half, width), (n_head // nc, nc, half, width)
    ).reshape(n_head, half, width)
    mine = lax.all_to_all(spread, HEAD_AXES, 0, 0, tiled=True)
    theirs = _send(mine, core_perm)
    w_local = w_qkv[:, 0, :].reshape(n_head, width, -1)
    dims = (((0, 2), (0, 1)), ((), ()))
    proj_own = lax.dot_general(mine, w_local, dims, preferred_element_type=jnp.float32)
    proj_oth = lax.dot_general(theirs, w_local, dims, preferred_element_type=jnp.float32)
    projected = jnp.where(
        me_c == 0,
        jnp.concatenate([proj_own, proj_oth], axis=0),
        jnp.concatenate([proj_oth, proj_own], axis=0),
    )
    return projected


def reduce_out(attended, w_out, sizes):
    nx, ny, nc = sizes
    n_head = nx * ny * nc
    core_perm = _core_perm(*sizes)
    me_c = lax.axis_index("hc")
    rows = attended.shape[0]
    w_full = w_out[0]
    cols = w_full.shape[1] // nc
    full = jnp.dot(attended, w_full, preferred_element_type=jnp.float32)
    keep = lax.dynamic_slice_in_dim(full, me_c * cols, cols, 1)
    give = lax.dynamic_slice_in_dim(full, (1 - me_c) * cols, cols, 1)
    got = _send(give.astype(jnp.bfloat16), core_perm)
    summed = (keep + got.astype(jnp.float32)).astype(jnp.bfloat16)
    chunks = summed.reshape(n_head, rows // n_head, cols)
    parts = lax.all_to_all(chunks, HEAD_AXES, 0, 0, tiled=True).astype(jnp.float32)
    parts = parts.reshape(n_head // nc, nc, rows // n_head, cols).sum(axis=0)
    out = jnp.concatenate([parts[i] for i in range(nc)], axis=1)
    return out.astype(jnp.bfloat16)


def solution(mesh):
    n_ctx, n_head = mesh.devices.shape
    devices = mesh.devices.reshape(n_ctx, 4, 4, n_head // 16)
    grid = Mesh(devices, ("ctx",) + HEAD_AXES)
    in_specs = (
        P("ctx", HEAD_AXES),
        P(None, HEAD_AXES, None),
        P(HEAD_AXES, None, None),
        P(HEAD_AXES, None, None),
        P(HEAD_AXES, "ctx"),
        P("ctx"),
    )
    out_specs = P(("ctx",) + HEAD_AXES, None)
    return jax.shard_map(
        on_device, mesh=grid, in_specs=in_specs, out_specs=out_specs, check_vma=False
    )
```

```python
import math

import jax
import jax.numpy as jnp
from jax import lax
from jax.sharding import Mesh
from jax.sharding import PartitionSpec as P

BLK = 256
HEAD_AXES = ("hx", "hy", "hc")


def _flat(x, y, c, ny, nc):
    return (x * ny + y) * nc + c


def _ring_perm(stage, d, nx, ny, nc):
    pairs = []
    for x in range(nx):
        for y in range(ny):
            for c in range(nc):
                along_y = (c == 0) == (stage == 0)
                if along_y:
                    tx, ty = x, (y + d) % ny
                else:
                    tx, ty = (x + d) % nx, y
                pairs.append((_flat(x, y, c, ny, nc), _flat(tx, ty, c, ny, nc)))
    return pairs


def _core_perm(nx, ny, nc):
    pairs = []
    for x in range(nx):
        for y in range(ny):
            for c in range(nc):
                pairs.append((_flat(x, y, c, ny, nc), _flat(x, y, 1 - c, ny, nc)))
    return pairs


def _send(value, perm):
    return lax.ppermute(value, HEAD_AXES, perm)


def gather_ring(blk, stage, sizes):
    p1 = _send(blk, _ring_perm(stage, 1, *sizes))
    m1 = _send(blk, _ring_perm(stage, -1, *sizes))
    h = blk.shape[0] // 2
    a = _send(p1[:h], _ring_perm(stage, 1, *sizes))
    b = _send(m1[h:], _ring_perm(stage, -1, *sizes))
    far = jnp.concatenate([a, b], axis=0)
    return jnp.stack([blk, p1, far, m1])


def reduce_ring(data, stage, sizes):
    h = data.shape[1] // 2
    rp = _send(data[2, :h].astype(jnp.bfloat16), _ring_perm(stage, 1, *sizes))
    rm = _send(data[2, h:].astype(jnp.bfloat16), _ring_perm(stage, -1, *sizes))
    ahead = jnp.concatenate([data[1, :h] + rp, data[1, h:]], axis=0)
    behind = jnp.concatenate([data[3, :h], data[3, h:] + rm], axis=0)
    gp = _send(ahead.astype(jnp.bfloat16), _ring_perm(stage, 1, *sizes))
    gm = _send(behind.astype(jnp.bfloat16), _ring_perm(stage, -1, *sizes))
    return data[0] + gp.astype(jnp.float32) + gm.astype(jnp.float32)


def attend_exact(queries, keys_win, vals_win, book, reach_one, prev_flag, block_len, scale):
    exact = (
        lax.dot_general(
            queries, keys_win, (((1,), (1,)), ((), ())), preferred_element_type=jnp.float32
        )
        * scale
    )
    coded = (
        lax.dot_general(queries, book, (((1,), (1,)), ((), ())), preferred_element_type=jnp.float32)
        * scale
    )
    rows = lax.broadcasted_iota(jnp.int32, exact.shape, 0)
    cols = lax.broadcasted_iota(jnp.int32, exact.shape, 1)
    prev_ok = (cols < block_len) & (cols >= block_len - reach_one) & prev_flag
    curr_ok = (cols >= block_len) & (cols - block_len <= rows)
    allowed = prev_ok | curr_ok
    top_e = jnp.max(jnp.where(allowed, exact, -jnp.inf), axis=1)
    probs = jnp.exp(jnp.where(allowed, exact - top_e[:, None], -jnp.inf))
    numer = jnp.dot(probs.astype(jnp.bfloat16), vals_win, preferred_element_type=jnp.float32)
    denom = jnp.sum(probs, axis=1)
    return top_e, numer, denom, coded


def attend_cache(top_e, numer_e, denom_e, coded, cache_v, cache_c):
    valid = cache_c > 0.5
    top = jnp.maximum(top_e, jnp.max(jnp.where(valid[None, :], coded, -jnp.inf), axis=1))
    alpha = jnp.exp(top_e - top)
    weights = jnp.exp(jnp.where(valid[None, :], coded - top[:, None], -jnp.inf))
    numer = alpha[:, None] * numer_e + jnp.dot(weights, cache_v, precision=lax.Precision.HIGHEST)
    denom = alpha * denom_e + jnp.dot(weights, cache_c, precision=lax.Precision.HIGHEST)
    return (numer / denom[:, None]).astype(jnp.bfloat16)


def on_device(tokens_in, w_qkv, w_out, codebook, codes, reach):
    nx, ny, nc = lax.axis_size("hx"), lax.axis_size("hy"), lax.axis_size("hc")
    sizes = (nx, ny, nc)
    core_perm = _core_perm(*sizes)
    me_x, me_y, me_c = lax.axis_index("hx"), lax.axis_index("hy"), lax.axis_index("hc")
    n_ctx = lax.axis_size("ctx")
    g = lax.axis_index("ctx")
    rows, width = tokens_in.shape
    head_dim = codebook.shape[2]
    num_codes = codebook.shape[1]
    scale = 1.0 / math.sqrt(head_dim)
    half = rows // 2

    projected = project(tokens_in, w_qkv, sizes)
    queries = projected[:, :head_dim].astype(jnp.bfloat16)
    key_vals = projected[:, head_dim:].astype(jnp.bfloat16)
    values = key_vals[:, head_dim:]

    code_row = codes[0]
    code_ids = jnp.arange(num_codes, dtype=jnp.int32)
    hi = (code_row // 16).astype(jnp.bfloat16).reshape(1, -1)
    lo = (code_row % 16).astype(jnp.bfloat16).reshape(1, -1)
    kvw = key_vals.shape[1]
    code_rows = jnp.pad(jnp.concatenate([hi, lo], axis=0), ((0, 0), (0, kvw - rows)))
    kv_blob = jnp.concatenate([key_vals, code_rows, jnp.zeros((14, kvw), jnp.bfloat16)], axis=0)
    route = [(i, i + 1) for i in range(n_ctx - 1)]
    prev_blob = lax.ppermute(kv_blob, "ctx", route)
    prev_kv = prev_blob[:rows]
    prev_codes = (
        prev_blob[rows, :rows].astype(jnp.int32) * 16 + prev_blob[rows + 1, :rows].astype(jnp.int32)
    )

    onehot_own = (code_row[:, None] == code_ids[None, :]).astype(jnp.bfloat16)
    sums = lax.dot_general(
        onehot_own, values, (((0,), (0,)), ((), ())), preferred_element_type=jnp.float32
    )
    counts = jnp.sum(onehot_own.astype(jnp.float32), axis=0)
    span = num_codes // n_ctx
    cache_v, cache_c = code_prefix(sums, counts, span, n_ctx, head_dim)
    prev_ok = (jnp.arange(rows, dtype=jnp.int32) < BLK - reach[0]) & (g > 0)
    onehot_prev = (
        (prev_codes[:, None] == code_ids[None, :]) & prev_ok[:, None]
    ).astype(jnp.bfloat16)
    cache_v = cache_v + lax.dot_general(
        onehot_prev, prev_kv[:, head_dim:], (((0,), (0,)), ((), ())),
        preferred_element_type=jnp.float32,
    )
    cache_c = cache_c + jnp.sum(onehot_prev.astype(jnp.float32), axis=0)

    ext_kv = jnp.concatenate([prev_kv, key_vals], axis=0)
    top_e, numer_e, denom_e, coded = attend_exact(
        queries,
        ext_kv[:, :head_dim],
        ext_kv[:, head_dim:],
        codebook[0],
        reach[0],
        g > 0,
        BLK,
        scale,
    )
    attended = attend_cache(top_e, numer_e, denom_e, coded, cache_v, cache_c)

    return reduce_out(attended, w_out, sizes)


def _pack(sums, counts, span, n, head_dim):
    hi = jnp.floor(counts / 64.0)
    lo = counts - hi * 64.0
    tail = jnp.zeros((n, 8, head_dim), jnp.float32)
    tail = tail.at[:, 0, :span].set(hi.reshape(n, span)).at[:, 1, :span].set(lo.reshape(n, span))
    return jnp.concatenate([sums.reshape(n, span, head_dim), tail], axis=1).astype(jnp.bfloat16)


def _unpack(blob, span):
    blob = blob.astype(jnp.float32)
    sums = blob[:, :span]
    counts = blob[:, span, :span] * 64.0 + blob[:, span + 1, :span]
    return sums, counts


def code_prefix(sums, counts, span, n, head_dim):
    got = lax.all_to_all(_pack(sums, counts, span, n, head_dim), "ctx", 0, 0, tiled=True)
    block_sums, block_counts = _unpack(got, span)
    b = jnp.arange(n, dtype=jnp.int32)
    before = (b[None, :] <= b[:, None] - 2).astype(jnp.bfloat16)
    pre_sums = jnp.einsum(
        "bc,cxd->bxd", before, block_sums.astype(jnp.bfloat16), preferred_element_type=jnp.float32
    )
    pre_counts = jnp.dot(
        before, block_counts.astype(jnp.bfloat16), preferred_element_type=jnp.float32
    )
    back = lax.all_to_all(_pack(pre_sums, pre_counts, span, n, head_dim), "ctx", 0, 0, tiled=True)
    cache_v, cache_c = _unpack(back, span)
    return cache_v.reshape(n * span, head_dim), cache_c.reshape(n * span)


def project(tokens_in, w_qkv, sizes):
    nx, ny, nc = sizes
    n_head = nx * ny * nc
    core_perm = _core_perm(*sizes)
    me_c = lax.axis_index("hc")
    rows, width = tokens_in.shape
    half = rows // nc
    spread = jnp.broadcast_to(
        tokens_in.reshape(1, nc, half, width), (ny, nc, half, width)
    ).reshape(ny * nc, half, width)
    row_of_x = lax.all_to_all(spread, ("hy", "hc"), 0, 0, tiled=True)
    wide = jnp.broadcast_to(row_of_x[None], (nx,) + row_of_x.shape)
    mine = lax.all_to_all(wide, "hx", 0, 0, tiled=True).reshape(n_head, half, width)
    theirs = _send(mine, core_perm)
    w_local = w_qkv[:, 0, :].reshape(n_head, width, -1)
    dims = (((0, 2), (0, 1)), ((), ()))
    proj_own = lax.dot_general(mine, w_local, dims, preferred_element_type=jnp.float32)
    proj_oth = lax.dot_general(theirs, w_local, dims, preferred_element_type=jnp.float32)
    projected = jnp.where(
        me_c == 0,
        jnp.concatenate([proj_own, proj_oth], axis=0),
        jnp.concatenate([proj_oth, proj_own], axis=0),
    )
    return projected


def reduce_out(attended, w_out, sizes):
    nx, ny, nc = sizes
    core_perm = _core_perm(*sizes)
    me_c = lax.axis_index("hc")
    rows = attended.shape[0]
    w_full = w_out[0]
    cols = w_full.shape[1] // nc
    w_keep = lax.dynamic_slice_in_dim(w_full, me_c * cols, cols, 1)
    w_give = lax.dynamic_slice_in_dim(w_full, (1 - me_c) * cols, cols, 1)
    keep = jnp.dot(attended, w_keep, preferred_element_type=jnp.float32)
    give = jnp.dot(attended, w_give, preferred_element_type=jnp.float32).astype(jnp.bfloat16)
    got = _send(give, core_perm)
    summed = (keep + got.astype(jnp.float32)).astype(jnp.bfloat16)
    by_x = lax.all_to_all(summed.reshape(nx, rows // nx, cols), "hx", 0, 0, tiled=True)
    part = by_x.astype(jnp.float32).sum(axis=0).astype(jnp.bfloat16)
    chunks = part.reshape(ny * nc, rows // (nx * ny * nc), cols)
    parts = lax.all_to_all(chunks, ("hy", "hc"), 0, 0, tiled=True).astype(jnp.float32)
    parts = parts.reshape(ny, nc, rows // (nx * ny * nc), cols).sum(axis=0)
    out = jnp.concatenate([parts[i] for i in range(nc)], axis=1)
    return out.astype(jnp.bfloat16)


def solution(mesh):
    n_ctx, n_head = mesh.devices.shape
    devices = mesh.devices.reshape(n_ctx, 4, 4, n_head // 16)
    grid = Mesh(devices, ("ctx",) + HEAD_AXES)
    in_specs = (
        P("ctx", HEAD_AXES),
        P(None, HEAD_AXES, None),
        P(HEAD_AXES, None, None),
        P(HEAD_AXES, None, None),
        P(HEAD_AXES, "ctx"),
        P("ctx"),
    )
    out_specs = P(("ctx",) + HEAD_AXES, None)
    return jax.shard_map(
        on_device, mesh=grid, in_specs=in_specs, out_specs=out_specs, check_vma=False
    )
```

```python
import math

import jax
import jax.numpy as jnp
from jax import lax
from jax.sharding import Mesh
from jax.sharding import PartitionSpec as P

BLK = 256
HEAD_AXES = ("hx", "hy", "hc")


def _flat(x, y, c, ny, nc):
    return (x * ny + y) * nc + c


def _ring_perm(stage, d, nx, ny, nc):
    pairs = []
    for x in range(nx):
        for y in range(ny):
            for c in range(nc):
                along_y = (c == 0) == (stage == 0)
                if along_y:
                    tx, ty = x, (y + d) % ny
                else:
                    tx, ty = (x + d) % nx, y
                pairs.append((_flat(x, y, c, ny, nc), _flat(tx, ty, c, ny, nc)))
    return pairs


def _core_perm(nx, ny, nc):
    pairs = []
    for x in range(nx):
        for y in range(ny):
            for c in range(nc):
                pairs.append((_flat(x, y, c, ny, nc), _flat(x, y, 1 - c, ny, nc)))
    return pairs


def _send(value, perm):
    return lax.ppermute(value, HEAD_AXES, perm)


def gather_ring(blk, stage, sizes):
    p1 = _send(blk, _ring_perm(stage, 1, *sizes))
    m1 = _send(blk, _ring_perm(stage, -1, *sizes))
    h = blk.shape[0] // 2
    a = _send(p1[:h], _ring_perm(stage, 1, *sizes))
    b = _send(m1[h:], _ring_perm(stage, -1, *sizes))
    far = jnp.concatenate([a, b], axis=0)
    return jnp.stack([blk, p1, far, m1])


def reduce_ring(data, stage, sizes):
    h = data.shape[1] // 2
    rp = _send(data[2, :h].astype(jnp.bfloat16), _ring_perm(stage, 1, *sizes))
    rm = _send(data[2, h:].astype(jnp.bfloat16), _ring_perm(stage, -1, *sizes))
    ahead = jnp.concatenate([data[1, :h] + rp, data[1, h:]], axis=0)
    behind = jnp.concatenate([data[3, :h], data[3, h:] + rm], axis=0)
    gp = _send(ahead.astype(jnp.bfloat16), _ring_perm(stage, 1, *sizes))
    gm = _send(behind.astype(jnp.bfloat16), _ring_perm(stage, -1, *sizes))
    return data[0] + gp.astype(jnp.float32) + gm.astype(jnp.float32)


def attend_exact(queries, keys_win, vals_win, book, reach_one, prev_flag, block_len, scale):
    exact = (
        lax.dot_general(
            queries, keys_win, (((1,), (1,)), ((), ())), preferred_element_type=jnp.float32
        )
        * scale
    )
    coded = (
        lax.dot_general(queries, book, (((1,), (1,)), ((), ())), preferred_element_type=jnp.float32)
        * scale
    )
    rows = lax.broadcasted_iota(jnp.int32, exact.shape, 0)
    cols = lax.broadcasted_iota(jnp.int32, exact.shape, 1)
    prev_ok = (cols < block_len) & (cols >= block_len - reach_one) & prev_flag
    curr_ok = (cols >= block_len) & (cols - block_len <= rows)
    allowed = prev_ok | curr_ok
    top_e = jnp.max(jnp.where(allowed, exact, -jnp.inf), axis=1)
    probs = jnp.exp(jnp.where(allowed, exact - top_e[:, None], -jnp.inf))
    numer = jnp.dot(probs.astype(jnp.bfloat16), vals_win, preferred_element_type=jnp.float32)
    denom = jnp.sum(probs, axis=1)
    return top_e, numer, denom, coded


def attend_cache(top_e, numer_e, denom_e, coded, cache_v, cache_c):
    valid = cache_c > 0.5
    top = jnp.maximum(top_e, jnp.max(jnp.where(valid[None, :], coded, -jnp.inf), axis=1))
    alpha = jnp.exp(top_e - top)
    weights = jnp.exp(jnp.where(valid[None, :], coded - top[:, None], -jnp.inf))
    numer = alpha[:, None] * numer_e + jnp.dot(weights, cache_v, precision=lax.Precision.HIGHEST)
    denom = alpha * denom_e + jnp.dot(weights, cache_c, precision=lax.Precision.HIGHEST)
    return (numer / denom[:, None]).astype(jnp.bfloat16)


def on_device(tokens_in, w_qkv, w_out, codebook, codes, reach):
    nx, ny, nc = lax.axis_size("hx"), lax.axis_size("hy"), lax.axis_size("hc")
    sizes = (nx, ny, nc)
    core_perm = _core_perm(*sizes)
    me_x, me_y, me_c = lax.axis_index("hx"), lax.axis_index("hy"), lax.axis_index("hc")
    n_ctx = lax.axis_size("ctx")
    g = lax.axis_index("ctx")
    rows, width = tokens_in.shape
    head_dim = codebook.shape[2]
    num_codes = codebook.shape[1]
    scale = 1.0 / math.sqrt(head_dim)
    half = rows // 2

    projected = project(tokens_in, w_qkv, sizes)
    queries = projected[:, :head_dim].astype(jnp.bfloat16)
    key_vals = projected[:, head_dim:].astype(jnp.bfloat16)
    values = key_vals[:, head_dim:]

    code_row = codes[0]
    code_ids = jnp.arange(num_codes, dtype=jnp.int32)
    hi = (code_row // 16).astype(jnp.bfloat16).reshape(1, -1)
    lo = (code_row % 16).astype(jnp.bfloat16).reshape(1, -1)
    kvw = key_vals.shape[1]
    code_rows = jnp.pad(jnp.concatenate([hi, lo], axis=0), ((0, 0), (0, kvw - rows)))
    kv_blob = jnp.concatenate([key_vals, code_rows, jnp.zeros((14, kvw), jnp.bfloat16)], axis=0)
    route = [(i, i + 1) for i in range(n_ctx - 1)]
    prev_blob = lax.ppermute(kv_blob, "ctx", route)
    prev_kv = prev_blob[:rows]
    prev_codes = (
        prev_blob[rows, :rows].astype(jnp.int32) * 16 + prev_blob[rows + 1, :rows].astype(jnp.int32)
    )

    onehot_own = (code_row[:, None] == code_ids[None, :]).astype(jnp.bfloat16)
    sums = lax.dot_general(
        onehot_own, values, (((0,), (0,)), ((), ())), preferred_element_type=jnp.float32
    )
    counts = jnp.sum(onehot_own.astype(jnp.float32), axis=0)
    span = num_codes // n_ctx
    cache_v, cache_c = code_prefix(sums, counts, span, n_ctx, head_dim)
    prev_ok = (jnp.arange(rows, dtype=jnp.int32) < BLK - reach[0]) & (g > 0)
    onehot_prev = (
        (prev_codes[:, None] == code_ids[None, :]) & prev_ok[:, None]
    ).astype(jnp.bfloat16)
    cache_v = cache_v + lax.dot_general(
        onehot_prev, prev_kv[:, head_dim:], (((0,), (0,)), ((), ())),
        preferred_element_type=jnp.float32,
    )
    cache_c = cache_c + jnp.sum(onehot_prev.astype(jnp.float32), axis=0)

    ext_kv = jnp.concatenate([prev_kv, key_vals], axis=0)
    top_e, numer_e, denom_e, coded = attend_exact(
        queries,
        ext_kv[:, :head_dim],
        ext_kv[:, head_dim:],
        codebook[0],
        reach[0],
        g > 0,
        BLK,
        scale,
    )
    attended = attend_cache(top_e, numer_e, denom_e, coded, cache_v, cache_c)

    return reduce_out(attended, w_out, sizes)


def _pack(sums, counts, span, n, head_dim):
    hi = jnp.floor(counts / 64.0)
    lo = counts - hi * 64.0
    tail = jnp.zeros((n, 8, head_dim), jnp.float32)
    tail = tail.at[:, 0, :span].set(hi.reshape(n, span)).at[:, 1, :span].set(lo.reshape(n, span))
    return jnp.concatenate([sums.reshape(n, span, head_dim), tail], axis=1).astype(jnp.bfloat16)


def _unpack(blob, span):
    blob = blob.astype(jnp.float32)
    sums = blob[:, :span]
    counts = blob[:, span, :span] * 64.0 + blob[:, span + 1, :span]
    return sums, counts


def code_prefix(sums, counts, span, n, head_dim):
    got = lax.all_to_all(_pack(sums, counts, span, n, head_dim), "ctx", 0, 0, tiled=True)
    block_sums, block_counts = _unpack(got, span)
    b = jnp.arange(n, dtype=jnp.int32)
    before = (b[None, :] <= b[:, None] - 2).astype(jnp.bfloat16)
    pre_sums = jnp.einsum(
        "bc,cxd->bxd", before, block_sums.astype(jnp.bfloat16), preferred_element_type=jnp.float32
    )
    pre_counts = jnp.dot(
        before, block_counts.astype(jnp.bfloat16), preferred_element_type=jnp.float32
    )
    back = lax.all_to_all(_pack(pre_sums, pre_counts, span, n, head_dim), "ctx", 0, 0, tiled=True)
    cache_v, cache_c = _unpack(back, span)
    return cache_v.reshape(n * span, head_dim), cache_c.reshape(n * span)


def project(tokens_in, w_qkv, sizes):
    nx, ny, nc = sizes
    n_head = nx * ny * nc
    core_perm = _core_perm(*sizes)
    me_c = lax.axis_index("hc")
    rows, width = tokens_in.shape
    half = rows // nc
    spread = jnp.broadcast_to(
        tokens_in.reshape(1, nc, half, width), (n_head // nc, nc, half, width)
    ).reshape(n_head, half, width)
    mine = lax.all_to_all(spread, HEAD_AXES, 0, 0, tiled=True)
    theirs = _send(mine, core_perm)
    w_local = w_qkv[:, 0, :].reshape(n_head, width, -1)
    dims = (((0, 2), (0, 1)), ((), ()))
    proj_own = lax.dot_general(mine, w_local, dims, preferred_element_type=jnp.float32)
    proj_oth = lax.dot_general(theirs, w_local, dims, preferred_element_type=jnp.float32)
    projected = jnp.where(
        me_c == 0,
        jnp.concatenate([proj_own, proj_oth], axis=0),
        jnp.concatenate([proj_oth, proj_own], axis=0),
    )
    return projected


def reduce_out(attended, w_out, sizes):
    nx, ny, nc = sizes
    core_perm = _core_perm(*sizes)
    me_c = lax.axis_index("hc")
    rows = attended.shape[0]
    w_full = w_out[0]
    cols = w_full.shape[1] // nc
    w_keep = lax.dynamic_slice_in_dim(w_full, me_c * cols, cols, 1)
    w_give = lax.dynamic_slice_in_dim(w_full, (1 - me_c) * cols, cols, 1)
    keep = jnp.dot(attended, w_keep, preferred_element_type=jnp.float32)
    give = jnp.dot(attended, w_give, preferred_element_type=jnp.float32).astype(jnp.bfloat16)
    got = _send(give, core_perm)
    summed = (keep + got.astype(jnp.float32)).astype(jnp.bfloat16)
    n_head = nx * ny * nc
    chunks = summed.reshape(n_head, rows // n_head, cols)
    parts = lax.all_to_all(chunks, HEAD_AXES, 0, 0, tiled=True).astype(jnp.float32)
    parts = parts.reshape(n_head // nc, nc, rows // n_head, cols).sum(axis=0)
    out = jnp.concatenate([parts[i] for i in range(nc)], axis=1)
    return out.astype(jnp.bfloat16)


def solution(mesh):
    n_ctx, n_head = mesh.devices.shape
    devices = mesh.devices.reshape(n_ctx, 4, 4, n_head // 16)
    grid = Mesh(devices, ("ctx",) + HEAD_AXES)
    in_specs = (
        P("ctx", HEAD_AXES),
        P(None, HEAD_AXES, None),
        P(HEAD_AXES, None, None),
        P(HEAD_AXES, None, None),
        P(HEAD_AXES, "ctx"),
        P("ctx"),
    )
    out_specs = P(("ctx",) + HEAD_AXES, None)
    return jax.shard_map(
        on_device, mesh=grid, in_specs=in_specs, out_specs=out_specs, check_vma=False
    )
```

```python
import math

import jax
import jax.numpy as jnp
from jax import lax
from jax.sharding import Mesh
from jax.sharding import PartitionSpec as P

BLK = 256
HEAD_AXES = ("hx", "hy", "hc")
CTX_AXES = ("ca", "cb")


def _flat(x, y, c, ny, nc):
    return (x * ny + y) * nc + c


def _ring_perm(stage, d, nx, ny, nc):
    pairs = []
    for x in range(nx):
        for y in range(ny):
            for c in range(nc):
                along_y = (c == 0) == (stage == 0)
                if along_y:
                    tx, ty = x, (y + d) % ny
                else:
                    tx, ty = (x + d) % nx, y
                pairs.append((_flat(x, y, c, ny, nc), _flat(tx, ty, c, ny, nc)))
    return pairs


def _core_perm(nx, ny, nc):
    pairs = []
    for x in range(nx):
        for y in range(ny):
            for c in range(nc):
                pairs.append((_flat(x, y, c, ny, nc), _flat(x, y, 1 - c, ny, nc)))
    return pairs


def _send(value, perm):
    return lax.ppermute(value, HEAD_AXES, perm)


def gather_ring(blk, stage, sizes):
    p1 = _send(blk, _ring_perm(stage, 1, *sizes))
    m1 = _send(blk, _ring_perm(stage, -1, *sizes))
    h = blk.shape[0] // 2
    a = _send(p1[:h], _ring_perm(stage, 1, *sizes))
    b = _send(m1[h:], _ring_perm(stage, -1, *sizes))
    far = jnp.concatenate([a, b], axis=0)
    return jnp.stack([blk, p1, far, m1])


def reduce_ring(data, stage, sizes):
    h = data.shape[1] // 2
    rp = _send(data[2, :h].astype(jnp.bfloat16), _ring_perm(stage, 1, *sizes))
    rm = _send(data[2, h:].astype(jnp.bfloat16), _ring_perm(stage, -1, *sizes))
    ahead = jnp.concatenate([data[1, :h] + rp, data[1, h:]], axis=0)
    behind = jnp.concatenate([data[3, :h], data[3, h:] + rm], axis=0)
    gp = _send(ahead.astype(jnp.bfloat16), _ring_perm(stage, 1, *sizes))
    gm = _send(behind.astype(jnp.bfloat16), _ring_perm(stage, -1, *sizes))
    return data[0] + gp.astype(jnp.float32) + gm.astype(jnp.float32)


def attend_exact(queries, keys_win, vals_win, book, reach_one, prev_flag, block_len, scale):
    exact = (
        lax.dot_general(
            queries, keys_win, (((1,), (1,)), ((), ())), preferred_element_type=jnp.float32
        )
        * scale
    )
    coded = (
        lax.dot_general(queries, book, (((1,), (1,)), ((), ())), preferred_element_type=jnp.float32)
        * scale
    )
    rows = lax.broadcasted_iota(jnp.int32, exact.shape, 0)
    cols = lax.broadcasted_iota(jnp.int32, exact.shape, 1)
    prev_ok = (cols < block_len) & (cols >= block_len - reach_one) & prev_flag
    curr_ok = (cols >= block_len) & (cols - block_len <= rows)
    allowed = prev_ok | curr_ok
    top_e = jnp.max(jnp.where(allowed, exact, -jnp.inf), axis=1)
    probs = jnp.exp(jnp.where(allowed, exact - top_e[:, None], -jnp.inf))
    numer = jnp.dot(probs.astype(jnp.bfloat16), vals_win, preferred_element_type=jnp.float32)
    denom = jnp.sum(probs, axis=1)
    return top_e, numer, denom, coded


def attend_cache(top_e, numer_e, denom_e, coded, cache_v, cache_c):
    valid = cache_c > 0.5
    top = jnp.maximum(top_e, jnp.max(jnp.where(valid[None, :], coded, -jnp.inf), axis=1))
    alpha = jnp.exp(top_e - top)
    weights = jnp.exp(jnp.where(valid[None, :], coded - top[:, None], -jnp.inf))
    numer = alpha[:, None] * numer_e + jnp.dot(weights, cache_v, precision=lax.Precision.HIGHEST)
    denom = alpha * denom_e + jnp.dot(weights, cache_c, precision=lax.Precision.HIGHEST)
    return (numer / denom[:, None]).astype(jnp.bfloat16)


def on_device(tokens_in, w_qkv, w_out, codebook, codes, reach):
    nx, ny, nc = lax.axis_size("hx"), lax.axis_size("hy"), lax.axis_size("hc")
    sizes = (nx, ny, nc)
    core_perm = _core_perm(*sizes)
    me_x, me_y, me_c = lax.axis_index("hx"), lax.axis_index("hy"), lax.axis_index("hc")
    na, nb = lax.axis_size("ca"), lax.axis_size("cb")
    n_ctx = na * nb
    g = lax.axis_index("ca") * nb + lax.axis_index("cb")
    rows, width = tokens_in.shape
    head_dim = codebook.shape[2]
    num_codes = codebook.shape[1]
    scale = 1.0 / math.sqrt(head_dim)
    half = rows // 2

    projected = project(tokens_in, w_qkv, sizes)
    queries = projected[:, :head_dim].astype(jnp.bfloat16)
    key_vals = projected[:, head_dim:].astype(jnp.bfloat16)
    values = key_vals[:, head_dim:]

    code_row = codes[0]
    code_ids = jnp.arange(num_codes, dtype=jnp.int32)
    hi = (code_row // 16).astype(jnp.bfloat16).reshape(1, -1)
    lo = (code_row % 16).astype(jnp.bfloat16).reshape(1, -1)
    kvw = key_vals.shape[1]
    code_rows = jnp.pad(jnp.concatenate([hi, lo], axis=0), ((0, 0), (0, kvw - rows)))
    kv_blob = jnp.concatenate([key_vals, code_rows, jnp.zeros((14, kvw), jnp.bfloat16)], axis=0)
    route = [(i, i + 1) for i in range(n_ctx - 1)]
    prev_blob = lax.ppermute(kv_blob, CTX_AXES, route)
    prev_kv = prev_blob[:rows]
    prev_codes = (
        prev_blob[rows, :rows].astype(jnp.int32) * 16 + prev_blob[rows + 1, :rows].astype(jnp.int32)
    )

    onehot_own = (code_row[:, None] == code_ids[None, :]).astype(jnp.bfloat16)
    sums = lax.dot_general(
        onehot_own, values, (((0,), (0,)), ((), ())), preferred_element_type=jnp.float32
    )
    counts = jnp.sum(onehot_own.astype(jnp.float32), axis=0)
    span = num_codes // n_ctx
    cache_v, cache_c = code_prefix(sums, counts, span, na, nb, head_dim)
    prev_ok = (jnp.arange(rows, dtype=jnp.int32) < BLK - reach[0]) & (g > 0)
    onehot_prev = (
        (prev_codes[:, None] == code_ids[None, :]) & prev_ok[:, None]
    ).astype(jnp.bfloat16)
    cache_v = cache_v + lax.dot_general(
        onehot_prev, prev_kv[:, head_dim:], (((0,), (0,)), ((), ())),
        preferred_element_type=jnp.float32,
    )
    cache_c = cache_c + jnp.sum(onehot_prev.astype(jnp.float32), axis=0)

    ext_kv = jnp.concatenate([prev_kv, key_vals], axis=0)
    top_e, numer_e, denom_e, coded = attend_exact(
        queries,
        ext_kv[:, :head_dim],
        ext_kv[:, head_dim:],
        codebook[0],
        reach[0],
        g > 0,
        BLK,
        scale,
    )
    attended = attend_cache(top_e, numer_e, denom_e, coded, cache_v, cache_c)

    return reduce_out(attended, w_out, sizes)


def _pack(sums, counts, span, n, head_dim):
    hi = jnp.floor(counts / 64.0)
    lo = counts - hi * 64.0
    tail = jnp.zeros((n, 8, head_dim), jnp.float32)
    tail = tail.at[:, 0, :span].set(hi.reshape(n, span)).at[:, 1, :span].set(lo.reshape(n, span))
    return jnp.concatenate([sums.reshape(n, span, head_dim), tail], axis=1).astype(jnp.bfloat16)


def _unpack(blob, span):
    blob = blob.astype(jnp.float32)
    sums = blob[:, :span]
    counts = blob[:, span, :span] * 64.0 + blob[:, span + 1, :span]
    return sums, counts


def code_prefix(sums, counts, span, na, nb, head_dim):
    n = na * nb
    blob = _pack(sums, counts, span, n, head_dim)
    blob = blob.reshape(na, nb, -1, head_dim).transpose(1, 0, 2, 3)
    step = lax.all_to_all(blob, "cb", 0, 0, tiled=True).transpose(1, 0, 2, 3)
    got = lax.all_to_all(step, "ca", 0, 0, tiled=True).reshape(n, -1, head_dim)
    block_sums, block_counts = _unpack(got, span)
    b = jnp.arange(n, dtype=jnp.int32)
    before = (b[None, :] <= b[:, None] - 2).astype(jnp.bfloat16)
    pre_sums = jnp.einsum(
        "bc,cxd->bxd", before, block_sums.astype(jnp.bfloat16), preferred_element_type=jnp.float32
    )
    pre_counts = jnp.dot(
        before, block_counts.astype(jnp.bfloat16), preferred_element_type=jnp.float32
    )
    back = _pack(pre_sums, pre_counts, span, n, head_dim).reshape(na, nb, -1, head_dim)
    step = lax.all_to_all(back, "ca", 0, 0, tiled=True).transpose(1, 0, 2, 3)
    back = lax.all_to_all(step, "cb", 0, 0, tiled=True).transpose(1, 0, 2, 3)
    cache_v, cache_c = _unpack(back.reshape(n, -1, head_dim), span)
    return cache_v.reshape(n * span, head_dim), cache_c.reshape(n * span)

def project(tokens_in, w_qkv, sizes):
    nx, ny, nc = sizes
    n_head = nx * ny * nc
    core_perm = _core_perm(*sizes)
    me_c = lax.axis_index("hc")
    rows, width = tokens_in.shape
    half = rows // nc
    spread = jnp.broadcast_to(
        tokens_in.reshape(1, nc, half, width), (n_head // nc, nc, half, width)
    ).reshape(n_head, half, width)
    mine = lax.all_to_all(spread, HEAD_AXES, 0, 0, tiled=True)
    theirs = _send(mine, core_perm)
    w_local = w_qkv[:, 0, :].reshape(n_head, width, -1)
    dims = (((0, 2), (0, 1)), ((), ()))
    proj_own = lax.dot_general(mine, w_local, dims, preferred_element_type=jnp.float32)
    proj_oth = lax.dot_general(theirs, w_local, dims, preferred_element_type=jnp.float32)
    projected = jnp.where(
        me_c == 0,
        jnp.concatenate([proj_own, proj_oth], axis=0),
        jnp.concatenate([proj_oth, proj_own], axis=0),
    )
    return projected


def reduce_out(attended, w_out, sizes):
    nx, ny, nc = sizes
    core_perm = _core_perm(*sizes)
    me_c = lax.axis_index("hc")
    rows = attended.shape[0]
    w_full = w_out[0]
    cols = w_full.shape[1] // nc
    w_keep = lax.dynamic_slice_in_dim(w_full, me_c * cols, cols, 1)
    w_give = lax.dynamic_slice_in_dim(w_full, (1 - me_c) * cols, cols, 1)
    keep = jnp.dot(attended, w_keep, preferred_element_type=jnp.float32)
    give = jnp.dot(attended, w_give, preferred_element_type=jnp.float32).astype(jnp.bfloat16)
    got = _send(give, core_perm)
    summed = (keep + got.astype(jnp.float32)).astype(jnp.bfloat16)
    n_head = nx * ny * nc
    chunks = summed.reshape(n_head, rows // n_head, cols)
    parts = lax.all_to_all(chunks, HEAD_AXES, 0, 0, tiled=True).astype(jnp.float32)
    parts = parts.reshape(n_head // nc, nc, rows // n_head, cols).sum(axis=0)
    out = jnp.concatenate([parts[i] for i in range(nc)], axis=1)
    return out.astype(jnp.bfloat16)


def solution(mesh):
    n_ctx, n_head = mesh.devices.shape
    devices = mesh.devices.reshape(4, n_ctx // 4, 4, 4, n_head // 16)
    grid = Mesh(devices, CTX_AXES + HEAD_AXES)
    in_specs = (
        P(CTX_AXES, HEAD_AXES),
        P(None, HEAD_AXES, None),
        P(HEAD_AXES, None, None),
        P(HEAD_AXES, None, None),
        P(HEAD_AXES, CTX_AXES),
        P(CTX_AXES),
    )
    out_specs = P(CTX_AXES + HEAD_AXES, None)
    return jax.shard_map(
        on_device, mesh=grid, in_specs=in_specs, out_specs=out_specs, check_vma=False
    )
```

```python
import math

import jax
import jax.numpy as jnp
from jax import lax
from jax.sharding import Mesh
from jax.sharding import PartitionSpec as P

BLK = 256
HEAD_AXES = ("hx", "hy", "hc")


def _flat(x, y, c, ny, nc):
    return (x * ny + y) * nc + c


def _ring_perm(stage, d, nx, ny, nc):
    pairs = []
    for x in range(nx):
        for y in range(ny):
            for c in range(nc):
                along_y = (c == 0) == (stage == 0)
                if along_y:
                    tx, ty = x, (y + d) % ny
                else:
                    tx, ty = (x + d) % nx, y
                pairs.append((_flat(x, y, c, ny, nc), _flat(tx, ty, c, ny, nc)))
    return pairs


def _core_perm(nx, ny, nc):
    pairs = []
    for x in range(nx):
        for y in range(ny):
            for c in range(nc):
                pairs.append((_flat(x, y, c, ny, nc), _flat(x, y, 1 - c, ny, nc)))
    return pairs


def _send(value, perm):
    return lax.ppermute(value, HEAD_AXES, perm)


def gather_ring(blk, stage, sizes):
    p1 = _send(blk, _ring_perm(stage, 1, *sizes))
    m1 = _send(blk, _ring_perm(stage, -1, *sizes))
    h = blk.shape[0] // 2
    a = _send(p1[:h], _ring_perm(stage, 1, *sizes))
    b = _send(m1[h:], _ring_perm(stage, -1, *sizes))
    far = jnp.concatenate([a, b], axis=0)
    return jnp.stack([blk, p1, far, m1])


def reduce_ring(data, stage, sizes):
    h = data.shape[1] // 2
    rp = _send(data[2, :h].astype(jnp.bfloat16), _ring_perm(stage, 1, *sizes))
    rm = _send(data[2, h:].astype(jnp.bfloat16), _ring_perm(stage, -1, *sizes))
    ahead = jnp.concatenate([data[1, :h] + rp, data[1, h:]], axis=0)
    behind = jnp.concatenate([data[3, :h], data[3, h:] + rm], axis=0)
    gp = _send(ahead.astype(jnp.bfloat16), _ring_perm(stage, 1, *sizes))
    gm = _send(behind.astype(jnp.bfloat16), _ring_perm(stage, -1, *sizes))
    return data[0] + gp.astype(jnp.float32) + gm.astype(jnp.float32)


def attend_exact(queries, keys_win, vals_win, book, reach_one, prev_flag, block_len, scale):
    exact = (
        lax.dot_general(
            queries, keys_win, (((1,), (1,)), ((), ())), preferred_element_type=jnp.float32
        )
        * scale
    )
    coded = (
        lax.dot_general(queries, book, (((1,), (1,)), ((), ())), preferred_element_type=jnp.float32)
        * scale
    )
    rows = lax.broadcasted_iota(jnp.int32, exact.shape, 0)
    cols = lax.broadcasted_iota(jnp.int32, exact.shape, 1)
    prev_ok = (cols < block_len) & (cols >= block_len - reach_one) & prev_flag
    curr_ok = (cols >= block_len) & (cols - block_len <= rows)
    allowed = prev_ok | curr_ok
    top_e = jnp.max(jnp.where(allowed, exact, -jnp.inf), axis=1)
    probs = jnp.exp(jnp.where(allowed, exact - top_e[:, None], -jnp.inf))
    numer = jnp.dot(probs.astype(jnp.bfloat16), vals_win, preferred_element_type=jnp.float32)
    denom = jnp.sum(probs, axis=1)
    return top_e, numer, denom, coded


def attend_cache(top_e, numer_e, denom_e, coded, cache_v, cache_c):
    valid = cache_c > 0.5
    top = jnp.maximum(top_e, jnp.max(jnp.where(valid[None, :], coded, -jnp.inf), axis=1))
    alpha = jnp.exp(top_e - top)
    weights = jnp.exp(jnp.where(valid[None, :], coded - top[:, None], -jnp.inf))
    numer = alpha[:, None] * numer_e + jnp.dot(weights, cache_v, precision=lax.Precision.HIGHEST)
    denom = alpha * denom_e + jnp.dot(weights, cache_c, precision=lax.Precision.HIGHEST)
    return (numer / denom[:, None]).astype(jnp.bfloat16)


def on_device(tokens_in, w_qkv, w_out, codebook, codes, reach):
    nx, ny, nc = lax.axis_size("hx"), lax.axis_size("hy"), lax.axis_size("hc")
    sizes = (nx, ny, nc)
    core_perm = _core_perm(*sizes)
    me_x, me_y, me_c = lax.axis_index("hx"), lax.axis_index("hy"), lax.axis_index("hc")
    n_ctx = lax.axis_size("ctx")
    g = lax.axis_index("ctx")
    rows, width = tokens_in.shape
    head_dim = codebook.shape[2]
    num_codes = codebook.shape[1]
    scale = 1.0 / math.sqrt(head_dim)
    half = rows // 2

    code_row = codes[0]
    code_ids = jnp.arange(num_codes, dtype=jnp.int32)
    codes_all = lax.all_to_all(
        jnp.broadcast_to(code_row[None], (n_ctx, rows)), "ctx", 0, 0, tiled=True
    )
    limit = g * BLK - reach[0]
    cached = jnp.arange(n_ctx * rows, dtype=jnp.int32).reshape(n_ctx, rows) < limit
    cache_c = jnp.sum(
        ((codes_all[:, :, None] == code_ids[None, None, :]) & cached[:, :, None]).astype(
            jnp.float32
        ),
        axis=(0, 1),
    )

    projected = project(tokens_in, w_qkv, sizes)
    queries = projected[:, :head_dim].astype(jnp.bfloat16)
    key_vals = projected[:, head_dim:].astype(jnp.bfloat16)
    values = key_vals[:, head_dim:]

    route = [(i, i + 1) for i in range(n_ctx - 1)]
    prev_kv = lax.ppermute(key_vals, "ctx", route)
    prev_codes = lax.dynamic_index_in_dim(codes_all, jnp.maximum(g - 1, 0), 0, keepdims=False)

    onehot_own = (code_row[:, None] == code_ids[None, :]).astype(jnp.bfloat16)
    sums = lax.dot_general(
        onehot_own, values, (((0,), (0,)), ((), ())), preferred_element_type=jnp.float32
    )
    span = num_codes // n_ctx
    cache_v = code_prefix(sums, span, n_ctx, head_dim)
    prev_ok = (jnp.arange(rows, dtype=jnp.int32) < BLK - reach[0]) & (g > 0)
    onehot_prev = (
        (prev_codes[:, None] == code_ids[None, :]) & prev_ok[:, None]
    ).astype(jnp.bfloat16)
    cache_v = cache_v + lax.dot_general(
        onehot_prev, prev_kv[:, head_dim:], (((0,), (0,)), ((), ())),
        preferred_element_type=jnp.float32,
    )

    ext_kv = jnp.concatenate([prev_kv, key_vals], axis=0)
    top_e, numer_e, denom_e, coded = attend_exact(
        queries,
        ext_kv[:, :head_dim],
        ext_kv[:, head_dim:],
        codebook[0],
        reach[0],
        g > 0,
        BLK,
        scale,
    )
    attended = attend_cache(top_e, numer_e, denom_e, coded, cache_v, cache_c)

    return reduce_out(attended, w_out, sizes)


def code_prefix(sums, span, n, head_dim):
    blob = sums.reshape(n, span, head_dim).astype(jnp.bfloat16)
    got = lax.all_to_all(blob, "ctx", 0, 0, tiled=True)
    b = jnp.arange(n, dtype=jnp.int32)
    before = (b[None, :] <= b[:, None] - 2).astype(jnp.bfloat16)
    pre_sums = jnp.einsum("bc,cxd->bxd", before, got, preferred_element_type=jnp.float32)
    back = lax.all_to_all(pre_sums.astype(jnp.bfloat16), "ctx", 0, 0, tiled=True)
    return back.astype(jnp.float32).reshape(n * span, head_dim)

def project(tokens_in, w_qkv, sizes):
    nx, ny, nc = sizes
    n_head = nx * ny * nc
    core_perm = _core_perm(*sizes)
    me_c = lax.axis_index("hc")
    rows, width = tokens_in.shape
    half = rows // nc
    spread = jnp.broadcast_to(
        tokens_in.reshape(1, nc, half, width), (n_head // nc, nc, half, width)
    ).reshape(n_head, half, width)
    mine = lax.all_to_all(spread, HEAD_AXES, 0, 0, tiled=True)
    theirs = _send(mine, core_perm)
    w_local = w_qkv[:, 0, :].reshape(n_head, width, -1)
    dims = (((0, 2), (0, 1)), ((), ()))
    proj_own = lax.dot_general(mine, w_local, dims, preferred_element_type=jnp.float32)
    proj_oth = lax.dot_general(theirs, w_local, dims, preferred_element_type=jnp.float32)
    projected = jnp.where(
        me_c == 0,
        jnp.concatenate([proj_own, proj_oth], axis=0),
        jnp.concatenate([proj_oth, proj_own], axis=0),
    )
    return projected


def reduce_out(attended, w_out, sizes):
    nx, ny, nc = sizes
    core_perm = _core_perm(*sizes)
    me_c = lax.axis_index("hc")
    rows = attended.shape[0]
    w_full = w_out[0]
    cols = w_full.shape[1] // nc
    w_keep = lax.dynamic_slice_in_dim(w_full, me_c * cols, cols, 1)
    w_give = lax.dynamic_slice_in_dim(w_full, (1 - me_c) * cols, cols, 1)
    keep = jnp.dot(attended, w_keep, preferred_element_type=jnp.float32)
    give = jnp.dot(attended, w_give, preferred_element_type=jnp.float32).astype(jnp.bfloat16)
    got = _send(give, core_perm)
    summed = (keep + got.astype(jnp.float32)).astype(jnp.bfloat16)
    n_head = nx * ny * nc
    chunks = summed.reshape(n_head, rows // n_head, cols)
    parts = lax.all_to_all(chunks, HEAD_AXES, 0, 0, tiled=True).astype(jnp.float32)
    parts = parts.reshape(n_head // nc, nc, rows // n_head, cols).sum(axis=0)
    out = jnp.concatenate([parts[i] for i in range(nc)], axis=1)
    return out.astype(jnp.bfloat16)


def solution(mesh):
    n_ctx, n_head = mesh.devices.shape
    devices = mesh.devices.reshape(n_ctx, 4, 4, n_head // 16)
    grid = Mesh(devices, ("ctx",) + HEAD_AXES)
    in_specs = (
        P("ctx", HEAD_AXES),
        P(None, HEAD_AXES, None),
        P(HEAD_AXES, None, None),
        P(HEAD_AXES, None, None),
        P(HEAD_AXES, "ctx"),
        P("ctx"),
    )
    out_specs = P(("ctx",) + HEAD_AXES, None)
    return jax.shard_map(
        on_device, mesh=grid, in_specs=in_specs, out_specs=out_specs, check_vma=False
    )
```

```python
import math

import jax
import jax.numpy as jnp
from jax import lax
from jax.sharding import Mesh
from jax.sharding import PartitionSpec as P

BLK = 256
HEAD_AXES = ("hx", "hy", "hc")


def _flat(x, y, c, ny, nc):
    return (x * ny + y) * nc + c


def _ring_perm(stage, d, nx, ny, nc):
    pairs = []
    for x in range(nx):
        for y in range(ny):
            for c in range(nc):
                along_y = (c == 0) == (stage == 0)
                if along_y:
                    tx, ty = x, (y + d) % ny
                else:
                    tx, ty = (x + d) % nx, y
                pairs.append((_flat(x, y, c, ny, nc), _flat(tx, ty, c, ny, nc)))
    return pairs


def _core_perm(nx, ny, nc):
    pairs = []
    for x in range(nx):
        for y in range(ny):
            for c in range(nc):
                pairs.append((_flat(x, y, c, ny, nc), _flat(x, y, 1 - c, ny, nc)))
    return pairs


def _send(value, perm):
    return lax.ppermute(value, HEAD_AXES, perm)


def gather_ring(blk, stage, sizes):
    p1 = _send(blk, _ring_perm(stage, 1, *sizes))
    m1 = _send(blk, _ring_perm(stage, -1, *sizes))
    h = blk.shape[0] // 2
    a = _send(p1[:h], _ring_perm(stage, 1, *sizes))
    b = _send(m1[h:], _ring_perm(stage, -1, *sizes))
    far = jnp.concatenate([a, b], axis=0)
    return jnp.stack([blk, p1, far, m1])


def reduce_ring(data, stage, sizes):
    h = data.shape[1] // 2
    rp = _send(data[2, :h].astype(jnp.bfloat16), _ring_perm(stage, 1, *sizes))
    rm = _send(data[2, h:].astype(jnp.bfloat16), _ring_perm(stage, -1, *sizes))
    ahead = jnp.concatenate([data[1, :h] + rp, data[1, h:]], axis=0)
    behind = jnp.concatenate([data[3, :h], data[3, h:] + rm], axis=0)
    gp = _send(ahead.astype(jnp.bfloat16), _ring_perm(stage, 1, *sizes))
    gm = _send(behind.astype(jnp.bfloat16), _ring_perm(stage, -1, *sizes))
    return data[0] + gp.astype(jnp.float32) + gm.astype(jnp.float32)


def attend_exact(queries, keys_win, vals_win, book, reach_one, prev_flag, block_len, scale):
    exact = (
        lax.dot_general(
            queries, keys_win, (((1,), (1,)), ((), ())), preferred_element_type=jnp.float32
        )
        * scale
    )
    coded = (
        lax.dot_general(queries, book, (((1,), (1,)), ((), ())), preferred_element_type=jnp.float32)
        * scale
    )
    rows = lax.broadcasted_iota(jnp.int32, exact.shape, 0)
    cols = lax.broadcasted_iota(jnp.int32, exact.shape, 1)
    prev_ok = (cols < block_len) & (cols >= block_len - reach_one) & prev_flag
    curr_ok = (cols >= block_len) & (cols - block_len <= rows)
    allowed = prev_ok | curr_ok
    top_e = jnp.max(jnp.where(allowed, exact, -jnp.inf), axis=1)
    probs = jnp.exp(jnp.where(allowed, exact - top_e[:, None], -jnp.inf))
    numer = jnp.dot(probs.astype(jnp.bfloat16), vals_win, preferred_element_type=jnp.float32)
    denom = jnp.sum(probs, axis=1)
    return top_e, numer, denom, coded


def attend_cache(top_e, numer_e, denom_e, coded, cache_v, cache_c):
    valid = cache_c > 0.5
    top = jnp.maximum(top_e, jnp.max(jnp.where(valid[None, :], coded, -jnp.inf), axis=1))
    alpha = jnp.exp(top_e - top)
    weights = jnp.exp(jnp.where(valid[None, :], coded - top[:, None], -jnp.inf))
    numer = alpha[:, None] * numer_e + jnp.dot(weights, cache_v, precision=lax.Precision.HIGHEST)
    denom = alpha * denom_e + jnp.dot(weights, cache_c, precision=lax.Precision.HIGHEST)
    return (numer / denom[:, None]).astype(jnp.bfloat16)


def on_device(tokens_in, w_qkv, w_out, codebook, codes, reach):
    nx, ny, nc = lax.axis_size("hx"), lax.axis_size("hy"), lax.axis_size("hc")
    sizes = (nx, ny, nc)
    core_perm = _core_perm(*sizes)
    me_x, me_y, me_c = lax.axis_index("hx"), lax.axis_index("hy"), lax.axis_index("hc")
    n_ctx = lax.axis_size("ctx")
    g = lax.axis_index("ctx")
    rows, width = tokens_in.shape
    head_dim = codebook.shape[2]
    num_codes = codebook.shape[1]
    scale = 1.0 / math.sqrt(head_dim)
    half = rows // 2

    projected = project(tokens_in, w_qkv, sizes)
    queries = projected[:, :head_dim].astype(jnp.bfloat16)
    key_vals = projected[:, head_dim:].astype(jnp.bfloat16)
    values = key_vals[:, head_dim:]

    code_row = codes[0]
    code_ids = jnp.arange(num_codes, dtype=jnp.int32)
    hi = (code_row // 16).astype(jnp.bfloat16).reshape(1, -1)
    lo = (code_row % 16).astype(jnp.bfloat16).reshape(1, -1)
    kvw = key_vals.shape[1]
    code_rows = jnp.pad(jnp.concatenate([hi, lo], axis=0), ((0, 0), (0, kvw - rows)))
    kv_blob = jnp.concatenate([key_vals, code_rows, jnp.zeros((14, kvw), jnp.bfloat16)], axis=0)
    route = [(i, i + 1) for i in range(n_ctx - 1)]
    prev_blob = lax.ppermute(kv_blob, "ctx", route)
    prev_kv = prev_blob[:rows]
    prev_codes = (
        prev_blob[rows, :rows].astype(jnp.int32) * 16 + prev_blob[rows + 1, :rows].astype(jnp.int32)
    )

    onehot_own = (code_row[:, None] == code_ids[None, :]).astype(jnp.bfloat16)
    sums = lax.dot_general(
        onehot_own, values, (((0,), (0,)), ((), ())), preferred_element_type=jnp.float32
    )
    counts = jnp.sum(onehot_own.astype(jnp.float32), axis=0)
    span = num_codes // n_ctx
    cache_v, cache_c = code_prefix(sums, counts, span, n_ctx, head_dim)
    prev_ok = (jnp.arange(rows, dtype=jnp.int32) < BLK - reach[0]) & (g > 0)
    onehot_prev = (
        (prev_codes[:, None] == code_ids[None, :]) & prev_ok[:, None]
    ).astype(jnp.bfloat16)
    cache_v = cache_v + lax.dot_general(
        onehot_prev, prev_kv[:, head_dim:], (((0,), (0,)), ((), ())),
        preferred_element_type=jnp.float32,
    )
    cache_c = cache_c + jnp.sum(onehot_prev.astype(jnp.float32), axis=0)

    ext_kv = jnp.concatenate([prev_kv, key_vals], axis=0)
    top_e, numer_e, denom_e, coded = attend_exact(
        queries,
        ext_kv[:, :head_dim],
        ext_kv[:, head_dim:],
        codebook[0],
        reach[0],
        g > 0,
        BLK,
        scale,
    )
    attended = attend_cache(top_e, numer_e, denom_e, coded, cache_v, cache_c)

    return reduce_out(attended, w_out, sizes)


def _pack(sums, counts, span, n, head_dim):
    hi = jnp.floor(counts / 64.0)
    lo = counts - hi * 64.0
    tail = jnp.zeros((n, 8, head_dim), jnp.float32)
    tail = tail.at[:, 0, :span].set(hi.reshape(n, span)).at[:, 1, :span].set(lo.reshape(n, span))
    return jnp.concatenate([sums.reshape(n, span, head_dim), tail], axis=1).astype(jnp.bfloat16)


def _unpack(blob, span):
    blob = blob.astype(jnp.float32)
    sums = blob[:, :span]
    counts = blob[:, span, :span] * 64.0 + blob[:, span + 1, :span]
    return sums, counts


def code_prefix(sums, counts, span, n, head_dim):
    got = lax.all_to_all(_pack(sums, counts, span, n, head_dim), "ctx", 0, 0, tiled=True)
    b = jnp.arange(n, dtype=jnp.int32)
    before = (b[None, :] <= b[:, None] - 2).astype(jnp.bfloat16)
    pre = jnp.einsum("bc,cxd->bxd", before, got, preferred_element_type=jnp.float32)
    total = pre[:, span] * 64.0 + pre[:, span + 1]
    hi = jnp.floor(total / 64.0)
    lo = total - hi * 64.0
    rows = lax.broadcasted_iota(jnp.int32, pre.shape, 1)
    pre = jnp.where(rows == span, hi[:, None, :], jnp.where(rows == span + 1, lo[:, None, :], pre))
    back = lax.all_to_all(pre.astype(jnp.bfloat16), "ctx", 0, 0, tiled=True)
    cache_v, cache_c = _unpack(back, span)
    return cache_v.reshape(n * span, head_dim), cache_c.reshape(n * span)

def project(tokens_in, w_qkv, sizes):
    nx, ny, nc = sizes
    n_head = nx * ny * nc
    core_perm = _core_perm(*sizes)
    me_c = lax.axis_index("hc")
    rows, width = tokens_in.shape
    half = rows // nc
    spread = jnp.broadcast_to(
        tokens_in.reshape(nc, half, width).transpose(1, 0, 2)[:, None],
        (half, n_head // nc, nc, width),
    ).reshape(half, n_head, width)
    mine = lax.all_to_all(spread, HEAD_AXES, 1, 1, tiled=True).reshape(half, n_head * width)
    theirs = _send(mine, core_perm)
    w_local = w_qkv[:, 0, :]
    proj_own = jnp.dot(mine, w_local, preferred_element_type=jnp.float32)
    proj_oth = jnp.dot(theirs, w_local, preferred_element_type=jnp.float32)
    projected = jnp.where(
        me_c == 0,
        jnp.concatenate([proj_own, proj_oth], axis=0),
        jnp.concatenate([proj_oth, proj_own], axis=0),
    )
    return projected


def reduce_out(attended, w_out, sizes):
    nx, ny, nc = sizes
    core_perm = _core_perm(*sizes)
    me_c = lax.axis_index("hc")
    rows = attended.shape[0]
    w_full = w_out[0]
    cols = w_full.shape[1] // nc
    w_keep = lax.dynamic_slice_in_dim(w_full, me_c * cols, cols, 1)
    w_give = lax.dynamic_slice_in_dim(w_full, (1 - me_c) * cols, cols, 1)
    keep = jnp.dot(attended, w_keep, preferred_element_type=jnp.float32)
    give = jnp.dot(attended, w_give, preferred_element_type=jnp.float32).astype(jnp.bfloat16)
    got = _send(give, core_perm)
    summed = (keep + got.astype(jnp.float32)).astype(jnp.bfloat16)
    n_head = nx * ny * nc
    chunks = summed.reshape(n_head, rows // n_head, cols)
    parts = lax.all_to_all(chunks, HEAD_AXES, 0, 0, tiled=True).astype(jnp.float32)
    parts = parts.reshape(n_head // nc, nc, rows // n_head, cols).sum(axis=0)
    out = jnp.concatenate([parts[i] for i in range(nc)], axis=1)
    return out.astype(jnp.bfloat16)


def solution(mesh):
    n_ctx, n_head = mesh.devices.shape
    devices = mesh.devices.reshape(n_ctx, 4, 4, n_head // 16)
    grid = Mesh(devices, ("ctx",) + HEAD_AXES)
    in_specs = (
        P("ctx", HEAD_AXES),
        P(None, HEAD_AXES, None),
        P(HEAD_AXES, None, None),
        P(HEAD_AXES, None, None),
        P(HEAD_AXES, "ctx"),
        P("ctx"),
    )
    out_specs = P(("ctx",) + HEAD_AXES, None)
    return jax.shard_map(
        on_device, mesh=grid, in_specs=in_specs, out_specs=out_specs, check_vma=False
    )
```

```python
import math

import jax
import jax.numpy as jnp
from jax import lax
from jax.sharding import Mesh
from jax.sharding import PartitionSpec as P

BLK = 256
HEAD_AXES = ("hx", "hy", "hc")


def _flat(x, y, c, ny, nc):
    return (x * ny + y) * nc + c


def _ring_perm(stage, d, nx, ny, nc):
    pairs = []
    for x in range(nx):
        for y in range(ny):
            for c in range(nc):
                along_y = (c == 0) == (stage == 0)
                if along_y:
                    tx, ty = x, (y + d) % ny
                else:
                    tx, ty = (x + d) % nx, y
                pairs.append((_flat(x, y, c, ny, nc), _flat(tx, ty, c, ny, nc)))
    return pairs


def _core_perm(nx, ny, nc):
    pairs = []
    for x in range(nx):
        for y in range(ny):
            for c in range(nc):
                pairs.append((_flat(x, y, c, ny, nc), _flat(x, y, 1 - c, ny, nc)))
    return pairs


def _send(value, perm):
    return lax.ppermute(value, HEAD_AXES, perm)


def gather_ring(blk, stage, sizes):
    p1 = _send(blk, _ring_perm(stage, 1, *sizes))
    m1 = _send(blk, _ring_perm(stage, -1, *sizes))
    h = blk.shape[0] // 2
    a = _send(p1[:h], _ring_perm(stage, 1, *sizes))
    b = _send(m1[h:], _ring_perm(stage, -1, *sizes))
    far = jnp.concatenate([a, b], axis=0)
    return jnp.stack([blk, p1, far, m1])


def reduce_ring(data, stage, sizes):
    h = data.shape[1] // 2
    rp = _send(data[2, :h].astype(jnp.bfloat16), _ring_perm(stage, 1, *sizes))
    rm = _send(data[2, h:].astype(jnp.bfloat16), _ring_perm(stage, -1, *sizes))
    ahead = jnp.concatenate([data[1, :h] + rp, data[1, h:]], axis=0)
    behind = jnp.concatenate([data[3, :h], data[3, h:] + rm], axis=0)
    gp = _send(ahead.astype(jnp.bfloat16), _ring_perm(stage, 1, *sizes))
    gm = _send(behind.astype(jnp.bfloat16), _ring_perm(stage, -1, *sizes))
    return data[0] + gp.astype(jnp.float32) + gm.astype(jnp.float32)


def attend_exact(queries, keys_win, vals_win, book, reach_one, prev_flag, block_len, scale):
    exact = (
        lax.dot_general(
            queries, keys_win, (((1,), (1,)), ((), ())), preferred_element_type=jnp.float32
        )
        * scale
    )
    coded = (
        lax.dot_general(queries, book, (((1,), (1,)), ((), ())), preferred_element_type=jnp.float32)
        * scale
    )
    rows = lax.broadcasted_iota(jnp.int32, exact.shape, 0)
    cols = lax.broadcasted_iota(jnp.int32, exact.shape, 1)
    prev_ok = (cols < block_len) & (cols >= block_len - reach_one) & prev_flag
    curr_ok = (cols >= block_len) & (cols - block_len <= rows)
    allowed = prev_ok | curr_ok
    top_e = jnp.max(jnp.where(allowed, exact, -jnp.inf), axis=1)
    probs = jnp.exp(jnp.where(allowed, exact - top_e[:, None], -jnp.inf))
    numer = jnp.dot(probs.astype(jnp.bfloat16), vals_win, preferred_element_type=jnp.float32)
    denom = jnp.sum(probs, axis=1)
    return top_e, numer, denom, coded


def attend_cache(top_e, numer_e, denom_e, coded, cache_v, cache_c):
    valid = cache_c > 0.5
    top = jnp.maximum(top_e, jnp.max(jnp.where(valid[None, :], coded, -jnp.inf), axis=1))
    alpha = jnp.exp(top_e - top)
    weights = jnp.exp(jnp.where(valid[None, :], coded - top[:, None], -jnp.inf))
    numer = alpha[:, None] * numer_e + jnp.dot(weights, cache_v, precision=lax.Precision.HIGHEST)
    denom = alpha * denom_e + jnp.dot(weights, cache_c, precision=lax.Precision.HIGHEST)
    return (numer / denom[:, None]).astype(jnp.bfloat16)


def on_device(tokens_in, w_qkv, w_out, codebook, codes, reach):
    nx, ny, nc = lax.axis_size("hx"), lax.axis_size("hy"), lax.axis_size("hc")
    sizes = (nx, ny, nc)
    core_perm = _core_perm(*sizes)
    me_x, me_y, me_c = lax.axis_index("hx"), lax.axis_index("hy"), lax.axis_index("hc")
    n_ctx = lax.axis_size("ctx")
    g = lax.axis_index("ctx")
    rows, width = tokens_in.shape
    head_dim = codebook.shape[2]
    num_codes = codebook.shape[1]
    scale = 1.0 / math.sqrt(head_dim)
    half = rows // 2

    projected = project(tokens_in, w_qkv, sizes)
    queries = projected[:, :head_dim].astype(jnp.bfloat16)
    key_vals = projected[:, head_dim:].astype(jnp.bfloat16)
    values = key_vals[:, head_dim:]

    code_row = codes[0]
    code_ids = jnp.arange(num_codes, dtype=jnp.int32)
    hi = (code_row // 16).astype(jnp.bfloat16).reshape(1, -1)
    lo = (code_row % 16).astype(jnp.bfloat16).reshape(1, -1)
    kvw = key_vals.shape[1]
    code_rows = jnp.pad(jnp.concatenate([hi, lo], axis=0), ((0, 0), (0, kvw - rows)))
    kv_blob = jnp.concatenate([key_vals, code_rows, jnp.zeros((14, kvw), jnp.bfloat16)], axis=0)
    route = [(i, i + 1) for i in range(n_ctx - 1)]
    prev_blob = lax.ppermute(kv_blob, "ctx", route)
    prev_kv = prev_blob[:rows]
    prev_codes = (
        prev_blob[rows, :rows].astype(jnp.int32) * 16 + prev_blob[rows + 1, :rows].astype(jnp.int32)
    )

    onehot_own = (code_row[:, None] == code_ids[None, :]).astype(jnp.bfloat16)
    sums = lax.dot_general(
        onehot_own, values, (((0,), (0,)), ((), ())), preferred_element_type=jnp.float32
    )
    counts = jnp.sum(onehot_own.astype(jnp.float32), axis=0)
    span = num_codes // n_ctx
    cache_v, cache_c = code_prefix(sums, counts, span, n_ctx, head_dim)
    prev_ok = (jnp.arange(rows, dtype=jnp.int32) < BLK - reach[0]) & (g > 0)
    onehot_prev = (
        (prev_codes[:, None] == code_ids[None, :]) & prev_ok[:, None]
    ).astype(jnp.bfloat16)
    cache_v = cache_v + lax.dot_general(
        onehot_prev, prev_kv[:, head_dim:], (((0,), (0,)), ((), ())),
        preferred_element_type=jnp.float32,
    )
    cache_c = cache_c + jnp.sum(onehot_prev.astype(jnp.float32), axis=0)

    ext_kv = jnp.concatenate([prev_kv, key_vals], axis=0)
    top_e, numer_e, denom_e, coded = attend_exact(
        queries,
        ext_kv[:, :head_dim],
        ext_kv[:, head_dim:],
        codebook[0],
        reach[0],
        g > 0,
        BLK,
        scale,
    )
    attended = attend_cache(top_e, numer_e, denom_e, coded, cache_v, cache_c)

    return reduce_out(attended, w_out, sizes)


def _pack(sums, counts, span, n, head_dim):
    hi = jnp.floor(counts / 64.0)
    lo = counts - hi * 64.0
    tail = jnp.zeros((n, 8, head_dim), jnp.float32)
    tail = tail.at[:, 0, :span].set(hi.reshape(n, span)).at[:, 1, :span].set(lo.reshape(n, span))
    return jnp.concatenate([sums.reshape(n, span, head_dim), tail], axis=1).astype(jnp.bfloat16)


def _unpack(blob, span):
    blob = blob.astype(jnp.float32)
    sums = blob[:, :span]
    counts = blob[:, span, :span] * 64.0 + blob[:, span + 1, :span]
    return sums, counts


def code_prefix(sums, counts, span, n, head_dim):
    got = lax.all_to_all(_pack(sums, counts, span, n, head_dim), "ctx", 0, 0, tiled=True)
    b = jnp.arange(n, dtype=jnp.int32)
    before = (b[None, :] <= b[:, None] - 2).astype(jnp.bfloat16)
    pre = jnp.einsum("bc,cxd->bxd", before, got, preferred_element_type=jnp.float32)
    total = pre[:, span] * 64.0 + pre[:, span + 1]
    hi = jnp.floor(total / 64.0)
    lo = total - hi * 64.0
    rows = lax.broadcasted_iota(jnp.int32, pre.shape, 1)
    pre = jnp.where(rows == span, hi[:, None, :], jnp.where(rows == span + 1, lo[:, None, :], pre))
    back = lax.all_to_all(pre.astype(jnp.bfloat16), "ctx", 0, 0, tiled=True)
    cache_v, cache_c = _unpack(back, span)
    return cache_v.reshape(n * span, head_dim), cache_c.reshape(n * span)

def project(tokens_in, w_qkv, sizes):
    nx, ny, nc = sizes
    n_head = nx * ny * nc
    core_perm = _core_perm(*sizes)
    me_c = lax.axis_index("hc")
    rows, width = tokens_in.shape
    half = rows // nc
    spread = jnp.broadcast_to(
        tokens_in.reshape(1, nc, half, width), (n_head // nc, nc, half, width)
    ).reshape(n_head, half, width)
    mine = lax.all_to_all(spread, HEAD_AXES, 0, 0, tiled=True)
    theirs = _send(mine, core_perm)
    w_local = w_qkv[:, 0, :].reshape(n_head, width, -1)
    dims = (((0, 2), (0, 1)), ((), ()))
    proj_own = lax.dot_general(mine, w_local, dims, preferred_element_type=jnp.float32)
    proj_oth = lax.dot_general(theirs, w_local, dims, preferred_element_type=jnp.float32)
    projected = jnp.where(
        me_c == 0,
        jnp.concatenate([proj_own, proj_oth], axis=0),
        jnp.concatenate([proj_oth, proj_own], axis=0),
    )
    return projected


def reduce_out(attended, w_out, sizes):
    nx, ny, nc = sizes
    core_perm = _core_perm(*sizes)
    me_c = lax.axis_index("hc")
    rows = attended.shape[0]
    w_full = w_out[0]
    cols = w_full.shape[1] // nc
    w_keep = lax.dynamic_slice_in_dim(w_full, me_c * cols, cols, 1)
    w_give = lax.dynamic_slice_in_dim(w_full, (1 - me_c) * cols, cols, 1)
    w_theirs = _send(w_give, core_perm)
    att_theirs = _send(attended, core_perm)
    summed = (
        jnp.dot(attended, w_keep, preferred_element_type=jnp.float32)
        + jnp.dot(att_theirs, w_theirs, preferred_element_type=jnp.float32)
    ).astype(jnp.bfloat16)
    n_head = nx * ny * nc
    chunks = summed.reshape(n_head, rows // n_head, cols)
    parts = lax.all_to_all(chunks, HEAD_AXES, 0, 0, tiled=True).astype(jnp.float32)
    parts = parts.reshape(n_head // nc, nc, rows // n_head, cols).sum(axis=0)
    out = jnp.concatenate([parts[i] for i in range(nc)], axis=1)
    return out.astype(jnp.bfloat16)


def solution(mesh):
    n_ctx, n_head = mesh.devices.shape
    devices = mesh.devices.reshape(n_ctx, 4, 4, n_head // 16)
    grid = Mesh(devices, ("ctx",) + HEAD_AXES)
    in_specs = (
        P("ctx", HEAD_AXES),
        P(None, HEAD_AXES, None),
        P(HEAD_AXES, None, None),
        P(HEAD_AXES, None, None),
        P(HEAD_AXES, "ctx"),
        P("ctx"),
    )
    out_specs = P(("ctx",) + HEAD_AXES, None)
    return jax.shard_map(
        on_device, mesh=grid, in_specs=in_specs, out_specs=out_specs, check_vma=False
    )
```

```python
import math

import jax
import jax.numpy as jnp
from jax import lax
from jax.sharding import Mesh
from jax.sharding import PartitionSpec as P

BLK = 256
HEAD_AXES = ("hx", "hy", "hc")


def _flat(x, y, c, ny, nc):
    return (x * ny + y) * nc + c


def _ring_perm(stage, d, nx, ny, nc):
    pairs = []
    for x in range(nx):
        for y in range(ny):
            for c in range(nc):
                along_y = (c == 0) == (stage == 0)
                if along_y:
                    tx, ty = x, (y + d) % ny
                else:
                    tx, ty = (x + d) % nx, y
                pairs.append((_flat(x, y, c, ny, nc), _flat(tx, ty, c, ny, nc)))
    return pairs


def _core_perm(nx, ny, nc):
    pairs = []
    for x in range(nx):
        for y in range(ny):
            for c in range(nc):
                pairs.append((_flat(x, y, c, ny, nc), _flat(x, y, 1 - c, ny, nc)))
    return pairs


def _send(value, perm):
    return lax.ppermute(value, HEAD_AXES, perm)


def gather_ring(blk, stage, sizes):
    p1 = _send(blk, _ring_perm(stage, 1, *sizes))
    m1 = _send(blk, _ring_perm(stage, -1, *sizes))
    h = blk.shape[0] // 2
    a = _send(p1[:h], _ring_perm(stage, 1, *sizes))
    b = _send(m1[h:], _ring_perm(stage, -1, *sizes))
    far = jnp.concatenate([a, b], axis=0)
    return jnp.stack([blk, p1, far, m1])


def reduce_ring(data, stage, sizes):
    h = data.shape[1] // 2
    rp = _send(data[2, :h].astype(jnp.bfloat16), _ring_perm(stage, 1, *sizes))
    rm = _send(data[2, h:].astype(jnp.bfloat16), _ring_perm(stage, -1, *sizes))
    ahead = jnp.concatenate([data[1, :h] + rp, data[1, h:]], axis=0)
    behind = jnp.concatenate([data[3, :h], data[3, h:] + rm], axis=0)
    gp = _send(ahead.astype(jnp.bfloat16), _ring_perm(stage, 1, *sizes))
    gm = _send(behind.astype(jnp.bfloat16), _ring_perm(stage, -1, *sizes))
    return data[0] + gp.astype(jnp.float32) + gm.astype(jnp.float32)


def attend_exact(queries, keys_win, vals_win, book, reach_one, prev_flag, block_len, scale):
    exact = (
        lax.dot_general(
            queries, keys_win, (((1,), (1,)), ((), ())), preferred_element_type=jnp.float32
        )
        * scale
    )
    coded = (
        lax.dot_general(queries, book, (((1,), (1,)), ((), ())), preferred_element_type=jnp.float32)
        * scale
    )
    rows = lax.broadcasted_iota(jnp.int32, exact.shape, 0)
    cols = lax.broadcasted_iota(jnp.int32, exact.shape, 1)
    prev_ok = (cols < block_len) & (cols >= block_len - reach_one) & prev_flag
    curr_ok = (cols >= block_len) & (cols - block_len <= rows)
    allowed = prev_ok | curr_ok
    top_e = jnp.max(jnp.where(allowed, exact, -jnp.inf), axis=1)
    probs = jnp.exp(jnp.where(allowed, exact - top_e[:, None], -jnp.inf))
    numer = jnp.dot(probs.astype(jnp.bfloat16), vals_win, preferred_element_type=jnp.float32)
    denom = jnp.sum(probs, axis=1)
    return top_e, numer, denom, coded


def attend_cache(top_e, numer_e, denom_e, coded, cache_v, cache_c):
    valid = cache_c > 0.5
    top = jnp.maximum(top_e, jnp.max(jnp.where(valid[None, :], coded, -jnp.inf), axis=1))
    alpha = jnp.exp(top_e - top)
    weights = jnp.exp(jnp.where(valid[None, :], coded - top[:, None], -jnp.inf))
    numer = alpha[:, None] * numer_e + jnp.dot(weights, cache_v, precision=lax.Precision.HIGHEST)
    denom = alpha * denom_e + jnp.dot(weights, cache_c, precision=lax.Precision.HIGHEST)
    return (numer / denom[:, None]).astype(jnp.bfloat16)


def on_device(tokens_in, w_qkv, w_out, codebook, codes, reach):
    nx, ny, nc = lax.axis_size("hx"), lax.axis_size("hy"), lax.axis_size("hc")
    sizes = (nx, ny, nc)
    core_perm = _core_perm(*sizes)
    me_x, me_y, me_c = lax.axis_index("hx"), lax.axis_index("hy"), lax.axis_index("hc")
    n_ctx = lax.axis_size("ctx")
    g = lax.axis_index("ctx")
    rows, width = tokens_in.shape
    head_dim = codebook.shape[2]
    num_codes = codebook.shape[1]
    scale = 1.0 / math.sqrt(head_dim)
    half = rows // 2

    code_row = codes[0]
    code_ids = jnp.arange(num_codes, dtype=jnp.int32)
    route = [(i, i + 1) for i in range(n_ctx - 1)]
    prev_codes = lax.ppermute(code_row, "ctx", route)
    prev_codes, tokens_in = lax.optimization_barrier((prev_codes, tokens_in))

    projected = project(tokens_in, w_qkv, sizes)
    queries = projected[:, :head_dim].astype(jnp.bfloat16)
    key_vals = projected[:, head_dim:].astype(jnp.bfloat16)
    values = key_vals[:, head_dim:]
    prev_kv = lax.ppermute(key_vals, "ctx", route)

    onehot_own = (code_row[:, None] == code_ids[None, :]).astype(jnp.bfloat16)
    sums = lax.dot_general(
        onehot_own, values, (((0,), (0,)), ((), ())), preferred_element_type=jnp.float32
    )
    counts = jnp.sum(onehot_own.astype(jnp.float32), axis=0)
    span = num_codes // n_ctx
    cache_v, cache_c = code_prefix(sums, counts, span, n_ctx, head_dim)
    prev_ok = (jnp.arange(rows, dtype=jnp.int32) < BLK - reach[0]) & (g > 0)
    onehot_prev = (
        (prev_codes[:, None] == code_ids[None, :]) & prev_ok[:, None]
    ).astype(jnp.bfloat16)
    cache_v = cache_v + lax.dot_general(
        onehot_prev, prev_kv[:, head_dim:], (((0,), (0,)), ((), ())),
        preferred_element_type=jnp.float32,
    )
    cache_c = cache_c + jnp.sum(onehot_prev.astype(jnp.float32), axis=0)

    ext_kv = jnp.concatenate([prev_kv, key_vals], axis=0)
    top_e, numer_e, denom_e, coded = attend_exact(
        queries,
        ext_kv[:, :head_dim],
        ext_kv[:, head_dim:],
        codebook[0],
        reach[0],
        g > 0,
        BLK,
        scale,
    )
    attended = attend_cache(top_e, numer_e, denom_e, coded, cache_v, cache_c)

    return reduce_out(attended, w_out, sizes)


def _pack(sums, counts, span, n, head_dim):
    hi = jnp.floor(counts / 64.0)
    lo = counts - hi * 64.0
    tail = jnp.zeros((n, 8, head_dim), jnp.float32)
    tail = tail.at[:, 0, :span].set(hi.reshape(n, span)).at[:, 1, :span].set(lo.reshape(n, span))
    return jnp.concatenate([sums.reshape(n, span, head_dim), tail], axis=1).astype(jnp.bfloat16)


def _unpack(blob, span):
    blob = blob.astype(jnp.float32)
    sums = blob[:, :span]
    counts = blob[:, span, :span] * 64.0 + blob[:, span + 1, :span]
    return sums, counts


def code_prefix(sums, counts, span, n, head_dim):
    got = lax.all_to_all(_pack(sums, counts, span, n, head_dim), "ctx", 0, 0, tiled=True)
    b = jnp.arange(n, dtype=jnp.int32)
    before = (b[None, :] <= b[:, None] - 2).astype(jnp.bfloat16)
    pre = jnp.einsum("bc,cxd->bxd", before, got, preferred_element_type=jnp.float32)
    total = pre[:, span] * 64.0 + pre[:, span + 1]
    hi = jnp.floor(total / 64.0)
    lo = total - hi * 64.0
    rows = lax.broadcasted_iota(jnp.int32, pre.shape, 1)
    pre = jnp.where(rows == span, hi[:, None, :], jnp.where(rows == span + 1, lo[:, None, :], pre))
    back = lax.all_to_all(pre.astype(jnp.bfloat16), "ctx", 0, 0, tiled=True)
    cache_v, cache_c = _unpack(back, span)
    return cache_v.reshape(n * span, head_dim), cache_c.reshape(n * span)

def project(tokens_in, w_qkv, sizes):
    nx, ny, nc = sizes
    n_head = nx * ny * nc
    core_perm = _core_perm(*sizes)
    me_c = lax.axis_index("hc")
    rows, width = tokens_in.shape
    half = rows // nc
    spread = jnp.broadcast_to(
        tokens_in.reshape(1, nc, half, width), (n_head // nc, nc, half, width)
    ).reshape(n_head, half, width)
    mine = lax.all_to_all(spread, HEAD_AXES, 0, 0, tiled=True)
    theirs = _send(mine, core_perm)
    w_local = w_qkv[:, 0, :].reshape(n_head, width, -1)
    dims = (((0, 2), (0, 1)), ((), ()))
    proj_own = lax.dot_general(mine, w_local, dims, preferred_element_type=jnp.float32)
    proj_oth = lax.dot_general(theirs, w_local, dims, preferred_element_type=jnp.float32)
    projected = jnp.where(
        me_c == 0,
        jnp.concatenate([proj_own, proj_oth], axis=0),
        jnp.concatenate([proj_oth, proj_own], axis=0),
    )
    return projected


def reduce_out(attended, w_out, sizes):
    nx, ny, nc = sizes
    core_perm = _core_perm(*sizes)
    me_c = lax.axis_index("hc")
    rows = attended.shape[0]
    w_full = w_out[0]
    cols = w_full.shape[1] // nc
    w_keep = lax.dynamic_slice_in_dim(w_full, me_c * cols, cols, 1)
    w_give = lax.dynamic_slice_in_dim(w_full, (1 - me_c) * cols, cols, 1)
    w_theirs = _send(w_give, core_perm)
    att_theirs = _send(attended, core_perm)
    summed = (
        jnp.dot(attended, w_keep, preferred_element_type=jnp.float32)
        + jnp.dot(att_theirs, w_theirs, preferred_element_type=jnp.float32)
    ).astype(jnp.bfloat16)
    n_head = nx * ny * nc
    chunks = summed.reshape(n_head, rows // n_head, cols)
    parts = lax.all_to_all(chunks, HEAD_AXES, 0, 0, tiled=True).astype(jnp.float32)
    parts = parts.reshape(n_head // nc, nc, rows // n_head, cols).sum(axis=0)
    out = jnp.concatenate([parts[i] for i in range(nc)], axis=1)
    return out.astype(jnp.bfloat16)


def solution(mesh):
    n_ctx, n_head = mesh.devices.shape
    devices = mesh.devices.reshape(n_ctx, 4, 4, n_head // 16)
    grid = Mesh(devices, ("ctx",) + HEAD_AXES)
    in_specs = (
        P("ctx", HEAD_AXES),
        P(None, HEAD_AXES, None),
        P(HEAD_AXES, None, None),
        P(HEAD_AXES, None, None),
        P(HEAD_AXES, "ctx"),
        P("ctx"),
    )
    out_specs = P(("ctx",) + HEAD_AXES, None)
    return jax.shard_map(
        on_device, mesh=grid, in_specs=in_specs, out_specs=out_specs, check_vma=False
    )
```

```python
import math

import jax
import jax.numpy as jnp
from jax import lax
from jax.sharding import Mesh
from jax.sharding import PartitionSpec as P

BLK = 256
HEAD_AXES = ("hx", "hy", "hc")


def _flat(x, y, c, ny, nc):
    return (x * ny + y) * nc + c


def _ring_perm(stage, d, nx, ny, nc):
    pairs = []
    for x in range(nx):
        for y in range(ny):
            for c in range(nc):
                along_y = (c == 0) == (stage == 0)
                if along_y:
                    tx, ty = x, (y + d) % ny
                else:
                    tx, ty = (x + d) % nx, y
                pairs.append((_flat(x, y, c, ny, nc), _flat(tx, ty, c, ny, nc)))
    return pairs


def _core_perm(nx, ny, nc):
    pairs = []
    for x in range(nx):
        for y in range(ny):
            for c in range(nc):
                pairs.append((_flat(x, y, c, ny, nc), _flat(x, y, 1 - c, ny, nc)))
    return pairs


def _send(value, perm):
    return lax.ppermute(value, HEAD_AXES, perm)


def gather_ring(blk, stage, sizes):
    p1 = _send(blk, _ring_perm(stage, 1, *sizes))
    m1 = _send(blk, _ring_perm(stage, -1, *sizes))
    h = blk.shape[0] // 2
    a = _send(p1[:h], _ring_perm(stage, 1, *sizes))
    b = _send(m1[h:], _ring_perm(stage, -1, *sizes))
    far = jnp.concatenate([a, b], axis=0)
    return jnp.stack([blk, p1, far, m1])


def reduce_ring(data, stage, sizes):
    h = data.shape[1] // 2
    rp = _send(data[2, :h].astype(jnp.bfloat16), _ring_perm(stage, 1, *sizes))
    rm = _send(data[2, h:].astype(jnp.bfloat16), _ring_perm(stage, -1, *sizes))
    ahead = jnp.concatenate([data[1, :h] + rp, data[1, h:]], axis=0)
    behind = jnp.concatenate([data[3, :h], data[3, h:] + rm], axis=0)
    gp = _send(ahead.astype(jnp.bfloat16), _ring_perm(stage, 1, *sizes))
    gm = _send(behind.astype(jnp.bfloat16), _ring_perm(stage, -1, *sizes))
    return data[0] + gp.astype(jnp.float32) + gm.astype(jnp.float32)


def attend_exact(queries, keys_win, vals_win, book, reach_one, prev_flag, block_len, scale):
    exact = (
        lax.dot_general(
            queries, keys_win, (((1,), (1,)), ((), ())), preferred_element_type=jnp.float32
        )
        * scale
    )
    coded = (
        lax.dot_general(queries, book, (((1,), (1,)), ((), ())), preferred_element_type=jnp.float32)
        * scale
    )
    rows = lax.broadcasted_iota(jnp.int32, exact.shape, 0)
    cols = lax.broadcasted_iota(jnp.int32, exact.shape, 1)
    prev_ok = (cols < block_len) & (cols >= block_len - reach_one) & prev_flag
    curr_ok = (cols >= block_len) & (cols - block_len <= rows)
    allowed = prev_ok | curr_ok
    top_e = jnp.max(jnp.where(allowed, exact, -jnp.inf), axis=1)
    probs = jnp.exp(jnp.where(allowed, exact - top_e[:, None], -jnp.inf))
    numer = jnp.dot(probs.astype(jnp.bfloat16), vals_win, preferred_element_type=jnp.float32)
    denom = jnp.sum(probs, axis=1)
    return top_e, numer, denom, coded


def attend_cache(top_e, numer_e, denom_e, coded, cache_v, cache_c):
    valid = cache_c > 0.5
    top = jnp.maximum(top_e, jnp.max(jnp.where(valid[None, :], coded, -jnp.inf), axis=1))
    alpha = jnp.exp(top_e - top)
    weights = jnp.exp(jnp.where(valid[None, :], coded - top[:, None], -jnp.inf))
    numer = alpha[:, None] * numer_e + jnp.dot(weights, cache_v, precision=lax.Precision.HIGHEST)
    denom = alpha * denom_e + jnp.dot(weights, cache_c, precision=lax.Precision.HIGHEST)
    return (numer / denom[:, None]).astype(jnp.bfloat16)


def on_device(tokens_in, w_qkv, w_out, codebook, codes, reach):
    nx, ny, nc = lax.axis_size("hx"), lax.axis_size("hy"), lax.axis_size("hc")
    sizes = (nx, ny, nc)
    core_perm = _core_perm(*sizes)
    me_x, me_y, me_c = lax.axis_index("hx"), lax.axis_index("hy"), lax.axis_index("hc")
    n_ctx = lax.axis_size("ctx")
    g = lax.axis_index("ctx")
    rows, width = tokens_in.shape
    head_dim = codebook.shape[2]
    num_codes = codebook.shape[1]
    scale = 1.0 / math.sqrt(head_dim)
    half = rows // 2

    projected = project(tokens_in, w_qkv, sizes)
    queries = projected[:, :head_dim].astype(jnp.bfloat16)
    key_vals = projected[:, head_dim:].astype(jnp.bfloat16)
    values = key_vals[:, head_dim:]

    code_row = codes[0]
    code_ids = jnp.arange(num_codes, dtype=jnp.int32)
    hi = (code_row // 16).astype(jnp.bfloat16).reshape(1, -1)
    lo = (code_row % 16).astype(jnp.bfloat16).reshape(1, -1)
    kvw = key_vals.shape[1]
    code_rows = jnp.pad(jnp.concatenate([hi, lo], axis=0), ((0, 0), (0, kvw - rows)))
    kv_blob = jnp.concatenate([key_vals, code_rows, jnp.zeros((14, kvw), jnp.bfloat16)], axis=0)
    route = [(i, i + 1) for i in range(n_ctx - 1)]
    prev_blob = lax.ppermute(kv_blob, "ctx", route)
    prev_kv = prev_blob[:rows]
    prev_codes = (
        prev_blob[rows, :rows].astype(jnp.int32) * 16 + prev_blob[rows + 1, :rows].astype(jnp.int32)
    )

    onehot_own = (code_row[:, None] == code_ids[None, :]).astype(jnp.bfloat16)
    sums = lax.dot_general(
        onehot_own, values, (((0,), (0,)), ((), ())), preferred_element_type=jnp.float32
    )
    counts = jnp.sum(onehot_own.astype(jnp.float32), axis=0)
    span = num_codes // n_ctx
    cache_v, cache_c = code_prefix(sums, counts, span, n_ctx, head_dim)
    prev_ok = (jnp.arange(rows, dtype=jnp.int32) < BLK - reach[0]) & (g > 0)
    onehot_prev = (
        (prev_codes[:, None] == code_ids[None, :]) & prev_ok[:, None]
    ).astype(jnp.bfloat16)
    cache_v = cache_v + lax.dot_general(
        onehot_prev, prev_kv[:, head_dim:], (((0,), (0,)), ((), ())),
        preferred_element_type=jnp.float32,
    )
    cache_c = cache_c + jnp.sum(onehot_prev.astype(jnp.float32), axis=0)

    ext_kv = jnp.concatenate([prev_kv, key_vals], axis=0)
    top_e, numer_e, denom_e, coded = attend_exact(
        queries,
        ext_kv[:, :head_dim],
        ext_kv[:, head_dim:],
        codebook[0],
        reach[0],
        g > 0,
        BLK,
        scale,
    )
    attended = attend_cache(top_e, numer_e, denom_e, coded, cache_v, cache_c)

    return reduce_out(attended, w_out, sizes)


def _pack(sums, counts, span, n, head_dim):
    hi = jnp.floor(counts / 64.0)
    lo = counts - hi * 64.0
    tail = jnp.zeros((n, 8, head_dim), jnp.float32)
    tail = tail.at[:, 0, :span].set(hi.reshape(n, span)).at[:, 1, :span].set(lo.reshape(n, span))
    return jnp.concatenate([sums.reshape(n, span, head_dim), tail], axis=1).astype(jnp.bfloat16)


def _unpack(blob, span):
    blob = blob.astype(jnp.float32)
    sums = blob[:, :span]
    counts = blob[:, span, :span] * 64.0 + blob[:, span + 1, :span]
    return sums, counts


def code_prefix(sums, counts, span, n, head_dim):
    got = lax.all_to_all(_pack(sums, counts, span, n, head_dim), "ctx", 0, 0, tiled=True)
    b = jnp.arange(n, dtype=jnp.int32)
    before = (b[None, :] <= b[:, None] - 2).astype(jnp.bfloat16)
    pre = jnp.einsum("bc,cxd->bxd", before, got, preferred_element_type=jnp.float32)
    total = pre[:, span] * 64.0 + pre[:, span + 1]
    hi = jnp.floor(total / 64.0)
    lo = total - hi * 64.0
    rows = lax.broadcasted_iota(jnp.int32, pre.shape, 1)
    pre = jnp.where(rows == span, hi[:, None, :], jnp.where(rows == span + 1, lo[:, None, :], pre))
    back = lax.all_to_all(pre.astype(jnp.bfloat16), "ctx", 0, 0, tiled=True)
    cache_v, cache_c = _unpack(back, span)
    return cache_v.reshape(n * span, head_dim), cache_c.reshape(n * span)

def project(tokens_in, w_qkv, sizes):
    nx, ny, nc = sizes
    n_head = nx * ny * nc
    core_perm = _core_perm(*sizes)
    me_c = lax.axis_index("hc")
    rows, width = tokens_in.shape
    half = rows // nc
    spread = jnp.broadcast_to(
        tokens_in.reshape(1, nc, half, width), (n_head // nc, nc, half, width)
    ).reshape(n_head, half, width)
    mine = lax.all_to_all(spread, HEAD_AXES, 0, 0, tiled=True)
    theirs = _send(mine, core_perm)
    w_local = w_qkv[:, 0, :].reshape(n_head, width, -1)
    dims = (((0, 2), (0, 1)), ((), ()))
    proj_own = lax.dot_general(mine, w_local, dims, preferred_element_type=jnp.float32)
    proj_oth = lax.dot_general(theirs, w_local, dims, preferred_element_type=jnp.float32)
    projected = jnp.where(
        me_c == 0,
        jnp.concatenate([proj_own, proj_oth], axis=0),
        jnp.concatenate([proj_oth, proj_own], axis=0),
    )
    return projected


def reduce_out(attended, w_out, sizes):
    nx, ny, nc = sizes
    core_perm = _core_perm(*sizes)
    me_c = lax.axis_index("hc")
    rows = attended.shape[0]
    w_full = w_out[0]
    cols = w_full.shape[1] // nc
    w_keep = lax.dynamic_slice_in_dim(w_full, me_c * cols, cols, 1)
    w_give = lax.dynamic_slice_in_dim(w_full, (1 - me_c) * cols, cols, 1)
    w_theirs = _send(w_give, core_perm)
    att_theirs = _send(attended, core_perm)
    summed = (
        jnp.dot(attended, w_keep, preferred_element_type=jnp.float32)
        + jnp.dot(att_theirs, w_theirs, preferred_element_type=jnp.float32)
    ).astype(jnp.bfloat16)
    n_chip = nx * ny
    per_chip = rows // n_chip
    chunks = summed.reshape(n_chip, per_chip, cols)
    parts = lax.all_to_all(chunks, ("hx", "hy"), 0, 0, tiled=True).astype(jnp.float32)
    parts = parts.sum(axis=0).reshape(nc, per_chip // nc, cols)
    mine = lax.dynamic_index_in_dim(parts, me_c, 0, keepdims=False)
    other = lax.dynamic_index_in_dim(parts, 1 - me_c, 0, keepdims=False).astype(jnp.bfloat16)
    got = _send(other, core_perm).astype(jnp.float32)
    out = jnp.where(
        me_c == 0, jnp.concatenate([mine, got], axis=1), jnp.concatenate([got, mine], axis=1)
    )
    return out.astype(jnp.bfloat16)


def solution(mesh):
    n_ctx, n_head = mesh.devices.shape
    devices = mesh.devices.reshape(n_ctx, 4, 4, n_head // 16)
    grid = Mesh(devices, ("ctx",) + HEAD_AXES)
    in_specs = (
        P("ctx", HEAD_AXES),
        P(None, HEAD_AXES, None),
        P(HEAD_AXES, None, None),
        P(HEAD_AXES, None, None),
        P(HEAD_AXES, "ctx"),
        P("ctx"),
    )
    out_specs = P(("ctx",) + HEAD_AXES, None)
    return jax.shard_map(
        on_device, mesh=grid, in_specs=in_specs, out_specs=out_specs, check_vma=False
    )
```

```python
import math

import jax
import jax.numpy as jnp
from jax import lax
from jax.sharding import Mesh
from jax.sharding import PartitionSpec as P

BLK = 256
HEAD_AXES = ("hx", "hy", "hc")


def _flat(x, y, c, ny, nc):
    return (x * ny + y) * nc + c


def _ring_perm(stage, d, nx, ny, nc):
    pairs = []
    for x in range(nx):
        for y in range(ny):
            for c in range(nc):
                along_y = (c == 0) == (stage == 0)
                if along_y:
                    tx, ty = x, (y + d) % ny
                else:
                    tx, ty = (x + d) % nx, y
                pairs.append((_flat(x, y, c, ny, nc), _flat(tx, ty, c, ny, nc)))
    return pairs


def _core_perm(nx, ny, nc):
    pairs = []
    for x in range(nx):
        for y in range(ny):
            for c in range(nc):
                pairs.append((_flat(x, y, c, ny, nc), _flat(x, y, 1 - c, ny, nc)))
    return pairs


def _send(value, perm):
    return lax.ppermute(value, HEAD_AXES, perm)


def gather_ring(blk, stage, sizes):
    p1 = _send(blk, _ring_perm(stage, 1, *sizes))
    m1 = _send(blk, _ring_perm(stage, -1, *sizes))
    h = blk.shape[0] // 2
    a = _send(p1[:h], _ring_perm(stage, 1, *sizes))
    b = _send(m1[h:], _ring_perm(stage, -1, *sizes))
    far = jnp.concatenate([a, b], axis=0)
    return jnp.stack([blk, p1, far, m1])


def reduce_ring(data, stage, sizes):
    h = data.shape[1] // 2
    rp = _send(data[2, :h].astype(jnp.bfloat16), _ring_perm(stage, 1, *sizes))
    rm = _send(data[2, h:].astype(jnp.bfloat16), _ring_perm(stage, -1, *sizes))
    ahead = jnp.concatenate([data[1, :h] + rp, data[1, h:]], axis=0)
    behind = jnp.concatenate([data[3, :h], data[3, h:] + rm], axis=0)
    gp = _send(ahead.astype(jnp.bfloat16), _ring_perm(stage, 1, *sizes))
    gm = _send(behind.astype(jnp.bfloat16), _ring_perm(stage, -1, *sizes))
    return data[0] + gp.astype(jnp.float32) + gm.astype(jnp.float32)


def attend_exact(queries, keys_win, vals_win, book, reach_one, prev_flag, block_len, scale):
    exact = (
        lax.dot_general(
            queries, keys_win, (((1,), (1,)), ((), ())), preferred_element_type=jnp.float32
        )
        * scale
    )
    coded = (
        lax.dot_general(queries, book, (((1,), (1,)), ((), ())), preferred_element_type=jnp.float32)
        * scale
    )
    rows = lax.broadcasted_iota(jnp.int32, exact.shape, 0)
    cols = lax.broadcasted_iota(jnp.int32, exact.shape, 1)
    prev_ok = (cols < block_len) & (cols >= block_len - reach_one) & prev_flag
    curr_ok = (cols >= block_len) & (cols - block_len <= rows)
    allowed = prev_ok | curr_ok
    top_e = jnp.max(jnp.where(allowed, exact, -jnp.inf), axis=1)
    probs = jnp.exp(jnp.where(allowed, exact - top_e[:, None], -jnp.inf))
    numer = jnp.dot(probs.astype(jnp.bfloat16), vals_win, preferred_element_type=jnp.float32)
    denom = jnp.sum(probs, axis=1)
    return top_e, numer, denom, coded


def attend_cache(top_e, numer_e, denom_e, coded, cache_v, cache_c):
    valid = cache_c > 0.5
    top = jnp.maximum(top_e, jnp.max(jnp.where(valid[None, :], coded, -jnp.inf), axis=1))
    alpha = jnp.exp(top_e - top)
    weights = jnp.exp(jnp.where(valid[None, :], coded - top[:, None], -jnp.inf))
    numer = alpha[:, None] * numer_e + jnp.dot(weights, cache_v, precision=lax.Precision.HIGHEST)
    denom = alpha * denom_e + jnp.dot(weights, cache_c, precision=lax.Precision.HIGHEST)
    return (numer / denom[:, None]).astype(jnp.bfloat16)


def on_device(tokens_in, w_qkv, w_out, codebook, codes, reach):
    nx, ny, nc = lax.axis_size("hx"), lax.axis_size("hy"), lax.axis_size("hc")
    sizes = (nx, ny, nc)
    core_perm = _core_perm(*sizes)
    me_x, me_y, me_c = lax.axis_index("hx"), lax.axis_index("hy"), lax.axis_index("hc")
    n_ctx = lax.axis_size("ctx")
    g = lax.axis_index("ctx")
    rows, width = tokens_in.shape
    head_dim = codebook.shape[2]
    num_codes = codebook.shape[1]
    scale = 1.0 / math.sqrt(head_dim)
    half = rows // 2

    projected = project(tokens_in, w_qkv, sizes)
    queries = projected[:, :head_dim].astype(jnp.bfloat16)
    key_vals = projected[:, head_dim:].astype(jnp.bfloat16)
    values = key_vals[:, head_dim:]

    code_row = codes[0]
    code_ids = jnp.arange(num_codes, dtype=jnp.int32)
    hi = (code_row // 16).astype(jnp.bfloat16).reshape(1, -1)
    lo = (code_row % 16).astype(jnp.bfloat16).reshape(1, -1)
    kvw = key_vals.shape[1]
    code_rows = jnp.pad(jnp.concatenate([hi, lo], axis=0), ((0, 0), (0, kvw - rows)))
    kv_blob = jnp.concatenate([key_vals, code_rows, jnp.zeros((14, kvw), jnp.bfloat16)], axis=0)
    route = [(i, i + 1) for i in range(n_ctx - 1)]
    prev_blob = lax.ppermute(kv_blob, "ctx", route)
    prev_kv = prev_blob[:rows]
    prev_codes = (
        prev_blob[rows, :rows].astype(jnp.int32) * 16 + prev_blob[rows + 1, :rows].astype(jnp.int32)
    )

    onehot_own = (code_row[:, None] == code_ids[None, :]).astype(jnp.bfloat16)
    sums = lax.dot_general(
        onehot_own, values, (((0,), (0,)), ((), ())), preferred_element_type=jnp.float32
    )
    counts = jnp.sum(onehot_own.astype(jnp.float32), axis=0)
    span = num_codes // n_ctx
    cache_v, cache_c = code_prefix(sums, counts, span, n_ctx, head_dim)
    prev_ok = (jnp.arange(rows, dtype=jnp.int32) < BLK - reach[0]) & (g > 0)
    onehot_prev = (
        (prev_codes[:, None] == code_ids[None, :]) & prev_ok[:, None]
    ).astype(jnp.bfloat16)
    cache_v = cache_v + lax.dot_general(
        onehot_prev, prev_kv[:, head_dim:], (((0,), (0,)), ((), ())),
        preferred_element_type=jnp.float32,
    )
    cache_c = cache_c + jnp.sum(onehot_prev.astype(jnp.float32), axis=0)

    ext_kv = jnp.concatenate([prev_kv, key_vals], axis=0)
    top_e, numer_e, denom_e, coded = attend_exact(
        queries,
        ext_kv[:, :head_dim],
        ext_kv[:, head_dim:],
        codebook[0],
        reach[0],
        g > 0,
        BLK,
        scale,
    )
    attended = attend_cache(top_e, numer_e, denom_e, coded, cache_v, cache_c)

    return reduce_out(attended, w_out, sizes)


def _pack(sums, counts, span, n, head_dim):
    hi = jnp.floor(counts / 64.0)
    lo = counts - hi * 64.0
    tail = jnp.zeros((n, 8, head_dim), jnp.float32)
    tail = tail.at[:, 0, :span].set(hi.reshape(n, span)).at[:, 1, :span].set(lo.reshape(n, span))
    return jnp.concatenate([sums.reshape(n, span, head_dim), tail], axis=1).astype(jnp.bfloat16)


def _unpack(blob, span):
    blob = blob.astype(jnp.float32)
    sums = blob[:, :span]
    counts = blob[:, span, :span] * 64.0 + blob[:, span + 1, :span]
    return sums, counts


def code_prefix(sums, counts, span, n, head_dim):
    got = lax.all_to_all(_pack(sums, counts, span, n, head_dim), "ctx", 0, 0, tiled=True)
    b = jnp.arange(n, dtype=jnp.int32)
    before = (b[None, :] <= b[:, None] - 2).astype(jnp.bfloat16)
    pre = jnp.einsum("bc,cxd->bxd", before, got, preferred_element_type=jnp.float32)
    total = pre[:, span] * 64.0 + pre[:, span + 1]
    hi = jnp.floor(total / 64.0)
    lo = total - hi * 64.0
    rows = lax.broadcasted_iota(jnp.int32, pre.shape, 1)
    pre = jnp.where(rows == span, hi[:, None, :], jnp.where(rows == span + 1, lo[:, None, :], pre))
    back = lax.all_to_all(pre.astype(jnp.bfloat16), "ctx", 0, 0, tiled=True)
    cache_v, cache_c = _unpack(back, span)
    return cache_v.reshape(n * span, head_dim), cache_c.reshape(n * span)

def project(tokens_in, w_qkv, sizes):
    nx, ny, nc = sizes
    n_head = nx * ny * nc
    core_perm = _core_perm(*sizes)
    me_c = lax.axis_index("hc")
    rows, width = tokens_in.shape
    half = rows // nc
    spread = jnp.broadcast_to(
        tokens_in.reshape(1, nc, half, width), (n_head // nc, nc, half, width)
    ).reshape(n_head, half, width)
    mine = lax.all_to_all(spread, HEAD_AXES, 0, 0, tiled=True)
    theirs = _send(mine, core_perm)
    w_local = w_qkv[:, 0, :].reshape(n_head, width, -1)
    both = jnp.where(
        me_c == 0, jnp.concatenate([mine, theirs], axis=1), jnp.concatenate([theirs, mine], axis=1)
    )
    dims = (((0, 2), (0, 1)), ((), ()))
    projected = lax.dot_general(both, w_local, dims, preferred_element_type=jnp.float32)
    return projected


def reduce_out(attended, w_out, sizes):
    nx, ny, nc = sizes
    core_perm = _core_perm(*sizes)
    me_c = lax.axis_index("hc")
    rows = attended.shape[0]
    w_full = w_out[0]
    cols = w_full.shape[1] // nc
    w_keep = lax.dynamic_slice_in_dim(w_full, me_c * cols, cols, 1)
    w_give = lax.dynamic_slice_in_dim(w_full, (1 - me_c) * cols, cols, 1)
    w_theirs = _send(w_give, core_perm)
    att_theirs = _send(attended, core_perm)
    summed = (
        jnp.dot(attended, w_keep, preferred_element_type=jnp.float32)
        + jnp.dot(att_theirs, w_theirs, preferred_element_type=jnp.float32)
    ).astype(jnp.bfloat16)
    n_head = nx * ny * nc
    chunks = summed.reshape(n_head, rows // n_head, cols)
    parts = lax.all_to_all(chunks, HEAD_AXES, 0, 0, tiled=True).astype(jnp.float32)
    parts = parts.reshape(n_head // nc, nc, rows // n_head, cols).sum(axis=0)
    out = jnp.concatenate([parts[i] for i in range(nc)], axis=1)
    return out.astype(jnp.bfloat16)


def solution(mesh):
    n_ctx, n_head = mesh.devices.shape
    devices = mesh.devices.reshape(n_ctx, 4, 4, n_head // 16)
    grid = Mesh(devices, ("ctx",) + HEAD_AXES)
    in_specs = (
        P("ctx", HEAD_AXES),
        P(None, HEAD_AXES, None),
        P(HEAD_AXES, None, None),
        P(HEAD_AXES, None, None),
        P(HEAD_AXES, "ctx"),
        P("ctx"),
    )
    out_specs = P(("ctx",) + HEAD_AXES, None)
    return jax.shard_map(
        on_device, mesh=grid, in_specs=in_specs, out_specs=out_specs, check_vma=False
    )
```

```python
import math

import jax
import jax.numpy as jnp
from jax import lax
from jax.sharding import Mesh
from jax.sharding import PartitionSpec as P

BLK = 256
HEAD_AXES = ("hx", "hy", "hc")


def _flat(x, y, c, ny, nc):
    return (x * ny + y) * nc + c


def _ring_perm(stage, d, nx, ny, nc):
    pairs = []
    for x in range(nx):
        for y in range(ny):
            for c in range(nc):
                along_y = (c == 0) == (stage == 0)
                if along_y:
                    tx, ty = x, (y + d) % ny
                else:
                    tx, ty = (x + d) % nx, y
                pairs.append((_flat(x, y, c, ny, nc), _flat(tx, ty, c, ny, nc)))
    return pairs


def _core_perm(nx, ny, nc):
    pairs = []
    for x in range(nx):
        for y in range(ny):
            for c in range(nc):
                pairs.append((_flat(x, y, c, ny, nc), _flat(x, y, 1 - c, ny, nc)))
    return pairs


def _send(value, perm):
    return lax.ppermute(value, HEAD_AXES, perm)


def gather_ring(blk, stage, sizes):
    p1 = _send(blk, _ring_perm(stage, 1, *sizes))
    m1 = _send(blk, _ring_perm(stage, -1, *sizes))
    h = blk.shape[0] // 2
    a = _send(p1[:h], _ring_perm(stage, 1, *sizes))
    b = _send(m1[h:], _ring_perm(stage, -1, *sizes))
    far = jnp.concatenate([a, b], axis=0)
    return jnp.stack([blk, p1, far, m1])


def reduce_ring(data, stage, sizes):
    h = data.shape[1] // 2
    rp = _send(data[2, :h].astype(jnp.bfloat16), _ring_perm(stage, 1, *sizes))
    rm = _send(data[2, h:].astype(jnp.bfloat16), _ring_perm(stage, -1, *sizes))
    ahead = jnp.concatenate([data[1, :h] + rp, data[1, h:]], axis=0)
    behind = jnp.concatenate([data[3, :h], data[3, h:] + rm], axis=0)
    gp = _send(ahead.astype(jnp.bfloat16), _ring_perm(stage, 1, *sizes))
    gm = _send(behind.astype(jnp.bfloat16), _ring_perm(stage, -1, *sizes))
    return data[0] + gp.astype(jnp.float32) + gm.astype(jnp.float32)


def attend_exact(queries, keys_win, vals_win, book, reach_one, prev_flag, block_len, scale):
    exact = (
        lax.dot_general(
            queries, keys_win, (((1,), (1,)), ((), ())), preferred_element_type=jnp.float32
        )
        * scale
    )
    coded = (
        lax.dot_general(queries, book, (((1,), (1,)), ((), ())), preferred_element_type=jnp.float32)
        * scale
    )
    rows = lax.broadcasted_iota(jnp.int32, exact.shape, 0)
    cols = lax.broadcasted_iota(jnp.int32, exact.shape, 1)
    prev_ok = (cols < block_len) & (cols >= block_len - reach_one) & prev_flag
    curr_ok = (cols >= block_len) & (cols - block_len <= rows)
    allowed = prev_ok | curr_ok
    top_e = jnp.max(jnp.where(allowed, exact, -jnp.inf), axis=1)
    probs = jnp.exp(jnp.where(allowed, exact - top_e[:, None], -jnp.inf))
    numer = jnp.dot(probs.astype(jnp.bfloat16), vals_win, preferred_element_type=jnp.float32)
    denom = jnp.sum(probs, axis=1)
    return top_e, numer, denom, coded


def attend_cache(top_e, numer_e, denom_e, coded, cache_v, cache_c):
    valid = cache_c > 0.5
    top = jnp.maximum(top_e, jnp.max(jnp.where(valid[None, :], coded, -jnp.inf), axis=1))
    alpha = jnp.exp(top_e - top)
    weights = jnp.exp(jnp.where(valid[None, :], coded - top[:, None], -jnp.inf))
    numer = alpha[:, None] * numer_e + jnp.dot(weights, cache_v, precision=lax.Precision.HIGHEST)
    denom = alpha * denom_e + jnp.dot(weights, cache_c, precision=lax.Precision.HIGHEST)
    return (numer / denom[:, None]).astype(jnp.bfloat16)


def on_device(tokens_in, w_qkv, w_out, codebook, codes, reach):
    nx, ny, nc = lax.axis_size("hx"), lax.axis_size("hy"), lax.axis_size("hc")
    sizes = (nx, ny, nc)
    core_perm = _core_perm(*sizes)
    me_x, me_y, me_c = lax.axis_index("hx"), lax.axis_index("hy"), lax.axis_index("hc")
    n_ctx = lax.axis_size("ctx")
    g = lax.axis_index("ctx")
    rows, width = tokens_in.shape
    head_dim = codebook.shape[2]
    num_codes = codebook.shape[1]
    scale = 1.0 / math.sqrt(head_dim)
    half = rows // 2

    projected = project(tokens_in, w_qkv, sizes)
    queries = projected[:, :head_dim].astype(jnp.bfloat16)
    key_vals = projected[:, head_dim:].astype(jnp.bfloat16)
    values = key_vals[:, head_dim:]

    code_row = codes[0]
    code_ids = jnp.arange(num_codes, dtype=jnp.int32)
    hi = (code_row // 16).astype(jnp.bfloat16).reshape(1, -1)
    lo = (code_row % 16).astype(jnp.bfloat16).reshape(1, -1)
    kvw = key_vals.shape[1]
    code_rows = jnp.pad(jnp.concatenate([hi, lo], axis=0), ((0, 0), (0, kvw - rows)))
    kv_blob = jnp.concatenate([key_vals, code_rows, jnp.zeros((14, kvw), jnp.bfloat16)], axis=0)
    route = [(i, i + 1) for i in range(n_ctx - 1)]
    prev_blob = lax.ppermute(kv_blob, "ctx", route)
    prev_kv = prev_blob[:rows]
    prev_codes = (
        prev_blob[rows, :rows].astype(jnp.int32) * 16 + prev_blob[rows + 1, :rows].astype(jnp.int32)
    )

    onehot_own = (code_row[:, None] == code_ids[None, :]).astype(jnp.bfloat16)
    sums = lax.dot_general(
        onehot_own, values, (((0,), (0,)), ((), ())), preferred_element_type=jnp.float32
    )
    counts = jnp.sum(onehot_own.astype(jnp.float32), axis=0)
    span = num_codes // n_ctx
    cache_v, cache_c = code_prefix(sums, counts, span, n_ctx, head_dim)
    prev_ok = (jnp.arange(rows, dtype=jnp.int32) < BLK - reach[0]) & (g > 0)
    onehot_prev = (
        (prev_codes[:, None] == code_ids[None, :]) & prev_ok[:, None]
    ).astype(jnp.bfloat16)
    cache_v = cache_v + lax.dot_general(
        onehot_prev, prev_kv[:, head_dim:], (((0,), (0,)), ((), ())),
        preferred_element_type=jnp.float32,
    )
    cache_c = cache_c + jnp.sum(onehot_prev.astype(jnp.float32), axis=0)

    ext_kv = jnp.concatenate([prev_kv, key_vals], axis=0)
    top_e, numer_e, denom_e, coded = attend_exact(
        queries,
        ext_kv[:, :head_dim],
        ext_kv[:, head_dim:],
        codebook[0],
        reach[0],
        g > 0,
        BLK,
        scale,
    )
    attended = attend_cache(top_e, numer_e, denom_e, coded, cache_v, cache_c)

    return reduce_out(attended, w_out, sizes)


def _pack(sums, counts, span, n, head_dim):
    hi = jnp.floor(counts / 64.0)
    lo = counts - hi * 64.0
    tail = jnp.zeros((n, 8, head_dim), jnp.float32)
    tail = tail.at[:, 0, :span].set(hi.reshape(n, span)).at[:, 1, :span].set(lo.reshape(n, span))
    return jnp.concatenate([sums.reshape(n, span, head_dim), tail], axis=1).astype(jnp.bfloat16)


def _unpack(blob, span):
    blob = blob.astype(jnp.float32)
    sums = blob[:, :span]
    counts = blob[:, span, :span] * 64.0 + blob[:, span + 1, :span]
    return sums, counts


def code_prefix(sums, counts, span, n, head_dim):
    got = lax.all_to_all(_pack(sums, counts, span, n, head_dim), "ctx", 0, 0, tiled=True)
    b = jnp.arange(n, dtype=jnp.int32)
    before = (b[None, :] <= b[:, None] - 2).astype(jnp.bfloat16)
    pre = jnp.einsum("bc,cxd->bxd", before, got, preferred_element_type=jnp.float32)
    total = pre[:, span] * 64.0 + pre[:, span + 1]
    hi = jnp.floor(total / 64.0)
    lo = total - hi * 64.0
    rows = lax.broadcasted_iota(jnp.int32, pre.shape, 1)
    pre = jnp.where(rows == span, hi[:, None, :], jnp.where(rows == span + 1, lo[:, None, :], pre))
    back = lax.all_to_all(pre.astype(jnp.bfloat16), "ctx", 0, 0, tiled=True)
    cache_v, cache_c = _unpack(back, span)
    return cache_v.reshape(n * span, head_dim), cache_c.reshape(n * span)

def project(tokens_in, w_qkv, sizes):
    nx, ny, nc = sizes
    n_head = nx * ny * nc
    core_perm = _core_perm(*sizes)
    me_c = lax.axis_index("hc")
    rows, width = tokens_in.shape
    half = rows // nc
    spread = jnp.broadcast_to(
        tokens_in.reshape(1, nc, half, width), (n_head // nc, nc, half, width)
    ).reshape(n_head, half, width)
    mine = lax.all_to_all(spread, HEAD_AXES, 0, 0, tiled=True)
    theirs = _send(mine, core_perm)
    w_local = w_qkv[:, 0, :].reshape(n_head, width, -1)
    dims = (((0, 2), (0, 1)), ((), ()))
    proj_own = lax.dot_general(mine, w_local, dims, preferred_element_type=jnp.float32)
    proj_oth = lax.dot_general(theirs, w_local, dims, preferred_element_type=jnp.float32)
    projected = jnp.where(
        me_c == 0,
        jnp.concatenate([proj_own, proj_oth], axis=0),
        jnp.concatenate([proj_oth, proj_own], axis=0),
    )
    return projected


def reduce_out(attended, w_out, sizes):
    nx, ny, nc = sizes
    core_perm = _core_perm(*sizes)
    me_c = lax.axis_index("hc")
    rows = attended.shape[0]
    w_full = w_out[0]
    cols = w_full.shape[1] // nc
    w_keep = lax.dynamic_slice_in_dim(w_full, me_c * cols, cols, 1)
    w_give = lax.dynamic_slice_in_dim(w_full, (1 - me_c) * cols, cols, 1)
    w_theirs = _send(w_give, core_perm)
    att_theirs = _send(attended, core_perm)
    own = lax.optimization_barrier(jnp.dot(attended, w_keep, preferred_element_type=jnp.float32))
    summed = (own + jnp.dot(att_theirs, w_theirs, preferred_element_type=jnp.float32)).astype(
        jnp.bfloat16
    )
    n_head = nx * ny * nc
    chunks = summed.reshape(n_head, rows // n_head, cols)
    parts = lax.all_to_all(chunks, HEAD_AXES, 0, 0, tiled=True).astype(jnp.float32)
    parts = parts.reshape(n_head // nc, nc, rows // n_head, cols).sum(axis=0)
    out = parts.transpose(1, 0, 2).reshape(rows // n_head, nc * cols)
    return out.astype(jnp.bfloat16)


def solution(mesh):
    n_ctx, n_head = mesh.devices.shape
    devices = mesh.devices.reshape(n_ctx, 4, 4, n_head // 16)
    grid = Mesh(devices, ("ctx",) + HEAD_AXES)
    in_specs = (
        P("ctx", HEAD_AXES),
        P(None, HEAD_AXES, None),
        P(HEAD_AXES, None, None),
        P(HEAD_AXES, None, None),
        P(HEAD_AXES, "ctx"),
        P("ctx"),
    )
    out_specs = P(("ctx",) + HEAD_AXES, None)
    return jax.shard_map(
        on_device, mesh=grid, in_specs=in_specs, out_specs=out_specs, check_vma=False
    )
```

```python
import math

import jax
import jax.numpy as jnp
from jax import lax
from jax.sharding import Mesh
from jax.sharding import PartitionSpec as P

BLK = 256
HEAD_AXES = ("hx", "hy", "hc")


def _flat(x, y, c, ny, nc):
    return (x * ny + y) * nc + c


def _ring_perm(stage, d, nx, ny, nc):
    pairs = []
    for x in range(nx):
        for y in range(ny):
            for c in range(nc):
                along_y = (c == 0) == (stage == 0)
                if along_y:
                    tx, ty = x, (y + d) % ny
                else:
                    tx, ty = (x + d) % nx, y
                pairs.append((_flat(x, y, c, ny, nc), _flat(tx, ty, c, ny, nc)))
    return pairs


def _core_perm(nx, ny, nc):
    pairs = []
    for x in range(nx):
        for y in range(ny):
            for c in range(nc):
                pairs.append((_flat(x, y, c, ny, nc), _flat(x, y, 1 - c, ny, nc)))
    return pairs


def _send(value, perm):
    return lax.ppermute(value, HEAD_AXES, perm)


def gather_ring(blk, stage, sizes):
    p1 = _send(blk, _ring_perm(stage, 1, *sizes))
    m1 = _send(blk, _ring_perm(stage, -1, *sizes))
    h = blk.shape[0] // 2
    a = _send(p1[:h], _ring_perm(stage, 1, *sizes))
    b = _send(m1[h:], _ring_perm(stage, -1, *sizes))
    far = jnp.concatenate([a, b], axis=0)
    return jnp.stack([blk, p1, far, m1])


def reduce_ring(data, stage, sizes):
    h = data.shape[1] // 2
    rp = _send(data[2, :h].astype(jnp.bfloat16), _ring_perm(stage, 1, *sizes))
    rm = _send(data[2, h:].astype(jnp.bfloat16), _ring_perm(stage, -1, *sizes))
    ahead = jnp.concatenate([data[1, :h] + rp, data[1, h:]], axis=0)
    behind = jnp.concatenate([data[3, :h], data[3, h:] + rm], axis=0)
    gp = _send(ahead.astype(jnp.bfloat16), _ring_perm(stage, 1, *sizes))
    gm = _send(behind.astype(jnp.bfloat16), _ring_perm(stage, -1, *sizes))
    return data[0] + gp.astype(jnp.float32) + gm.astype(jnp.float32)


def attend_exact(queries, keys_win, vals_win, book, reach_one, prev_flag, block_len, scale):
    exact = (
        lax.dot_general(
            queries, keys_win, (((1,), (1,)), ((), ())), preferred_element_type=jnp.float32
        )
        * scale
    )
    coded = (
        lax.dot_general(queries, book, (((1,), (1,)), ((), ())), preferred_element_type=jnp.float32)
        * scale
    )
    rows = lax.broadcasted_iota(jnp.int32, exact.shape, 0)
    cols = lax.broadcasted_iota(jnp.int32, exact.shape, 1)
    prev_ok = (cols < block_len) & (cols >= block_len - reach_one) & prev_flag
    curr_ok = (cols >= block_len) & (cols - block_len <= rows)
    allowed = prev_ok | curr_ok
    top_e = jnp.max(jnp.where(allowed, exact, -jnp.inf), axis=1)
    probs = jnp.exp(jnp.where(allowed, exact - top_e[:, None], -jnp.inf))
    numer = jnp.dot(probs.astype(jnp.bfloat16), vals_win, preferred_element_type=jnp.float32)
    denom = jnp.sum(probs, axis=1)
    return top_e, numer, denom, coded


def attend_cache(top_e, numer_e, denom_e, coded, cache_v, cache_c):
    valid = cache_c > 0.5
    top = jnp.maximum(top_e, jnp.max(jnp.where(valid[None, :], coded, -jnp.inf), axis=1))
    alpha = jnp.exp(top_e - top)
    weights = jnp.exp(jnp.where(valid[None, :], coded - top[:, None], -jnp.inf))
    numer = alpha[:, None] * numer_e + jnp.dot(weights, cache_v, precision=lax.Precision.HIGHEST)
    denom = alpha * denom_e + jnp.dot(weights, cache_c, precision=lax.Precision.HIGHEST)
    return (numer / denom[:, None]).astype(jnp.bfloat16)


def on_device(tokens_in, w_qkv, w_out, codebook, codes, reach):
    nx, ny, nc = lax.axis_size("hx"), lax.axis_size("hy"), lax.axis_size("hc")
    sizes = (nx, ny, nc)
    core_perm = _core_perm(*sizes)
    me_x, me_y, me_c = lax.axis_index("hx"), lax.axis_index("hy"), lax.axis_index("hc")
    n_ctx = lax.axis_size("ctx")
    g = lax.axis_index("ctx")
    rows, width = tokens_in.shape
    head_dim = codebook.shape[2]
    num_codes = codebook.shape[1]
    scale = 1.0 / math.sqrt(head_dim)
    half = rows // 2

    projected = project(tokens_in, w_qkv, sizes)
    queries = projected[:, :head_dim].astype(jnp.bfloat16)
    key_vals = projected[:, head_dim:].astype(jnp.bfloat16)
    values = key_vals[:, head_dim:]

    code_row = codes[0]
    code_ids = jnp.arange(num_codes, dtype=jnp.int32)
    hi = (code_row // 16).astype(jnp.bfloat16).reshape(1, -1)
    lo = (code_row % 16).astype(jnp.bfloat16).reshape(1, -1)
    kvw = key_vals.shape[1]
    code_rows = jnp.pad(jnp.concatenate([hi, lo], axis=0), ((0, 0), (0, kvw - rows)))
    kv_blob = jnp.concatenate([key_vals, code_rows, jnp.zeros((14, kvw), jnp.bfloat16)], axis=0)
    route = [(i, i + 1) for i in range(n_ctx - 1)]
    prev_blob = lax.ppermute(kv_blob, "ctx", route)
    prev_kv = prev_blob[:rows]
    prev_codes = (
        prev_blob[rows, :rows].astype(jnp.int32) * 16 + prev_blob[rows + 1, :rows].astype(jnp.int32)
    )

    onehot_own = (code_row[:, None] == code_ids[None, :]).astype(jnp.bfloat16)
    sums = lax.dot_general(
        onehot_own, values, (((0,), (0,)), ((), ())), preferred_element_type=jnp.float32
    )
    counts = jnp.sum(onehot_own.astype(jnp.float32), axis=0)
    span = num_codes // n_ctx
    cache_v, cache_c = code_prefix(sums, counts, span, n_ctx, head_dim)
    prev_ok = (jnp.arange(rows, dtype=jnp.int32) < BLK - reach[0]) & (g > 0)
    onehot_prev = (
        (prev_codes[:, None] == code_ids[None, :]) & prev_ok[:, None]
    ).astype(jnp.bfloat16)
    cache_v = cache_v + lax.dot_general(
        onehot_prev, prev_kv[:, head_dim:], (((0,), (0,)), ((), ())),
        preferred_element_type=jnp.float32,
    )
    cache_c = cache_c + jnp.sum(onehot_prev.astype(jnp.float32), axis=0)

    ext_kv = jnp.concatenate([prev_kv, key_vals], axis=0)
    top_e, numer_e, denom_e, coded = attend_exact(
        queries,
        ext_kv[:, :head_dim],
        ext_kv[:, head_dim:],
        codebook[0],
        reach[0],
        g > 0,
        BLK,
        scale,
    )
    attended = attend_cache(top_e, numer_e, denom_e, coded, cache_v, cache_c)

    return reduce_out(attended, w_out, sizes)


def _pack(sums, counts, span, n, head_dim):
    hi = jnp.floor(counts / 64.0).reshape(n, 1, span)
    lo = counts.reshape(n, 1, span) - hi * 64.0
    lanes = lax.broadcasted_iota(jnp.int32, (n, 8, head_dim), 2)
    rows = lax.broadcasted_iota(jnp.int32, (n, 8, head_dim), 1)
    wide_hi = jnp.pad(hi, ((0, 0), (0, 0), (0, head_dim - span)))
    wide_lo = jnp.pad(lo, ((0, 0), (0, 0), (0, head_dim - span)))
    tail = jnp.where(
        (rows == 0) & (lanes < span), wide_hi, jnp.where((rows == 1) & (lanes < span), wide_lo, 0.0)
    )
    return jnp.concatenate([sums.reshape(n, span, head_dim), tail], axis=1).astype(jnp.bfloat16)


def _unpack(blob, span):
    blob = blob.astype(jnp.float32)
    sums = blob[:, :span]
    counts = blob[:, span, :span] * 64.0 + blob[:, span + 1, :span]
    return sums, counts


def code_prefix(sums, counts, span, n, head_dim):
    got = lax.all_to_all(_pack(sums, counts, span, n, head_dim), "ctx", 0, 0, tiled=True)
    b = jnp.arange(n, dtype=jnp.int32)
    before = (b[None, :] <= b[:, None] - 2).astype(jnp.bfloat16)
    pre = jnp.einsum("bc,cxd->bxd", before, got, preferred_element_type=jnp.float32)
    total = pre[:, span] * 64.0 + pre[:, span + 1]
    hi = jnp.floor(total / 64.0)
    lo = total - hi * 64.0
    rows = lax.broadcasted_iota(jnp.int32, pre.shape, 1)
    pre = jnp.where(rows == span, hi[:, None, :], jnp.where(rows == span + 1, lo[:, None, :], pre))
    back = lax.all_to_all(pre.astype(jnp.bfloat16), "ctx", 0, 0, tiled=True)
    cache_v, cache_c = _unpack(back, span)
    return cache_v.reshape(n * span, head_dim), cache_c.reshape(n * span)

def project(tokens_in, w_qkv, sizes):
    nx, ny, nc = sizes
    n_head = nx * ny * nc
    core_perm = _core_perm(*sizes)
    me_c = lax.axis_index("hc")
    rows, width = tokens_in.shape
    half = rows // nc
    spread = jnp.broadcast_to(
        tokens_in.reshape(1, nc, half, width), (n_head // nc, nc, half, width)
    ).reshape(n_head, half, width)
    mine = lax.all_to_all(spread, HEAD_AXES, 0, 0, tiled=True)
    theirs = _send(mine, core_perm)
    w_local = w_qkv[:, 0, :].reshape(n_head, width, -1)
    dims = (((0, 2), (0, 1)), ((), ()))
    proj_own = lax.dot_general(mine, w_local, dims, preferred_element_type=jnp.float32)
    proj_oth = lax.dot_general(theirs, w_local, dims, preferred_element_type=jnp.float32)
    projected = jnp.where(
        me_c == 0,
        jnp.concatenate([proj_own, proj_oth], axis=0),
        jnp.concatenate([proj_oth, proj_own], axis=0),
    )
    return projected


def reduce_out(attended, w_out, sizes):
    nx, ny, nc = sizes
    core_perm = _core_perm(*sizes)
    me_c = lax.axis_index("hc")
    rows = attended.shape[0]
    w_full = w_out[0]
    cols = w_full.shape[1] // nc
    w_keep = lax.dynamic_slice_in_dim(w_full, me_c * cols, cols, 1)
    w_give = lax.dynamic_slice_in_dim(w_full, (1 - me_c) * cols, cols, 1)
    w_theirs = _send(w_give, core_perm)
    att_theirs = _send(attended, core_perm)
    own = lax.optimization_barrier(jnp.dot(attended, w_keep, preferred_element_type=jnp.float32))
    summed = (own + jnp.dot(att_theirs, w_theirs, preferred_element_type=jnp.float32)).astype(
        jnp.bfloat16
    )
    n_head = nx * ny * nc
    chunks = summed.reshape(n_head, rows // n_head, cols)
    parts = lax.all_to_all(chunks, HEAD_AXES, 0, 0, tiled=True).astype(jnp.float32)
    parts = parts.reshape(n_head // nc, nc, rows // n_head, cols).sum(axis=0)
    out = parts.transpose(1, 0, 2).reshape(rows // n_head, nc * cols)
    return out.astype(jnp.bfloat16)


def solution(mesh):
    n_ctx, n_head = mesh.devices.shape
    devices = mesh.devices.reshape(n_ctx, 4, 4, n_head // 16)
    grid = Mesh(devices, ("ctx",) + HEAD_AXES)
    in_specs = (
        P("ctx", HEAD_AXES),
        P(None, HEAD_AXES, None),
        P(HEAD_AXES, None, None),
        P(HEAD_AXES, None, None),
        P(HEAD_AXES, "ctx"),
        P("ctx"),
    )
    out_specs = P(("ctx",) + HEAD_AXES, None)
    return jax.shard_map(
        on_device, mesh=grid, in_specs=in_specs, out_specs=out_specs, check_vma=False
    )
```

```python
import math

import jax
import jax.numpy as jnp
from jax import lax
from jax.sharding import Mesh
from jax.sharding import PartitionSpec as P

BLK = 256
HEAD_AXES = ("hx", "hy", "hc")


def _flat(x, y, c, ny, nc):
    return (x * ny + y) * nc + c


def _ring_perm(stage, d, nx, ny, nc):
    pairs = []
    for x in range(nx):
        for y in range(ny):
            for c in range(nc):
                along_y = (c == 0) == (stage == 0)
                if along_y:
                    tx, ty = x, (y + d) % ny
                else:
                    tx, ty = (x + d) % nx, y
                pairs.append((_flat(x, y, c, ny, nc), _flat(tx, ty, c, ny, nc)))
    return pairs


def _core_perm(nx, ny, nc):
    pairs = []
    for x in range(nx):
        for y in range(ny):
            for c in range(nc):
                pairs.append((_flat(x, y, c, ny, nc), _flat(x, y, 1 - c, ny, nc)))
    return pairs


def _send(value, perm):
    return lax.ppermute(value, HEAD_AXES, perm)


def gather_ring(blk, stage, sizes):
    p1 = _send(blk, _ring_perm(stage, 1, *sizes))
    m1 = _send(blk, _ring_perm(stage, -1, *sizes))
    h = blk.shape[0] // 2
    a = _send(p1[:h], _ring_perm(stage, 1, *sizes))
    b = _send(m1[h:], _ring_perm(stage, -1, *sizes))
    far = jnp.concatenate([a, b], axis=0)
    return jnp.stack([blk, p1, far, m1])


def reduce_ring(data, stage, sizes):
    h = data.shape[1] // 2
    rp = _send(data[2, :h].astype(jnp.bfloat16), _ring_perm(stage, 1, *sizes))
    rm = _send(data[2, h:].astype(jnp.bfloat16), _ring_perm(stage, -1, *sizes))
    ahead = jnp.concatenate([data[1, :h] + rp, data[1, h:]], axis=0)
    behind = jnp.concatenate([data[3, :h], data[3, h:] + rm], axis=0)
    gp = _send(ahead.astype(jnp.bfloat16), _ring_perm(stage, 1, *sizes))
    gm = _send(behind.astype(jnp.bfloat16), _ring_perm(stage, -1, *sizes))
    return data[0] + gp.astype(jnp.float32) + gm.astype(jnp.float32)


def attend_exact(queries, keys_win, vals_win, book, reach_one, prev_flag, block_len, scale):
    exact = (
        lax.dot_general(
            queries, keys_win, (((1,), (1,)), ((), ())), preferred_element_type=jnp.float32
        )
        * scale
    )
    coded = (
        lax.dot_general(queries, book, (((1,), (1,)), ((), ())), preferred_element_type=jnp.float32)
        * scale
    )
    rows = lax.broadcasted_iota(jnp.int32, exact.shape, 0)
    cols = lax.broadcasted_iota(jnp.int32, exact.shape, 1)
    prev_ok = (cols < block_len) & (cols >= block_len - reach_one) & prev_flag
    curr_ok = (cols >= block_len) & (cols - block_len <= rows)
    allowed = prev_ok | curr_ok
    top_e = jnp.max(jnp.where(allowed, exact, -jnp.inf), axis=1)
    probs = jnp.exp(jnp.where(allowed, exact - top_e[:, None], -jnp.inf))
    numer = jnp.dot(probs.astype(jnp.bfloat16), vals_win, preferred_element_type=jnp.float32)
    denom = jnp.sum(probs, axis=1)
    return top_e, numer, denom, coded


def attend_cache(top_e, numer_e, denom_e, coded, cache_v, cache_c):
    valid = cache_c > 0.5
    top = jnp.maximum(top_e, jnp.max(jnp.where(valid[None, :], coded, -jnp.inf), axis=1))
    alpha = jnp.exp(top_e - top)
    weights = jnp.exp(jnp.where(valid[None, :], coded - top[:, None], -jnp.inf))
    numer = alpha[:, None] * numer_e + jnp.dot(weights, cache_v, precision=lax.Precision.HIGHEST)
    denom = alpha * denom_e + jnp.dot(weights, cache_c, precision=lax.Precision.HIGHEST)
    return (numer / denom[:, None]).astype(jnp.bfloat16)


def on_device(tokens_in, w_qkv, w_out, codebook, codes, reach):
    nx, ny, nc = lax.axis_size("hx"), lax.axis_size("hy"), lax.axis_size("hc")
    sizes = (nx, ny, nc)
    core_perm = _core_perm(*sizes)
    me_x, me_y, me_c = lax.axis_index("hx"), lax.axis_index("hy"), lax.axis_index("hc")
    n_ctx = lax.axis_size("ctx")
    g = lax.axis_index("ctx")
    rows, width = tokens_in.shape
    head_dim = codebook.shape[2]
    num_codes = codebook.shape[1]
    scale = 1.0 / math.sqrt(head_dim)
    half = rows // 2

    projected = project(tokens_in, w_qkv, sizes)
    queries = projected[:, :head_dim].astype(jnp.bfloat16)
    key_vals = projected[:, head_dim:].astype(jnp.bfloat16)
    values = key_vals[:, head_dim:]

    code_row = codes[0]
    code_ids = jnp.arange(num_codes, dtype=jnp.int32)
    hi = (code_row // 16).astype(jnp.bfloat16).reshape(1, -1)
    lo = (code_row % 16).astype(jnp.bfloat16).reshape(1, -1)
    kvw = key_vals.shape[1]
    code_rows = jnp.pad(jnp.concatenate([hi, lo], axis=0), ((0, 0), (0, kvw - rows)))
    kv_blob = jnp.concatenate([key_vals, code_rows, jnp.zeros((14, kvw), jnp.bfloat16)], axis=0)
    route = [(i, i + 1) for i in range(n_ctx - 1)]
    prev_blob = lax.ppermute(kv_blob, "ctx", route)
    prev_kv = prev_blob[:rows]
    prev_codes = (
        prev_blob[rows, :rows].astype(jnp.int32) * 16 + prev_blob[rows + 1, :rows].astype(jnp.int32)
    )

    onehot_own = (code_row[:, None] == code_ids[None, :]).astype(jnp.bfloat16)
    sums = lax.dot_general(
        onehot_own, values, (((0,), (0,)), ((), ())), preferred_element_type=jnp.float32
    )
    counts = jnp.sum(onehot_own.astype(jnp.float32), axis=0)
    span = num_codes // n_ctx
    cache_v, cache_c = code_prefix(sums, counts, span, n_ctx, head_dim)
    prev_ok = (jnp.arange(rows, dtype=jnp.int32) < BLK - reach[0]) & (g > 0)
    onehot_prev = (
        (prev_codes[:, None] == code_ids[None, :]) & prev_ok[:, None]
    ).astype(jnp.bfloat16)
    cache_v = cache_v + lax.dot_general(
        onehot_prev, prev_kv[:, head_dim:], (((0,), (0,)), ((), ())),
        preferred_element_type=jnp.float32,
    )
    cache_c = cache_c + jnp.sum(onehot_prev.astype(jnp.float32), axis=0)

    ext_kv = jnp.concatenate([prev_kv, key_vals], axis=0)
    top_e, numer_e, denom_e, coded = attend_exact(
        queries,
        ext_kv[:, :head_dim],
        ext_kv[:, head_dim:],
        codebook[0],
        reach[0],
        g > 0,
        BLK,
        scale,
    )
    attended = attend_cache(top_e, numer_e, denom_e, coded, cache_v, cache_c)

    return reduce_out(attended, w_out, sizes)


def _pack(sums, counts, span, n, head_dim):
    hi = jnp.floor(counts / 64.0).reshape(n, 1, span)
    lo = counts.reshape(n, 1, span) - hi * 64.0
    lanes = lax.broadcasted_iota(jnp.int32, (n, 8, head_dim), 2)
    rows = lax.broadcasted_iota(jnp.int32, (n, 8, head_dim), 1)
    wide_hi = jnp.pad(hi, ((0, 0), (0, 0), (0, head_dim - span)))
    wide_lo = jnp.pad(lo, ((0, 0), (0, 0), (0, head_dim - span)))
    tail = jnp.where(
        (rows == 0) & (lanes < span), wide_hi, jnp.where((rows == 1) & (lanes < span), wide_lo, 0.0)
    )
    return jnp.concatenate([sums.reshape(n, span, head_dim), tail], axis=1).astype(jnp.bfloat16)


def _unpack(blob, span):
    blob = blob.astype(jnp.float32)
    sums = blob[:, :span]
    counts = blob[:, span, :span] * 64.0 + blob[:, span + 1, :span]
    return sums, counts


def code_prefix(sums, counts, span, n, head_dim):
    got = lax.all_to_all(_pack(sums, counts, span, n, head_dim), "ctx", 0, 0, tiled=True)
    b = jnp.arange(n, dtype=jnp.int32)
    before = (b[None, :] <= b[:, None] - 2).astype(jnp.bfloat16)
    pre = jnp.einsum("bc,cxd->bxd", before, got, preferred_element_type=jnp.float32)
    total = pre[:, span] * 64.0 + pre[:, span + 1]
    hi = jnp.floor(total / 64.0)
    lo = total - hi * 64.0
    rows = lax.broadcasted_iota(jnp.int32, pre.shape, 1)
    pre = jnp.where(rows == span, hi[:, None, :], jnp.where(rows == span + 1, lo[:, None, :], pre))
    back = lax.all_to_all(pre.astype(jnp.bfloat16), "ctx", 0, 0, tiled=True)
    cache_v, cache_c = _unpack(back, span)
    return cache_v.reshape(n * span, head_dim), cache_c.reshape(n * span)

def project(tokens_in, w_qkv, sizes):
    nx, ny, nc = sizes
    n_head = nx * ny * nc
    core_perm = _core_perm(*sizes)
    me_c = lax.axis_index("hc")
    rows, width = tokens_in.shape
    half = rows // nc
    spread = jnp.tile(tokens_in, (n_head // nc, 1)).reshape(n_head, half, width)
    mine = lax.all_to_all(spread, HEAD_AXES, 0, 0, tiled=True)
    theirs = _send(mine, core_perm)
    w_local = w_qkv[:, 0, :].reshape(n_head, width, -1)
    dims = (((0, 2), (0, 1)), ((), ()))
    proj_own = lax.dot_general(mine, w_local, dims, preferred_element_type=jnp.float32)
    proj_oth = lax.dot_general(theirs, w_local, dims, preferred_element_type=jnp.float32)
    projected = jnp.where(
        me_c == 0,
        jnp.concatenate([proj_own, proj_oth], axis=0),
        jnp.concatenate([proj_oth, proj_own], axis=0),
    )
    return projected


def reduce_out(attended, w_out, sizes):
    nx, ny, nc = sizes
    core_perm = _core_perm(*sizes)
    me_c = lax.axis_index("hc")
    rows = attended.shape[0]
    w_full = w_out[0]
    cols = w_full.shape[1] // nc
    w_keep = lax.dynamic_slice_in_dim(w_full, me_c * cols, cols, 1)
    w_give = lax.dynamic_slice_in_dim(w_full, (1 - me_c) * cols, cols, 1)
    w_theirs = _send(w_give, core_perm)
    att_theirs = _send(attended, core_perm)
    own = lax.optimization_barrier(jnp.dot(attended, w_keep, preferred_element_type=jnp.float32))
    summed = (own + jnp.dot(att_theirs, w_theirs, preferred_element_type=jnp.float32)).astype(
        jnp.bfloat16
    )
    n_head = nx * ny * nc
    chunks = summed.reshape(n_head, rows // n_head, cols)
    parts = lax.all_to_all(chunks, HEAD_AXES, 0, 0, tiled=True).astype(jnp.float32)
    parts = parts.reshape(n_head // nc, nc, rows // n_head, cols).sum(axis=0)
    out = parts.transpose(1, 0, 2).reshape(rows // n_head, nc * cols)
    return out.astype(jnp.bfloat16)


def solution(mesh):
    n_ctx, n_head = mesh.devices.shape
    devices = mesh.devices.reshape(n_ctx, 4, 4, n_head // 16)
    grid = Mesh(devices, ("ctx",) + HEAD_AXES)
    in_specs = (
        P("ctx", HEAD_AXES),
        P(None, HEAD_AXES, None),
        P(HEAD_AXES, None, None),
        P(HEAD_AXES, None, None),
        P(HEAD_AXES, "ctx"),
        P("ctx"),
    )
    out_specs = P(("ctx",) + HEAD_AXES, None)
    return jax.shard_map(
        on_device, mesh=grid, in_specs=in_specs, out_specs=out_specs, check_vma=False
    )
```

```python
import math

import jax
import jax.numpy as jnp
from jax import lax
from jax.sharding import Mesh
from jax.sharding import PartitionSpec as P

BLK = 256
HEAD_AXES = ("hx", "hy", "hc")


def _flat(x, y, c, ny, nc):
    return (x * ny + y) * nc + c


def _ring_perm(stage, d, nx, ny, nc):
    pairs = []
    for x in range(nx):
        for y in range(ny):
            for c in range(nc):
                along_y = (c == 0) == (stage == 0)
                if along_y:
                    tx, ty = x, (y + d) % ny
                else:
                    tx, ty = (x + d) % nx, y
                pairs.append((_flat(x, y, c, ny, nc), _flat(tx, ty, c, ny, nc)))
    return pairs


def _core_perm(nx, ny, nc):
    pairs = []
    for x in range(nx):
        for y in range(ny):
            for c in range(nc):
                pairs.append((_flat(x, y, c, ny, nc), _flat(x, y, 1 - c, ny, nc)))
    return pairs


def _send(value, perm):
    return lax.ppermute(value, HEAD_AXES, perm)


def gather_ring(blk, stage, sizes):
    p1 = _send(blk, _ring_perm(stage, 1, *sizes))
    m1 = _send(blk, _ring_perm(stage, -1, *sizes))
    h = blk.shape[0] // 2
    a = _send(p1[:h], _ring_perm(stage, 1, *sizes))
    b = _send(m1[h:], _ring_perm(stage, -1, *sizes))
    far = jnp.concatenate([a, b], axis=0)
    return jnp.stack([blk, p1, far, m1])


def reduce_ring(data, stage, sizes):
    h = data.shape[1] // 2
    rp = _send(data[2, :h].astype(jnp.bfloat16), _ring_perm(stage, 1, *sizes))
    rm = _send(data[2, h:].astype(jnp.bfloat16), _ring_perm(stage, -1, *sizes))
    ahead = jnp.concatenate([data[1, :h] + rp, data[1, h:]], axis=0)
    behind = jnp.concatenate([data[3, :h], data[3, h:] + rm], axis=0)
    gp = _send(ahead.astype(jnp.bfloat16), _ring_perm(stage, 1, *sizes))
    gm = _send(behind.astype(jnp.bfloat16), _ring_perm(stage, -1, *sizes))
    return data[0] + gp.astype(jnp.float32) + gm.astype(jnp.float32)


def attend_exact(queries, keys_win, vals_win, book, reach_one, prev_flag, block_len, scale):
    exact = (
        lax.dot_general(
            queries, keys_win, (((1,), (1,)), ((), ())), preferred_element_type=jnp.float32
        )
        * scale
    )
    coded = (
        lax.dot_general(queries, book, (((1,), (1,)), ((), ())), preferred_element_type=jnp.float32)
        * scale
    )
    rows = lax.broadcasted_iota(jnp.int32, exact.shape, 0)
    cols = lax.broadcasted_iota(jnp.int32, exact.shape, 1)
    prev_ok = (cols < block_len) & (cols >= block_len - reach_one) & prev_flag
    curr_ok = (cols >= block_len) & (cols - block_len <= rows)
    allowed = prev_ok | curr_ok
    top_e = jnp.max(jnp.where(allowed, exact, -jnp.inf), axis=1)
    probs = jnp.exp(jnp.where(allowed, exact - top_e[:, None], -jnp.inf))
    numer = jnp.dot(probs.astype(jnp.bfloat16), vals_win, preferred_element_type=jnp.float32)
    denom = jnp.sum(probs, axis=1)
    return top_e, numer, denom, coded


def attend_cache(top_e, numer_e, denom_e, coded, cache_v, cache_c):
    valid = cache_c > 0.5
    top = jnp.maximum(top_e, jnp.max(jnp.where(valid[None, :], coded, -jnp.inf), axis=1))
    alpha = jnp.exp(top_e - top)
    weights = jnp.exp(jnp.where(valid[None, :], coded - top[:, None], -jnp.inf))
    numer = alpha[:, None] * numer_e + jnp.dot(weights, cache_v, precision=lax.Precision.HIGH)
    denom = alpha * denom_e + jnp.dot(weights, cache_c, precision=lax.Precision.HIGH)
    return (numer / denom[:, None]).astype(jnp.bfloat16)


def on_device(tokens_in, w_qkv, w_out, codebook, codes, reach):
    nx, ny, nc = lax.axis_size("hx"), lax.axis_size("hy"), lax.axis_size("hc")
    sizes = (nx, ny, nc)
    core_perm = _core_perm(*sizes)
    me_x, me_y, me_c = lax.axis_index("hx"), lax.axis_index("hy"), lax.axis_index("hc")
    n_ctx = lax.axis_size("ctx")
    g = lax.axis_index("ctx")
    rows, width = tokens_in.shape
    head_dim = codebook.shape[2]
    num_codes = codebook.shape[1]
    scale = 1.0 / math.sqrt(head_dim)
    half = rows // 2

    projected = project(tokens_in, w_qkv, sizes)
    queries = projected[:, :head_dim].astype(jnp.bfloat16)
    key_vals = projected[:, head_dim:].astype(jnp.bfloat16)
    values = key_vals[:, head_dim:]

    code_row = codes[0]
    code_ids = jnp.arange(num_codes, dtype=jnp.int32)
    hi = (code_row // 16).astype(jnp.bfloat16).reshape(1, -1)
    lo = (code_row % 16).astype(jnp.bfloat16).reshape(1, -1)
    kvw = key_vals.shape[1]
    code_rows = jnp.pad(jnp.concatenate([hi, lo], axis=0), ((0, 0), (0, kvw - rows)))
    kv_blob = jnp.concatenate([key_vals, code_rows, jnp.zeros((14, kvw), jnp.bfloat16)], axis=0)
    route = [(i, i + 1) for i in range(n_ctx - 1)]
    prev_blob = lax.ppermute(kv_blob, "ctx", route)
    prev_kv = prev_blob[:rows]
    prev_codes = (
        prev_blob[rows, :rows].astype(jnp.int32) * 16 + prev_blob[rows + 1, :rows].astype(jnp.int32)
    )

    onehot_own = (code_row[:, None] == code_ids[None, :]).astype(jnp.bfloat16)
    sums = lax.dot_general(
        onehot_own, values, (((0,), (0,)), ((), ())), preferred_element_type=jnp.float32
    )
    counts = jnp.sum(onehot_own.astype(jnp.float32), axis=0)
    span = num_codes // n_ctx
    cache_v, cache_c = code_prefix(sums, counts, span, n_ctx, head_dim)
    prev_ok = (jnp.arange(rows, dtype=jnp.int32) < BLK - reach[0]) & (g > 0)
    onehot_prev = (
        (prev_codes[:, None] == code_ids[None, :]) & prev_ok[:, None]
    ).astype(jnp.bfloat16)
    cache_v = cache_v + lax.dot_general(
        onehot_prev, prev_kv[:, head_dim:], (((0,), (0,)), ((), ())),
        preferred_element_type=jnp.float32,
    )
    cache_c = cache_c + jnp.sum(onehot_prev.astype(jnp.float32), axis=0)

    ext_kv = jnp.concatenate([prev_kv, key_vals], axis=0)
    top_e, numer_e, denom_e, coded = attend_exact(
        queries,
        ext_kv[:, :head_dim],
        ext_kv[:, head_dim:],
        codebook[0],
        reach[0],
        g > 0,
        BLK,
        scale,
    )
    attended = attend_cache(top_e, numer_e, denom_e, coded, cache_v, cache_c)

    return reduce_out(attended, w_out, sizes)


def _pack(sums, counts, span, n, head_dim):
    hi = jnp.floor(counts / 64.0).reshape(n, 1, span)
    lo = counts.reshape(n, 1, span) - hi * 64.0
    lanes = lax.broadcasted_iota(jnp.int32, (n, 8, head_dim), 2)
    rows = lax.broadcasted_iota(jnp.int32, (n, 8, head_dim), 1)
    wide_hi = jnp.pad(hi, ((0, 0), (0, 0), (0, head_dim - span)))
    wide_lo = jnp.pad(lo, ((0, 0), (0, 0), (0, head_dim - span)))
    tail = jnp.where(
        (rows == 0) & (lanes < span), wide_hi, jnp.where((rows == 1) & (lanes < span), wide_lo, 0.0)
    )
    return jnp.concatenate([sums.reshape(n, span, head_dim), tail], axis=1).astype(jnp.bfloat16)


def _unpack(blob, span):
    blob = blob.astype(jnp.float32)
    sums = blob[:, :span]
    counts = blob[:, span, :span] * 64.0 + blob[:, span + 1, :span]
    return sums, counts


def code_prefix(sums, counts, span, n, head_dim):
    got = lax.all_to_all(_pack(sums, counts, span, n, head_dim), "ctx", 0, 0, tiled=True)
    b = jnp.arange(n, dtype=jnp.int32)
    before = (b[None, :] <= b[:, None] - 2).astype(jnp.bfloat16)
    pre = jnp.einsum("bc,cxd->bxd", before, got, preferred_element_type=jnp.float32)
    total = pre[:, span] * 64.0 + pre[:, span + 1]
    hi = jnp.floor(total / 64.0)
    lo = total - hi * 64.0
    rows = lax.broadcasted_iota(jnp.int32, pre.shape, 1)
    pre = jnp.where(rows == span, hi[:, None, :], jnp.where(rows == span + 1, lo[:, None, :], pre))
    back = lax.all_to_all(pre.astype(jnp.bfloat16), "ctx", 0, 0, tiled=True)
    cache_v, cache_c = _unpack(back, span)
    return cache_v.reshape(n * span, head_dim), cache_c.reshape(n * span)

def project(tokens_in, w_qkv, sizes):
    nx, ny, nc = sizes
    n_head = nx * ny * nc
    core_perm = _core_perm(*sizes)
    me_c = lax.axis_index("hc")
    rows, width = tokens_in.shape
    half = rows // nc
    spread = jnp.broadcast_to(
        tokens_in.reshape(1, nc, half, width), (n_head // nc, nc, half, width)
    ).reshape(n_head, half, width)
    mine = lax.all_to_all(spread, HEAD_AXES, 0, 0, tiled=True)
    theirs = _send(mine, core_perm)
    w_local = w_qkv[:, 0, :].reshape(n_head, width, -1)
    dims = (((0, 2), (0, 1)), ((), ()))
    proj_own = lax.dot_general(mine, w_local, dims, preferred_element_type=jnp.float32)
    proj_oth = lax.dot_general(theirs, w_local, dims, preferred_element_type=jnp.float32)
    projected = jnp.where(
        me_c == 0,
        jnp.concatenate([proj_own, proj_oth], axis=0),
        jnp.concatenate([proj_oth, proj_own], axis=0),
    )
    return projected


def reduce_out(attended, w_out, sizes):
    nx, ny, nc = sizes
    core_perm = _core_perm(*sizes)
    me_c = lax.axis_index("hc")
    rows = attended.shape[0]
    w_full = w_out[0]
    cols = w_full.shape[1] // nc
    w_keep = lax.dynamic_slice_in_dim(w_full, me_c * cols, cols, 1)
    w_give = lax.dynamic_slice_in_dim(w_full, (1 - me_c) * cols, cols, 1)
    w_theirs = _send(w_give, core_perm)
    att_theirs = _send(attended, core_perm)
    own = lax.optimization_barrier(jnp.dot(attended, w_keep, preferred_element_type=jnp.float32))
    summed = (own + jnp.dot(att_theirs, w_theirs, preferred_element_type=jnp.float32)).astype(
        jnp.bfloat16
    )
    n_head = nx * ny * nc
    chunks = summed.reshape(n_head, rows // n_head, cols)
    parts = lax.all_to_all(chunks, HEAD_AXES, 0, 0, tiled=True).astype(jnp.float32)
    parts = parts.reshape(n_head // nc, nc, rows // n_head, cols).sum(axis=0)
    out = parts.transpose(1, 0, 2).reshape(rows // n_head, nc * cols)
    return out.astype(jnp.bfloat16)


def solution(mesh):
    n_ctx, n_head = mesh.devices.shape
    devices = mesh.devices.reshape(n_ctx, 4, 4, n_head // 16)
    grid = Mesh(devices, ("ctx",) + HEAD_AXES)
    in_specs = (
        P("ctx", HEAD_AXES),
        P(None, HEAD_AXES, None),
        P(HEAD_AXES, None, None),
        P(HEAD_AXES, None, None),
        P(HEAD_AXES, "ctx"),
        P("ctx"),
    )
    out_specs = P(("ctx",) + HEAD_AXES, None)
    return jax.shard_map(
        on_device, mesh=grid, in_specs=in_specs, out_specs=out_specs, check_vma=False
    )
```
